32 devices in a mesh: lat: 8 (over y, x, core), lon: 4 (over z).
Axes of the slice: x: 2, y: 2, z: 4, core: 2. Of those that a mesh axis runs over, the one named last changes fastest.
Arguments:
- features: bfloat16 [192, 180, 256], P('lat', 'lon'), may hold values from -6 to 6
- obs_mask: int32 [192, 180, 8], P('lat', 'lon'), may hold values 0 or 1
- filter_taps: bfloat16 [192, 4, 3, 17], replicated, may hold values from 0.049804688 to 1
- band_width: int32 [192], replicated, may hold values from 1 to 8, as said below
- mixing: bfloat16 [8, 4, 32, 32], replicated, may hold values from -0.5 to 0.5
- cotangent: bfloat16 [192, 180, 256], P('lat', 'lon'), may hold values from -6 to 6
Outputs:
- infilled: bfloat16 [192, 180, 256], P('lat', 'lon')
- input_grad: bfloat16 [192, 180, 256], P('lat', 'lon')
- weight_grad: float32 [8, 4, 32, 32], replicated
The draws below stay inside these ranges and needn't reach their ends.
Inputs may be any that keep to these rules, and one draw needn't show every extreme that they name: band_width is 8 at the first and last cycle and 1 at cycle 192 // 2.
All inputs are finite; a program needn't handle non-finite values. No bound on the sum of `obs_mask` on one device may be relied on, other than what follows from the above.
Results may differ from the reference program's by a relative error of at most 0.005.
Values may be sent and summed in bfloat16 or wider, within the bound.
No kernel may reach another device: no remote copies, remote signals or barrier semaphores. Data moves between devices by JAX's collectives and lax.ppermute only.
A program may use at most 128 MiB of HBM per device.

```python
import math
import jax
import jax.numpy as jnp
from jax import lax

C = 256
G = 8
B = 4
H = 8
LAT_DEV = 24
CG = 32
NLAT = 192
NLON = 180
N_LAT = 8


def draw_band_width(key, part):
    cycle_index = jnp.arange(NLAT, dtype=jnp.int32)
    distance = jnp.abs(2 * cycle_index - (NLAT - 1))
    baseline = 1 + (H - 1) * distance // max(NLAT - 1, 1)
    jitter = jax.random.randint(key, (NLAT,), -1, 2)
    widths = jnp.clip(baseline + jitter, 1, H)
    widths = widths.at[0].set(H).at[NLAT - 1].set(H).at[NLAT // 2].set(1)
    return widths.astype(jnp.int32)


def place_ends(entries, key, least, high):
    longest = entries.shape.index(max(entries.shape))
    spots = []
    for shift in (0, 1):
        where = [jax.random.randint(jax.random.fold_in(key, axis), (), 0, length) for axis, length in enumerate(entries.shape)]
        where[longest] = (where[longest] + shift) % entries.shape[longest]
        spots.append(tuple(where))
    return entries.at[spots[0]].set(least).at[spots[1]].set(high)


def shard_levels(stream_key, extent, cuts, low, high):
    gain, own = 1.0, jax.random.fold_in(stream_key, 6)
    for position, blocks in cuts:
        heights = jnp.exp(jax.random.uniform(jax.random.fold_in(own, position), (blocks,), jnp.float32, low / len(cuts), high / len(cuts)))
        gain = gain * jnp.repeat(heights, extent[position] // blocks).reshape([-1 if axis == position else 1 for axis in range(len(extent))])
    return gain


def bell_draw(key, dims, width, limit, cuts=(), kind=jnp.bfloat16):
    factor_of = shard_levels(key, dims, cuts, -0.22, 0.18) if cuts else 1.0
    drawn = jax.random.normal(key, dims, jnp.float32) * width * factor_of
    return jnp.minimum(jnp.maximum(drawn, -limit), limit).astype(kind)


def setup_inputs(seed: int = 0) -> dict:
    key_of = jax.random.split(jax.random.key(seed), 7)
    return {
        "features": bell_draw(key_of[0], (NLAT, NLON, C), 1.0, 6.0, ((0, 8), (1, 4))),
        "obs_mask": place_ends((jax.random.randint(key_of[1], (NLAT, NLON, G), 0, 2) < 1).astype(jnp.int32), jax.random.fold_in(key_of[1], 1), 0, 1),
        "filter_taps": jnp.clip(jnp.exp(jax.random.uniform(key_of[2], (NLAT, B, 3, 2 * H + 1), jnp.float32, math.log(0.049804688), math.log(1.0))), 0.049804688, 1.0).astype(jnp.bfloat16),
        "band_width": draw_band_width(jax.random.fold_in(key_of[6], 71), 0),
        "mixing": bell_draw(key_of[4], (G, B, CG, CG), (B * CG) ** -0.5, 0.5),
        "cotangent": bell_draw(key_of[5], (NLAT, NLON, C), 1.0, 6.0, ((0, 8), (1, 4))),
    }


def wrap_pad(values):
    widened = jnp.concatenate([values[:, NLON - H:], values, values[:, :H]], axis=1)
    return jnp.pad(widened, ((1, 1), (0, 0), (0, 0)))

def reference(features, obs_mask, filter_taps, band_width, mixing, cotangent):
    mask_float = obs_mask.astype(jnp.float32)
    masked = (features.astype(jnp.float32).reshape(NLAT, NLON, G, CG) * mask_float[..., None]).reshape(NLAT, NLON, C)
    offsets = jnp.arange(2 * H + 1) - H
    allowed = (jnp.abs(offsets)[None, :] <= band_width[:, None]).astype(jnp.float32)
    taps = filter_taps.astype(jnp.float32) * allowed[:, None, None, :]
    taps_pad = jnp.pad(taps, ((1, 1), (0, 0), (0, 0), (0, 0)))
    upstream = cotangent.astype(jnp.float32).reshape(NLAT, NLON, G, CG)
    masked_pad = wrap_pad(masked)
    mask_pad = wrap_pad(mask_float)
    starts = jnp.arange(N_LAT, dtype=jnp.int32) * LAT_DEV
    output_sum = jnp.zeros((NLAT, NLON, G, CG), jnp.float32)
    adjoint_sum = jnp.zeros((NLAT, NLON, C), jnp.float32)
    grad_list = []
    for basis in range(B):
        basis_mix = mixing[:, basis].astype(jnp.float32)
        basis_taps = taps[:, basis]
        padded_taps = taps_pad[:, basis]

        def forward_block(start):
            rows_in = lax.dynamic_slice_in_dim(masked_pad, start, LAT_DEV + 2, 0)
            rows_mask = lax.dynamic_slice_in_dim(mask_pad, start, LAT_DEV + 2, 0)
            block_taps = lax.dynamic_slice_in_dim(basis_taps, start, LAT_DEV, 0)
            up_rows = lax.dynamic_slice_in_dim(upstream, start, LAT_DEV, 0)
            numerator = jnp.zeros((LAT_DEV, NLON, C), jnp.float32)
            denominator = jnp.zeros((LAT_DEV, NLON, G), jnp.float32)
            for lat_step in range(3):
                for lon_step in range(2 * H + 1):
                    weight_col = block_taps[:, lat_step, lon_step][:, None, None]
                    numerator = numerator + weight_col * rows_in[lat_step:lat_step + LAT_DEV, lon_step:lon_step + NLON]
                    denominator = denominator + weight_col * rows_mask[lat_step:lat_step + LAT_DEV, lon_step:lon_step + NLON]
            safe_denom = jnp.maximum(denominator, 1.0)
            scaled = (numerator.reshape(LAT_DEV, NLON, G, CG) / safe_denom[..., None]).astype(jnp.bfloat16)
            scaled = lax.optimization_barrier(scaled).astype(jnp.float32)
            block_out = jnp.einsum('ijgc,gco->ijgo', scaled, basis_mix)
            block_grad = jnp.einsum('ijgc,ijgo->gco', scaled, up_rows)
            back_prop = jnp.einsum('ijgo,gco->ijgc', up_rows, basis_mix)
            pulled = (back_prop / safe_denom[..., None]).astype(jnp.bfloat16)
            pulled = lax.optimization_barrier(pulled).astype(jnp.float32).reshape(LAT_DEV, NLON, C)
            return (block_out, block_grad, pulled)
        block_outs, block_grads, pulled_all = lax.map(forward_block, starts)
        output_sum = output_sum + block_outs.reshape(NLAT, NLON, G, CG)
        grad_list.append(lax.optimization_barrier(jnp.sum(block_grads, axis=0)))
        pulled_pad = wrap_pad(pulled_all.reshape(NLAT, NLON, C))

        def adjoint_block(start):
            rows_grad = lax.dynamic_slice_in_dim(pulled_pad, start, LAT_DEV + 2, 0)
            rows_taps = lax.dynamic_slice_in_dim(padded_taps, start, LAT_DEV + 2, 0)
            total = jnp.zeros((LAT_DEV, NLON, C), jnp.float32)
            for lat_step in range(3):
                first = 2 - lat_step
                for lon_step in range(2 * H + 1):
                    column = 2 * H - lon_step
                    weight_col = rows_taps[first:first + LAT_DEV, lat_step, lon_step][:, None, None]
                    total = total + weight_col * rows_grad[first:first + LAT_DEV, column:column + NLON]
            return total
        adjoint_sum = adjoint_sum + lax.map(adjoint_block, starts).reshape(NLAT, NLON, C)
    infilled = output_sum.reshape(NLAT, NLON, C).astype(jnp.bfloat16)
    weight_grad = jnp.stack(grad_list, axis=1) / jnp.sqrt(jnp.float32(NLAT * NLON))
    input_grad = (adjoint_sum.reshape(NLAT, NLON, G, CG) * mask_float[..., None]).reshape(NLAT, NLON, C).astype(jnp.bfloat16)
    return (infilled, input_grad, weight_grad)
```

```python
import math

import jax
import jax.numpy as jnp
from jax import lax
from jax.sharding import PartitionSpec as P


def with_halo(block, sides, width, periodic):
    for axis, dim in sides:
        count = lax.axis_size(axis)
        forward = [(i, i + 1) for i in range(count - 1)]
        if periodic:
            forward.append((count - 1, 0))
        backward = [(target, source) for source, target in forward]
        low = lax.ppermute(
            lax.slice_in_dim(block, block.shape[dim] - width, None, axis=dim), axis, forward
        )
        high = lax.ppermute(lax.slice_in_dim(block, 0, width, axis=dim), axis, backward)
        block = jnp.concatenate([low, block, high], axis=dim)
    return block


def passed_along(block, axis, distance):
    devices = range(lax.axis_size(axis))
    route = [(i - distance, i) for i in devices if i - distance in devices]
    return lax.ppermute(block, axis, route)


def from_behind(x, axis, by):
    size = lax.axis_size(axis)
    return lax.ppermute(x, axis, [(i, (i + by) % size) for i in range(size)])


def butterfly_sum(value, axes):
    for axis in axes:
        count = lax.axis_size(axis)
        if count & (count - 1):
            value = lax.psum(value, axis)
            continue
        step = 1
        while step < count:
            partner = lax.ppermute(value, axis, [(i, i ^ step) for i in range(count)])
            value = value + partner
            step *= 2
    return value


def local(features, obs_mask, filter_taps, band_width, mixing, cotangent):
    row_count, col_count, chan_count = features.shape
    group_count = obs_mask.shape[2]
    group_width = chan_count // group_count
    basis_count = mixing.shape[1]
    tap_count = filter_taps.shape[3]
    tap_reach = (tap_count - 1) // 2
    padded_cols = col_count + 2 * tap_reach
    mask_values = obs_mask.astype(jnp.bfloat16)
    masked = (
        features.reshape(row_count, col_count, group_count, group_width) * mask_values[..., None]
    ).reshape(row_count, col_count, chan_count)
    wide_input, wide_mask = (
        with_halo(masked, (("lon", 1),), tap_reach, True),
        with_halo(mask_values, (("lon", 1),), tap_reach, True),
    )
    full_input, full_mask = (
        with_halo(wide_input, (("lat", 0),), 1, False),
        with_halo(wide_mask, (("lat", 0),), 1, False),
    )
    offsets = jnp.arange(tap_count) - tap_reach
    allowed = jnp.abs(offsets)[None, :] <= band_width[:, None]
    global_taps = filter_taps * allowed[:, None, None, :].astype(jnp.bfloat16)
    first_row = lax.axis_index("lat") * row_count
    local_taps = lax.dynamic_slice_in_dim(global_taps, first_row, row_count, 0)
    padded_index = jnp.arange(padded_cols)
    output_index = jnp.arange(col_count)
    tap_index = jnp.arange(tap_count)
    forward_table = (
        padded_index[None, :, None] - output_index[None, None, :] == tap_index[:, None, None]
    ).astype(jnp.bfloat16)
    band_blocks = jnp.einsum(
        "ibed,dpj->ibepj", local_taps, forward_table, preferred_element_type=jnp.float32
    ).astype(jnp.bfloat16)
    numerator = jnp.zeros((row_count, basis_count, col_count, chan_count), jnp.float32)
    denominator = jnp.zeros((row_count, basis_count, col_count, group_count), jnp.float32)
    for lat_step in range(3):
        band_block = band_blocks[:, :, lat_step]
        numerator = numerator + jnp.einsum(
            "ibpj,ipc->ibjc",
            band_block,
            full_input[lat_step : lat_step + row_count],
            preferred_element_type=jnp.float32,
        )
        denominator = denominator + jnp.einsum(
            "ibpj,ipg->ibjg",
            band_block,
            full_mask[lat_step : lat_step + row_count],
            preferred_element_type=jnp.float32,
        )
    safe_denom = jnp.maximum(denominator, 1.0)
    scaled = (
        numerator.reshape(row_count, basis_count, col_count, group_count, group_width)
        / safe_denom[..., None]
    ).astype(jnp.bfloat16)
    infilled = (
        jnp.einsum("ibjgc,gbco->ijgo", scaled, mixing, preferred_element_type=jnp.float32)
        .reshape(row_count, col_count, chan_count)
        .astype(jnp.bfloat16)
    )
    upstream = cotangent.reshape(row_count, col_count, group_count, group_width)
    local_grad = jnp.einsum(
        "ibjgc,ijgo->gbco", scaled, upstream, preferred_element_type=jnp.float32
    )
    cell_count = row_count * lax.axis_size("lat") * col_count * lax.axis_size("lon")
    weight_grad = butterfly_sum(local_grad, ("lon", "lat")) * (1.0 / math.sqrt(cell_count))
    back_prop = jnp.einsum("ijgo,gbco->ibjgc", upstream, mixing, preferred_element_type=jnp.float32)
    pulled = (
        (back_prop / safe_denom[..., None])
        .astype(jnp.bfloat16)
        .reshape(row_count, basis_count, col_count, chan_count)
    )
    collected = jnp.zeros((row_count + 2, padded_cols, chan_count), jnp.float32)
    for lat_step in range(3):
        term_rows = jnp.einsum(
            "ibpj,ibjc->ipc",
            band_blocks[:, :, lat_step],
            pulled,
            preferred_element_type=jnp.float32,
        )
        collected = collected.at[lat_step : lat_step + row_count].add(term_rows)
    from_below = passed_along(collected[0:1], "lat", -1)
    from_above = passed_along(collected[row_count + 1 : row_count + 2], "lat", 1)
    inner_rows = collected[1 : row_count + 1]
    inner_rows = inner_rows.at[row_count - 1 : row_count].add(from_below)
    inner_rows = inner_rows.at[0:1].add(from_above)
    left_rim = inner_rows[:, :tap_reach]
    right_rim = inner_rows[:, col_count + tap_reach :]
    from_right = from_behind(left_rim.astype(jnp.bfloat16), "lon", -1).astype(left_rim.dtype)
    from_left = from_behind(right_rim, "lon", 1)
    gathered = inner_rows[:, tap_reach : tap_reach + col_count]
    gathered = gathered.at[:, col_count - tap_reach :].add(from_right)
    gathered = gathered.at[:, :tap_reach].add(from_left)
    input_grad = (
        (gathered.reshape(row_count, col_count, group_count, group_width) * mask_values[..., None])
        .reshape(row_count, col_count, chan_count)
        .astype(jnp.bfloat16)
    )
    return (infilled, input_grad, weight_grad)


def solution(mesh):
    placed = (P("lat", "lon", None), P("lat", "lon", None), P(), P(), P(), P("lat", "lon", None))
    return jax.shard_map(
        local,
        mesh=mesh,
        in_specs=placed,
        out_specs=(P("lat", "lon", None), P("lat", "lon", None), P()),
        check_vma=False,
    )
```

```python
import math

import jax
import jax.numpy as jnp
from jax import lax
from jax.experimental import pallas as pl
from jax.experimental.pallas import tpu as pltpu
from jax.sharding import PartitionSpec as P


def with_halo(block, sides, width, periodic):
    for axis, dim in sides:
        count = lax.axis_size(axis)
        forward = [(i, i + 1) for i in range(count - 1)]
        if periodic:
            forward.append((count - 1, 0))
        backward = [(target, source) for source, target in forward]
        low = lax.ppermute(
            lax.slice_in_dim(block, block.shape[dim] - width, None, axis=dim), axis, forward
        )
        high = lax.ppermute(lax.slice_in_dim(block, 0, width, axis=dim), axis, backward)
        block = jnp.concatenate([low, block, high], axis=dim)
    return block


def passed_along(block, axis, distance):
    devices = range(lax.axis_size(axis))
    route = [(i - distance, i) for i in devices if i - distance in devices]
    return lax.ppermute(block, axis, route)


def from_behind(x, axis, by):
    size = lax.axis_size(axis)
    return lax.ppermute(x, axis, [(i, (i + by) % size) for i in range(size)])


def butterfly_sum(value, axes):
    for axis in axes:
        count = lax.axis_size(axis)
        if count & (count - 1):
            value = lax.psum(value, axis)
            continue
        step = 1
        while step < count:
            partner = lax.ppermute(value, axis, [(i, i ^ step) for i in range(count)])
            value = value + partner
            step *= 2
    return value


def conv_kernel(x_ref, m_ref, t_ref, cot_ref, w_ref, wt_ref, inf_ref, wg_ref, col_ref, pulled_ref):
    rows = t_ref.shape[0]
    basis_count = w_ref.shape[0]
    col_pad = cot_ref.shape[1]
    col_count = inf_ref.shape[1]
    lane_rows = x_ref.shape[0] // (rows + 2)
    window = 3 * lane_rows
    col_ref[...] = jnp.zeros_like(col_ref)
    wg_ref[...] = jnp.zeros_like(wg_ref)

    def body(i, carry):
        start = pl.multiple_of(i * lane_rows, lane_rows)
        band = t_ref[i]
        numerator = jnp.dot(band, x_ref[pl.ds(start, window), :], preferred_element_type=jnp.float32)
        denominator = jnp.dot(band, m_ref[pl.ds(start, window), :], preferred_element_type=jnp.float32)
        safe = jnp.maximum(denominator, 1.0)
        scaled = (numerator / safe).astype(jnp.bfloat16)
        upstream = cot_ref[i]
        out = jnp.zeros((col_pad, upstream.shape[1]), jnp.float32)
        for b in range(basis_count):
            part = scaled[b * col_pad : (b + 1) * col_pad]
            out = out + jnp.dot(part, w_ref[b], preferred_element_type=jnp.float32)
            wg_ref[b] += lax.dot_general(
                part, upstream, (((0,), (0,)), ((), ())), preferred_element_type=jnp.float32
            )
            back = jnp.dot(upstream, wt_ref[b], preferred_element_type=jnp.float32)
            pulled_ref[b * col_pad : (b + 1) * col_pad, :] = (
                back / safe[b * col_pad : (b + 1) * col_pad]
            ).astype(jnp.bfloat16)
        inf_ref[i] = out[:col_count].astype(inf_ref.dtype)
        term = lax.dot_general(
            band, pulled_ref[...], (((0,), (0,)), ((), ())), preferred_element_type=jnp.float32
        )
        col_ref[pl.ds(start, window), :] += term
        return carry

    lax.fori_loop(0, rows, body, 0)


def local(features, obs_mask, filter_taps, band_width, mixing, cotangent):
    row_count, col_count, chan_count = features.shape
    group_count = obs_mask.shape[2]
    group_width = chan_count // group_count
    basis_count = mixing.shape[1]
    tap_count = filter_taps.shape[3]
    tap_reach = (tap_count - 1) // 2
    padded_cols = col_count + 2 * tap_reach
    lane_rows = -(-padded_cols // 16) * 16
    col_pad = -(-col_count // 16) * 16
    mask_values = obs_mask.astype(jnp.bfloat16)
    masked = (
        features.reshape(row_count, col_count, group_count, group_width) * mask_values[..., None]
    ).reshape(row_count, col_count, chan_count)
    packed = jnp.concatenate([masked, mask_values], axis=-1)
    packed = with_halo(packed, (("lat", 0),), 1, False)
    packed = with_halo(packed, (("lon", 1),), tap_reach, True)
    packed = jnp.pad(packed, ((0, 0), (0, lane_rows - padded_cols), (0, 0)))
    full_input = packed[..., :chan_count].reshape((row_count + 2) * lane_rows, chan_count)
    full_mask = jnp.repeat(packed[..., chan_count:], group_width, axis=-1).reshape(
        (row_count + 2) * lane_rows, chan_count
    )

    offsets = jnp.arange(tap_count) - tap_reach
    allowed = jnp.abs(offsets)[None, :] <= band_width[:, None]
    global_taps = filter_taps * allowed[:, None, None, :].astype(jnp.bfloat16)
    first_row = lax.axis_index("lat") * row_count
    local_taps = lax.dynamic_slice_in_dim(global_taps, first_row, row_count, 0)
    padded_index = jnp.arange(lane_rows)
    output_index = jnp.arange(col_pad)
    tap_index = jnp.arange(tap_count)
    forward_table = (
        (padded_index[None, None, :] - output_index[None, :, None] == tap_index[:, None, None])
        & (output_index[None, :, None] < col_count)
    ).astype(jnp.bfloat16)
    band = (
        jnp.einsum("ibae,ejp->ibjap", local_taps, forward_table, preferred_element_type=jnp.float32)
        .astype(jnp.bfloat16)
        .reshape(row_count, basis_count * col_pad, 3 * lane_rows)
    )

    eye = jnp.eye(group_count, dtype=mixing.dtype)
    mix_blocks = jnp.einsum("gbco,gh->bgcho", mixing, eye).reshape(basis_count, chan_count, chan_count)
    mix_blocks_t = jnp.einsum("gbco,gh->bhogc", mixing, eye).reshape(
        basis_count, chan_count, chan_count
    )
    upstream = jnp.pad(cotangent, ((0, 0), (0, col_pad - col_count), (0, 0)))

    infilled, grad_blocks, collected = pl.pallas_call(
        conv_kernel,
        out_shape=(
            jax.ShapeDtypeStruct((row_count, col_count, chan_count), jnp.bfloat16),
            jax.ShapeDtypeStruct((basis_count, chan_count, chan_count), jnp.float32),
            jax.ShapeDtypeStruct(((row_count + 2) * lane_rows, chan_count), jnp.float32),
        ),
        in_specs=[pl.BlockSpec(memory_space=pltpu.VMEM)] * 6,
        out_specs=[pl.BlockSpec(memory_space=pltpu.VMEM)] * 3,
        scratch_shapes=[pltpu.VMEM((basis_count * col_pad, chan_count), jnp.bfloat16)],
        compiler_params=pltpu.CompilerParams(vmem_limit_bytes=48 * 1024 * 1024),
    )(full_input, full_mask, band, upstream, mix_blocks, mix_blocks_t)

    diagonal = jnp.eye(group_count, dtype=jnp.float32)[None, :, None, :, None]
    local_grad = jnp.sum(
        grad_blocks.reshape(basis_count, group_count, group_width, group_count, group_width)
        * diagonal,
        axis=3,
    ).transpose(1, 0, 2, 3)
    cell_count = row_count * lax.axis_size("lat") * col_count * lax.axis_size("lon")
    weight_grad = butterfly_sum(local_grad, ("lon", "lat")) * (1.0 / math.sqrt(cell_count))

    collected = collected.reshape(row_count + 2, lane_rows, chan_count)[:, :padded_cols]
    from_below = passed_along(collected[0:1], "lat", -1)
    from_above = passed_along(collected[row_count + 1 : row_count + 2], "lat", 1)
    inner_rows = collected[1 : row_count + 1]
    inner_rows = inner_rows.at[row_count - 1 : row_count].add(from_below)
    inner_rows = inner_rows.at[0:1].add(from_above)
    left_rim = inner_rows[:, :tap_reach]
    right_rim = inner_rows[:, col_count + tap_reach :]
    from_right = from_behind(left_rim.astype(jnp.bfloat16), "lon", -1).astype(left_rim.dtype)
    from_left = from_behind(right_rim, "lon", 1)
    gathered = inner_rows[:, tap_reach : tap_reach + col_count]
    gathered = gathered.at[:, col_count - tap_reach :].add(from_right)
    gathered = gathered.at[:, :tap_reach].add(from_left)
    input_grad = (
        (gathered.reshape(row_count, col_count, group_count, group_width) * mask_values[..., None])
        .reshape(row_count, col_count, chan_count)
        .astype(jnp.bfloat16)
    )
    return (infilled, input_grad, weight_grad)


def solution(mesh):
    placed = (P("lat", "lon", None), P("lat", "lon", None), P(), P(), P(), P("lat", "lon", None))
    return jax.shard_map(
        local,
        mesh=mesh,
        in_specs=placed,
        out_specs=(P("lat", "lon", None), P("lat", "lon", None), P()),
        check_vma=False,
    )
```

```python
import math

import jax
import jax.numpy as jnp
from jax import lax
from jax.experimental import pallas as pl
from jax.experimental.pallas import tpu as pltpu
from jax.sharding import PartitionSpec as P


def with_halo(block, sides, width, periodic):
    for axis, dim in sides:
        count = lax.axis_size(axis)
        forward = [(i, i + 1) for i in range(count - 1)]
        if periodic:
            forward.append((count - 1, 0))
        backward = [(target, source) for source, target in forward]
        low = lax.ppermute(
            lax.slice_in_dim(block, block.shape[dim] - width, None, axis=dim), axis, forward
        )
        high = lax.ppermute(lax.slice_in_dim(block, 0, width, axis=dim), axis, backward)
        block = jnp.concatenate([low, block, high], axis=dim)
    return block


def passed_along(block, axis, distance):
    devices = range(lax.axis_size(axis))
    route = [(i - distance, i) for i in devices if i - distance in devices]
    return lax.ppermute(block, axis, route)


def from_behind(x, axis, by):
    size = lax.axis_size(axis)
    return lax.ppermute(x, axis, [(i, (i + by) % size) for i in range(size)])


def butterfly_sum(value, axes):
    for axis in axes:
        count = lax.axis_size(axis)
        if count & (count - 1):
            value = lax.psum(value, axis)
            continue
        step = 1
        while step < count:
            partner = lax.ppermute(value, axis, [(i, i ^ step) for i in range(count)])
            value = value + partner
            step *= 2
    return value


def conv_kernel(x_ref, m_ref, t_ref, cot_ref, w_ref, wt_ref, inf_ref, wg_ref, col_ref, pulled_ref):
    rows, basis_count, lat_taps, col_pad, lane_rows = t_ref.shape
    col_count = inf_ref.shape[1]
    col_ref[...] = jnp.zeros_like(col_ref)
    wg_ref[...] = jnp.zeros_like(wg_ref)

    def body(i, carry):
        bands = [t_ref[i, :, a].reshape(basis_count * col_pad, lane_rows) for a in range(lat_taps)]
        numerator = None
        denominator = None
        for a in range(lat_taps):
            start = pl.multiple_of((i + a) * lane_rows, lane_rows)
            num = jnp.dot(bands[a], x_ref[pl.ds(start, lane_rows), :], preferred_element_type=jnp.float32)
            den = jnp.dot(bands[a], m_ref[pl.ds(start, lane_rows), :], preferred_element_type=jnp.float32)
            numerator = num if numerator is None else numerator + num
            denominator = den if denominator is None else denominator + den
        safe = jnp.maximum(denominator, 1.0)
        scaled = (numerator / safe).astype(jnp.bfloat16)
        upstream = cot_ref[i]
        out = jnp.zeros((col_pad, upstream.shape[1]), jnp.float32)
        for b in range(basis_count):
            part = scaled[b * col_pad : (b + 1) * col_pad]
            out = out + jnp.dot(part, w_ref[b], preferred_element_type=jnp.float32)
            wg_ref[b] += lax.dot_general(
                part, upstream, (((0,), (0,)), ((), ())), preferred_element_type=jnp.float32
            )
            back = jnp.dot(upstream, wt_ref[b], preferred_element_type=jnp.float32)
            pulled_ref[b * col_pad : (b + 1) * col_pad, :] = (
                back / safe[b * col_pad : (b + 1) * col_pad]
            ).astype(jnp.bfloat16)
        inf_ref[i] = out[:col_count].astype(inf_ref.dtype)
        pulled = pulled_ref[...]
        for a in range(lat_taps):
            start = pl.multiple_of((i + a) * lane_rows, lane_rows)
            term = lax.dot_general(
                bands[a], pulled, (((0,), (0,)), ((), ())), preferred_element_type=jnp.float32
            )
            col_ref[pl.ds(start, lane_rows), :] += term
        return carry

    lax.fori_loop(0, rows, body, 0)


def local(features, obs_mask, filter_taps, band_width, mixing, cotangent):
    row_count, col_count, chan_count = features.shape
    group_count = obs_mask.shape[2]
    group_width = chan_count // group_count
    basis_count = mixing.shape[1]
    tap_count = filter_taps.shape[3]
    tap_reach = (tap_count - 1) // 2
    padded_cols = col_count + 2 * tap_reach
    lane_rows = -(-padded_cols // 16) * 16
    col_pad = -(-col_count // 16) * 16
    mask_values = obs_mask.astype(jnp.bfloat16)
    masked = (
        features.reshape(row_count, col_count, group_count, group_width) * mask_values[..., None]
    ).reshape(row_count, col_count, chan_count)
    packed = jnp.concatenate([masked, mask_values], axis=-1)
    packed = with_halo(packed, (("lat", 0),), 1, False)
    packed = with_halo(packed, (("lon", 1),), tap_reach, True)
    packed = jnp.pad(packed, ((0, 0), (0, lane_rows - padded_cols), (0, 0)))
    full_input = packed[..., :chan_count].reshape((row_count + 2) * lane_rows, chan_count)
    full_mask = jnp.repeat(packed[..., chan_count:], group_width, axis=-1).reshape(
        (row_count + 2) * lane_rows, chan_count
    )

    offsets = jnp.arange(tap_count) - tap_reach
    allowed = jnp.abs(offsets)[None, :] <= band_width[:, None]
    global_taps = filter_taps * allowed[:, None, None, :].astype(jnp.bfloat16)
    first_row = lax.axis_index("lat") * row_count
    local_taps = lax.dynamic_slice_in_dim(global_taps, first_row, row_count, 0)
    padded_index = jnp.arange(lane_rows)
    output_index = jnp.arange(col_pad)
    tap_index = jnp.arange(tap_count)
    forward_table = (
        (padded_index[None, None, :] - output_index[None, :, None] == tap_index[:, None, None])
        & (output_index[None, :, None] < col_count)
    ).astype(jnp.bfloat16)
    band = (
        jnp.einsum("ibae,ejp->ibajp", local_taps, forward_table, preferred_element_type=jnp.float32)
        .astype(jnp.bfloat16)
    )

    eye = jnp.eye(group_count, dtype=mixing.dtype)
    mix_blocks = jnp.einsum("gbco,gh->bgcho", mixing, eye).reshape(basis_count, chan_count, chan_count)
    mix_blocks_t = jnp.einsum("gbco,gh->bhogc", mixing, eye).reshape(
        basis_count, chan_count, chan_count
    )
    upstream = jnp.pad(cotangent, ((0, 0), (0, col_pad - col_count), (0, 0)))

    infilled, grad_blocks, collected = pl.pallas_call(
        conv_kernel,
        out_shape=(
            jax.ShapeDtypeStruct((row_count, col_count, chan_count), jnp.bfloat16),
            jax.ShapeDtypeStruct((basis_count, chan_count, chan_count), jnp.float32),
            jax.ShapeDtypeStruct(((row_count + 2) * lane_rows, chan_count), jnp.float32),
        ),
        in_specs=[pl.BlockSpec(memory_space=pltpu.VMEM)] * 6,
        out_specs=[pl.BlockSpec(memory_space=pltpu.VMEM)] * 3,
        scratch_shapes=[pltpu.VMEM((basis_count * col_pad, chan_count), jnp.bfloat16)],
        compiler_params=pltpu.CompilerParams(vmem_limit_bytes=48 * 1024 * 1024),
    )(full_input, full_mask, band, upstream, mix_blocks, mix_blocks_t)

    diagonal = jnp.eye(group_count, dtype=jnp.float32)[None, :, None, :, None]
    local_grad = jnp.sum(
        grad_blocks.reshape(basis_count, group_count, group_width, group_count, group_width)
        * diagonal,
        axis=3,
    ).transpose(1, 0, 2, 3)
    cell_count = row_count * lax.axis_size("lat") * col_count * lax.axis_size("lon")
    dense = butterfly_sum(local_grad.reshape(-1, 128), ("lon", "lat"))
    weight_grad = dense.reshape(local_grad.shape) * (1.0 / math.sqrt(cell_count))

    collected = collected.reshape(row_count + 2, lane_rows, chan_count)[:, :padded_cols]
    from_below = passed_along(collected[0:1], "lat", -1)
    from_above = passed_along(collected[row_count + 1 : row_count + 2], "lat", 1)
    inner_rows = collected[1 : row_count + 1]
    inner_rows = inner_rows.at[row_count - 1 : row_count].add(from_below)
    inner_rows = inner_rows.at[0:1].add(from_above)
    left_rim = inner_rows[:, :tap_reach]
    right_rim = inner_rows[:, col_count + tap_reach :]
    from_right = from_behind(left_rim.astype(jnp.bfloat16), "lon", -1).astype(left_rim.dtype)
    from_left = from_behind(right_rim, "lon", 1)
    gathered = inner_rows[:, tap_reach : tap_reach + col_count]
    gathered = gathered.at[:, col_count - tap_reach :].add(from_right)
    gathered = gathered.at[:, :tap_reach].add(from_left)
    input_grad = (
        (gathered.reshape(row_count, col_count, group_count, group_width) * mask_values[..., None])
        .reshape(row_count, col_count, chan_count)
        .astype(jnp.bfloat16)
    )
    return (infilled, input_grad, weight_grad)


def solution(mesh):
    placed = (P("lat", "lon", None), P("lat", "lon", None), P(), P(), P(), P("lat", "lon", None))
    return jax.shard_map(
        local,
        mesh=mesh,
        in_specs=placed,
        out_specs=(P("lat", "lon", None), P("lat", "lon", None), P()),
        check_vma=False,
    )
```

```python
import math

import jax
import jax.numpy as jnp
from jax import lax
from jax.experimental import pallas as pl
from jax.experimental.pallas import tpu as pltpu
from jax.sharding import PartitionSpec as P


def with_halo(block, sides, width, periodic):
    for axis, dim in sides:
        count = lax.axis_size(axis)
        forward = [(i, i + 1) for i in range(count - 1)]
        if periodic:
            forward.append((count - 1, 0))
        backward = [(target, source) for source, target in forward]
        low = lax.ppermute(
            lax.slice_in_dim(block, block.shape[dim] - width, None, axis=dim), axis, forward
        )
        high = lax.ppermute(lax.slice_in_dim(block, 0, width, axis=dim), axis, backward)
        block = jnp.concatenate([low, block, high], axis=dim)
    return block


def passed_along(block, axis, distance):
    devices = range(lax.axis_size(axis))
    route = [(i - distance, i) for i in devices if i - distance in devices]
    return lax.ppermute(block, axis, route)


def from_behind(x, axis, by):
    size = lax.axis_size(axis)
    return lax.ppermute(x, axis, [(i, (i + by) % size) for i in range(size)])


def butterfly_sum(value, axes):
    for axis in axes:
        count = lax.axis_size(axis)
        if count & (count - 1):
            value = lax.psum(value, axis)
            continue
        step = 1
        while step < count:
            partner = lax.ppermute(value, axis, [(i, i ^ step) for i in range(count)])
            value = value + partner
            step *= 2
    return value


def conv_kernel(x_ref, m_ref, t_ref, cot_ref, w_ref, wt_ref, inf_ref, wg_ref, col_ref, pulled_ref):
    rows, basis_count, lat_taps, col_pad, lane_rows = t_ref.shape
    col_count = inf_ref.shape[1]
    col_ref[...] = jnp.zeros_like(col_ref)
    wg_ref[...] = jnp.zeros_like(wg_ref)

    def body(i, carry):
        bands = [t_ref[i, :, a].reshape(basis_count * col_pad, lane_rows) for a in range(lat_taps)]
        numerator = None
        denominator = None
        for a in range(lat_taps):
            start = pl.multiple_of((i + a) * lane_rows, lane_rows)
            num = jnp.dot(bands[a], x_ref[pl.ds(start, lane_rows), :], preferred_element_type=jnp.float32)
            den = jnp.dot(bands[a], m_ref[pl.ds(start, lane_rows), :], preferred_element_type=jnp.float32)
            numerator = num if numerator is None else numerator + num
            denominator = den if denominator is None else denominator + den
        safe = jnp.maximum(denominator, 1.0)
        scaled = (numerator / safe).astype(jnp.bfloat16)
        upstream = cot_ref[i]
        out = jnp.zeros((col_pad, upstream.shape[1]), jnp.float32)
        for b in range(basis_count):
            part = scaled[b * col_pad : (b + 1) * col_pad]
            out = out + jnp.dot(part, w_ref[b], preferred_element_type=jnp.float32)
            wg_ref[b] += lax.dot_general(
                part, upstream, (((0,), (0,)), ((), ())), preferred_element_type=jnp.float32
            )
            back = jnp.dot(upstream, wt_ref[b], preferred_element_type=jnp.float32)
            pulled_ref[b * col_pad : (b + 1) * col_pad, :] = (
                back / safe[b * col_pad : (b + 1) * col_pad]
            ).astype(jnp.bfloat16)
        inf_ref[i] = out[:col_count].astype(inf_ref.dtype)
        pulled = pulled_ref[...]
        for a in range(lat_taps):
            start = pl.multiple_of((i + a) * lane_rows, lane_rows)
            term = lax.dot_general(
                bands[a], pulled, (((0,), (0,)), ((), ())), preferred_element_type=jnp.float32
            )
            col_ref[pl.ds(start, lane_rows), :] += term
        return carry

    lax.fori_loop(0, rows, body, 0)


def local(features, obs_mask, filter_taps, band_width, mixing, cotangent):
    row_count, col_count, chan_count = features.shape
    group_count = obs_mask.shape[2]
    group_width = chan_count // group_count
    basis_count = mixing.shape[1]
    tap_count = filter_taps.shape[3]
    tap_reach = (tap_count - 1) // 2
    padded_cols = col_count + 2 * tap_reach
    lane_rows = -(-padded_cols // 16) * 16
    col_pad = -(-col_count // 16) * 16
    mask_values = obs_mask.astype(jnp.bfloat16)
    masked = (
        features.reshape(row_count, col_count, group_count, group_width) * mask_values[..., None]
    ).reshape(row_count, col_count, chan_count)
    packed = jnp.concatenate([masked, mask_values], axis=-1)
    packed = with_halo(packed, (("lat", 0),), 1, False)
    packed = with_halo(packed, (("lon", 1),), tap_reach, True)
    packed = jnp.pad(packed, ((0, 0), (0, lane_rows - padded_cols), (0, 0)))
    full_input = packed[..., :chan_count].reshape((row_count + 2) * lane_rows, chan_count)
    full_mask = jnp.repeat(packed[..., chan_count:], group_width, axis=-1).reshape(
        (row_count + 2) * lane_rows, chan_count
    )

    offsets = jnp.arange(tap_count) - tap_reach
    allowed = jnp.abs(offsets)[None, :] <= band_width[:, None]
    global_taps = filter_taps * allowed[:, None, None, :].astype(jnp.bfloat16)
    first_row = lax.axis_index("lat") * row_count
    local_taps = lax.dynamic_slice_in_dim(global_taps, first_row, row_count, 0)
    padded_index = jnp.arange(lane_rows)
    output_index = jnp.arange(col_pad)
    tap_index = jnp.arange(tap_count)
    forward_table = (
        (padded_index[None, None, :] - output_index[None, :, None] == tap_index[:, None, None])
        & (output_index[None, :, None] < col_count)
    ).astype(jnp.bfloat16)
    band = (
        jnp.einsum("ibae,ejp->ibajp", local_taps, forward_table, preferred_element_type=jnp.float32)
        .astype(jnp.bfloat16)
    )

    eye = jnp.eye(group_count, dtype=mixing.dtype)
    mix_blocks = jnp.einsum("gbco,gh->bgcho", mixing, eye).reshape(basis_count, chan_count, chan_count)
    mix_blocks_t = jnp.einsum("gbco,gh->bhogc", mixing, eye).reshape(
        basis_count, chan_count, chan_count
    )
    upstream = jnp.pad(cotangent, ((0, 0), (0, col_pad - col_count), (0, 0)))

    infilled, grad_blocks, collected = pl.pallas_call(
        conv_kernel,
        out_shape=(
            jax.ShapeDtypeStruct((row_count, col_count, chan_count), jnp.bfloat16),
            jax.ShapeDtypeStruct((basis_count, chan_count, chan_count), jnp.float32),
            jax.ShapeDtypeStruct(((row_count + 2) * lane_rows, chan_count), jnp.float32),
        ),
        in_specs=[pl.BlockSpec(memory_space=pltpu.VMEM)] * 6,
        out_specs=[pl.BlockSpec(memory_space=pltpu.VMEM)] * 3,
        scratch_shapes=[pltpu.VMEM((basis_count * col_pad, chan_count), jnp.bfloat16)],
        compiler_params=pltpu.CompilerParams(vmem_limit_bytes=48 * 1024 * 1024),
    )(full_input, full_mask, band, upstream, mix_blocks, mix_blocks_t)

    diagonal = jnp.eye(group_count, dtype=jnp.float32)[None, :, None, :, None]
    local_grad = jnp.sum(
        grad_blocks.reshape(basis_count, group_count, group_width, group_count, group_width)
        * diagonal,
        axis=3,
    ).transpose(1, 0, 2, 3)
    cell_count = row_count * lax.axis_size("lat") * col_count * lax.axis_size("lon")
    dense = lax.psum(local_grad.reshape(-1, 128), ("lat", "lon"))
    weight_grad = dense.reshape(local_grad.shape) * (1.0 / math.sqrt(cell_count))

    collected = collected.reshape(row_count + 2, lane_rows, chan_count)[:, :padded_cols]
    from_below = passed_along(collected[0:1], "lat", -1)
    from_above = passed_along(collected[row_count + 1 : row_count + 2], "lat", 1)
    inner_rows = collected[1 : row_count + 1]
    inner_rows = inner_rows.at[row_count - 1 : row_count].add(from_below)
    inner_rows = inner_rows.at[0:1].add(from_above)
    left_rim = inner_rows[:, :tap_reach]
    right_rim = inner_rows[:, col_count + tap_reach :]
    from_right = from_behind(left_rim.astype(jnp.bfloat16), "lon", -1).astype(left_rim.dtype)
    from_left = from_behind(right_rim, "lon", 1)
    gathered = inner_rows[:, tap_reach : tap_reach + col_count]
    gathered = gathered.at[:, col_count - tap_reach :].add(from_right)
    gathered = gathered.at[:, :tap_reach].add(from_left)
    input_grad = (
        (gathered.reshape(row_count, col_count, group_count, group_width) * mask_values[..., None])
        .reshape(row_count, col_count, chan_count)
        .astype(jnp.bfloat16)
    )
    return (infilled, input_grad, weight_grad)


def solution(mesh):
    placed = (P("lat", "lon", None), P("lat", "lon", None), P(), P(), P(), P("lat", "lon", None))
    return jax.shard_map(
        local,
        mesh=mesh,
        in_specs=placed,
        out_specs=(P("lat", "lon", None), P("lat", "lon", None), P()),
        check_vma=False,
    )
```

```python
import math

import jax
import jax.numpy as jnp
from jax import lax
from jax.experimental import pallas as pl
from jax.experimental.pallas import tpu as pltpu
from jax.sharding import PartitionSpec as P


def with_halo(block, sides, width, periodic):
    for axis, dim in sides:
        count = lax.axis_size(axis)
        forward = [(i, i + 1) for i in range(count - 1)]
        if periodic:
            forward.append((count - 1, 0))
        backward = [(target, source) for source, target in forward]
        low = lax.ppermute(
            lax.slice_in_dim(block, block.shape[dim] - width, None, axis=dim), axis, forward
        )
        high = lax.ppermute(lax.slice_in_dim(block, 0, width, axis=dim), axis, backward)
        block = jnp.concatenate([low, block, high], axis=dim)
    return block


def passed_along(block, axis, distance):
    devices = range(lax.axis_size(axis))
    route = [(i - distance, i) for i in devices if i - distance in devices]
    return lax.ppermute(block, axis, route)


def from_behind(x, axis, by):
    size = lax.axis_size(axis)
    return lax.ppermute(x, axis, [(i, (i + by) % size) for i in range(size)])


def butterfly_sum(value, axes, skip=0):
    for axis in axes:
        count = lax.axis_size(axis)
        if count & (count - 1):
            value = lax.psum(value, axis)
            continue
        step = 1
        while step < count:
            if skip:
                skip -= 1
                step *= 2
                continue
            partner = lax.ppermute(value, axis, [(i, i ^ step) for i in range(count)])
            value = value + partner
            step *= 2
    return value


def forward_kernel(x_ref, m_ref, t_ref, cot_ref, w_ref, wt_ref, inf_ref, wg_ref, pulled_ref, acc_ref):
    rows, basis_count, lat_taps, col_pad, lane_rows = t_ref.shape
    col_count = inf_ref.shape[1]
    chan_count = w_ref.shape[1]
    group_width = wg_ref.shape[1]
    acc_ref[...] = jnp.zeros_like(acc_ref)

    def body(i, carry):
        numerator = None
        denominator = None
        for a in range(lat_taps):
            band = t_ref[i, :, a].reshape(basis_count * col_pad, lane_rows)
            start = pl.multiple_of((i + a) * lane_rows, lane_rows)
            num = jnp.dot(band, x_ref[pl.ds(start, lane_rows), :], preferred_element_type=jnp.float32)
            den = jnp.dot(band, m_ref[pl.ds(start, lane_rows), :], preferred_element_type=jnp.float32)
            numerator = num if numerator is None else numerator + num
            denominator = den if denominator is None else denominator + den
        safe = jnp.maximum(denominator, 1.0)
        scaled = (numerator / safe).astype(jnp.bfloat16)
        upstream = cot_ref[i]
        out = jnp.zeros((col_pad, chan_count), jnp.float32)
        for b in range(basis_count):
            part = scaled[b * col_pad : (b + 1) * col_pad]
            out = out + jnp.dot(part, w_ref[b], preferred_element_type=jnp.float32)
            acc_ref[b] += lax.dot_general(
                part, upstream, (((0,), (0,)), ((), ())), preferred_element_type=jnp.float32
            )
            back = jnp.dot(upstream, wt_ref[b], preferred_element_type=jnp.float32)
            pulled_ref[i, b * col_pad : (b + 1) * col_pad, :] = (
                back / safe[b * col_pad : (b + 1) * col_pad]
            ).astype(jnp.bfloat16)
        inf_ref[i] = out[:col_count].astype(inf_ref.dtype)
        return carry

    lax.fori_loop(0, rows, body, 0)
    lane = lax.broadcasted_iota(jnp.int32, (group_width, chan_count), 1) // group_width
    for b in range(basis_count):
        total = jnp.zeros((group_width, chan_count), jnp.float32)
        for g in range(chan_count // group_width):
            block = acc_ref[b, g * group_width : (g + 1) * group_width, :]
            total = total + jnp.where(lane == g, block, 0.0)
        wg_ref[b] = total


def adjoint_kernel(t_ref, pulled_ref, order_ref, col_ref):
    rows, basis_count, lat_taps, col_pad, lane_rows = t_ref.shape
    col_ref[...] = jnp.zeros_like(col_ref)

    def body(i, carry):
        pulled = pulled_ref[i]
        for a in range(lat_taps):
            band = t_ref[i, :, a].reshape(basis_count * col_pad, lane_rows)
            start = pl.multiple_of((i + a) * lane_rows, lane_rows)
            term = lax.dot_general(
                band, pulled, (((0,), (0,)), ((), ())), preferred_element_type=jnp.float32
            )
            col_ref[pl.ds(start, lane_rows), :] += term
        return carry

    lax.fori_loop(0, rows, body, 0)


def local(features, obs_mask, filter_taps, band_width, mixing, cotangent):
    row_count, col_count, chan_count = features.shape
    group_count = obs_mask.shape[2]
    group_width = chan_count // group_count
    basis_count = mixing.shape[1]
    tap_count = filter_taps.shape[3]
    tap_reach = (tap_count - 1) // 2
    padded_cols = col_count + 2 * tap_reach
    lane_rows = -(-padded_cols // 16) * 16
    col_pad = -(-col_count // 16) * 16
    mask_values = obs_mask.astype(jnp.bfloat16)
    masked = (
        features.reshape(row_count, col_count, group_count, group_width) * mask_values[..., None]
    ).reshape(row_count, col_count, chan_count)
    packed = jnp.concatenate([masked, mask_values], axis=-1)
    packed = with_halo(packed, (("lat", 0),), 1, False)
    packed = with_halo(packed, (("lon", 1),), tap_reach, True)
    packed = jnp.pad(packed, ((0, 0), (0, lane_rows - padded_cols), (0, 0)))
    full_input = packed[..., :chan_count].reshape((row_count + 2) * lane_rows, chan_count)
    full_mask = jnp.repeat(packed[..., chan_count:], group_width, axis=-1).reshape(
        (row_count + 2) * lane_rows, chan_count
    )

    offsets = jnp.arange(tap_count) - tap_reach
    allowed = jnp.abs(offsets)[None, :] <= band_width[:, None]
    global_taps = filter_taps * allowed[:, None, None, :].astype(jnp.bfloat16)
    first_row = lax.axis_index("lat") * row_count
    local_taps = lax.dynamic_slice_in_dim(global_taps, first_row, row_count, 0)
    padded_index = jnp.arange(lane_rows)
    output_index = jnp.arange(col_pad)
    tap_index = jnp.arange(tap_count)
    forward_table = (
        (padded_index[None, None, :] - output_index[None, :, None] == tap_index[:, None, None])
        & (output_index[None, :, None] < col_count)
    ).astype(jnp.bfloat16)
    band = (
        jnp.einsum("ibae,ejp->ibajp", local_taps, forward_table, preferred_element_type=jnp.float32)
        .astype(jnp.bfloat16)
    )

    eye = jnp.eye(group_count, dtype=mixing.dtype)
    mix_blocks = jnp.einsum("gbco,gh->bgcho", mixing, eye).reshape(basis_count, chan_count, chan_count)
    mix_blocks_t = jnp.einsum("gbco,gh->bhogc", mixing, eye).reshape(
        basis_count, chan_count, chan_count
    )
    upstream = jnp.pad(cotangent, ((0, 0), (0, col_pad - col_count), (0, 0)))

    vmem = pl.BlockSpec(memory_space=pltpu.VMEM)
    params = pltpu.CompilerParams(vmem_limit_bytes=48 * 1024 * 1024)
    infilled, grad_blocks, pulled = pl.pallas_call(
        forward_kernel,
        out_shape=(
            jax.ShapeDtypeStruct((row_count, col_count, chan_count), jnp.bfloat16),
            jax.ShapeDtypeStruct((basis_count, group_width, chan_count), jnp.float32),
            jax.ShapeDtypeStruct((row_count, basis_count * col_pad, chan_count), jnp.bfloat16),
        ),
        in_specs=[vmem] * 6,
        out_specs=[vmem] * 3,
        scratch_shapes=[pltpu.VMEM((basis_count, chan_count, chan_count), jnp.float32)],
        compiler_params=params,
        cost_estimate=pl.CostEstimate(
            flops=2 * row_count * basis_count * col_pad * chan_count * (6 * lane_rows + 3 * chan_count),
            transcendentals=0,
            bytes_accessed=8 * (row_count + 2) * lane_rows * chan_count,
        ),
    )(full_input, full_mask, band, upstream, mix_blocks, mix_blocks_t)

    cell_count = row_count * lax.axis_size("lat") * col_count * lax.axis_size("lon")
    lat_count = lax.axis_size("lat")
    if lat_count % 2 == 0:
        first = lax.ppermute(grad_blocks, "lat", [(i, i ^ 1) for i in range(lat_count)])
        dense = butterfly_sum(grad_blocks + first, ("lat", "lon"), skip=1)
    else:
        first = grad_blocks
        dense = butterfly_sum(grad_blocks, ("lat", "lon"))
    dense = dense * (1.0 / math.sqrt(cell_count))
    weight_grad = dense.reshape(basis_count, group_width, group_count, group_width).transpose(2, 0, 1, 3)

    collected = pl.pallas_call(
        adjoint_kernel,
        out_shape=jax.ShapeDtypeStruct(((row_count + 2) * lane_rows, chan_count), jnp.float32),
        in_specs=[vmem, vmem, pl.BlockSpec(memory_space=pl.ANY)],
        out_specs=vmem,
        compiler_params=params,
        cost_estimate=pl.CostEstimate(
            flops=6 * row_count * basis_count * col_pad * lane_rows * chan_count,
            transcendentals=0,
            bytes_accessed=6 * (row_count + 2) * lane_rows * chan_count,
        ),
    )(band, pulled, first)

    collected = collected.reshape(row_count + 2, lane_rows, chan_count)[:, :padded_cols]
    from_below = passed_along(collected[0:1], "lat", -1)
    from_above = passed_along(collected[row_count + 1 : row_count + 2], "lat", 1)
    inner_rows = collected[1 : row_count + 1]
    inner_rows = inner_rows.at[row_count - 1 : row_count].add(from_below)
    inner_rows = inner_rows.at[0:1].add(from_above)
    left_rim = inner_rows[:, :tap_reach]
    right_rim = inner_rows[:, col_count + tap_reach :]
    from_right = from_behind(left_rim.astype(jnp.bfloat16), "lon", -1).astype(left_rim.dtype)
    from_left = from_behind(right_rim, "lon", 1)
    gathered = inner_rows[:, tap_reach : tap_reach + col_count]
    gathered = gathered.at[:, col_count - tap_reach :].add(from_right)
    gathered = gathered.at[:, :tap_reach].add(from_left)
    input_grad = (
        (gathered.reshape(row_count, col_count, group_count, group_width) * mask_values[..., None])
        .reshape(row_count, col_count, chan_count)
        .astype(jnp.bfloat16)
    )
    return (infilled, input_grad, weight_grad)


def solution(mesh):
    placed = (P("lat", "lon", None), P("lat", "lon", None), P(), P(), P(), P("lat", "lon", None))
    return jax.shard_map(
        local,
        mesh=mesh,
        in_specs=placed,
        out_specs=(P("lat", "lon", None), P("lat", "lon", None), P()),
        check_vma=False,
    )
```

```python
import math

import jax
import jax.numpy as jnp
from jax import lax
from jax.experimental import pallas as pl
from jax.experimental.pallas import tpu as pltpu
from jax.sharding import PartitionSpec as P


def with_halo(block, sides, width, periodic):
    for axis, dim in sides:
        count = lax.axis_size(axis)
        forward = [(i, i + 1) for i in range(count - 1)]
        if periodic:
            forward.append((count - 1, 0))
        backward = [(target, source) for source, target in forward]
        low = lax.ppermute(
            lax.slice_in_dim(block, block.shape[dim] - width, None, axis=dim), axis, forward
        )
        high = lax.ppermute(lax.slice_in_dim(block, 0, width, axis=dim), axis, backward)
        block = jnp.concatenate([low, block, high], axis=dim)
    return block


def passed_along(block, axis, distance):
    devices = range(lax.axis_size(axis))
    route = [(i - distance, i) for i in devices if i - distance in devices]
    return lax.ppermute(block, axis, route)


def from_behind(x, axis, by):
    size = lax.axis_size(axis)
    return lax.ppermute(x, axis, [(i, (i + by) % size) for i in range(size)])


def butterfly_sum(value, axes, skip=0):
    for axis in axes:
        count = lax.axis_size(axis)
        if count & (count - 1):
            value = lax.psum(value, axis)
            continue
        step = 1
        while step < count:
            if skip:
                skip -= 1
                step *= 2
                continue
            partner = lax.ppermute(value, axis, [(i, i ^ step) for i in range(count)])
            value = value + partner
            step *= 2
    return value


def forward_kernel(x_ref, m_ref, t_ref, cot_ref, w_ref, wt_ref, inf_ref, wg_ref, pulled_ref, acc_ref):
    rows, basis_count, lat_taps, col_pad, lane_rows = t_ref.shape
    col_count = inf_ref.shape[1]
    chan_count = w_ref.shape[1]
    group_width = wg_ref.shape[1]
    acc_ref[...] = jnp.zeros_like(acc_ref)

    def body(i, carry):
        numerator = None
        denominator = None
        for a in range(lat_taps):
            band = t_ref[i, :, a].reshape(basis_count * col_pad, lane_rows)
            start = pl.multiple_of((i + a) * lane_rows, lane_rows)
            num = jnp.dot(band, x_ref[pl.ds(start, lane_rows), :], preferred_element_type=jnp.float32)
            den = jnp.dot(band, m_ref[pl.ds(start, lane_rows), :], preferred_element_type=jnp.float32)
            numerator = num if numerator is None else numerator + num
            denominator = den if denominator is None else denominator + den
        safe = jnp.maximum(denominator, 1.0)
        scaled = (numerator / safe).astype(jnp.bfloat16)
        upstream = cot_ref[i]
        out = jnp.zeros((col_pad, chan_count), jnp.float32)
        for b in range(basis_count):
            part = scaled[b * col_pad : (b + 1) * col_pad]
            out = out + jnp.dot(part, w_ref[b], preferred_element_type=jnp.float32)
            acc_ref[b] += lax.dot_general(
                part, upstream, (((0,), (0,)), ((), ())), preferred_element_type=jnp.float32
            )
            back = jnp.dot(upstream, wt_ref[b], preferred_element_type=jnp.float32)
            pulled_ref[i, b * col_pad : (b + 1) * col_pad, :] = (
                back / safe[b * col_pad : (b + 1) * col_pad]
            ).astype(jnp.bfloat16)
        inf_ref[i] = out[:col_count].astype(inf_ref.dtype)
        return carry

    lax.fori_loop(0, rows, body, 0)
    lane = lax.broadcasted_iota(jnp.int32, (group_width, chan_count), 1) // group_width
    for b in range(basis_count):
        total = jnp.zeros((group_width, chan_count), jnp.float32)
        for g in range(chan_count // group_width):
            block = acc_ref[b, g * group_width : (g + 1) * group_width, :]
            total = total + jnp.where(lane == g, block, 0.0)
        wg_ref[b] = total


def adjoint_kernel(t_ref, pulled_ref, order_ref, col_ref):
    rows, basis_count, lat_taps, col_pad, lane_rows = t_ref.shape
    col_ref[...] = jnp.zeros_like(col_ref)

    def body(i, carry):
        pulled = pulled_ref[i]
        for a in range(lat_taps):
            band = t_ref[i, :, a].reshape(basis_count * col_pad, lane_rows)
            start = pl.multiple_of((i + a) * lane_rows, lane_rows)
            term = lax.dot_general(
                band, pulled, (((0,), (0,)), ((), ())), preferred_element_type=jnp.float32
            )
            col_ref[pl.ds(start, lane_rows), :] += term
        return carry

    lax.fori_loop(0, rows, body, 0)


def local(features, obs_mask, filter_taps, band_width, mixing, cotangent):
    row_count, col_count, chan_count = features.shape
    group_count = obs_mask.shape[2]
    group_width = chan_count // group_count
    basis_count = mixing.shape[1]
    tap_count = filter_taps.shape[3]
    tap_reach = (tap_count - 1) // 2
    padded_cols = col_count + 2 * tap_reach
    lane_rows = -(-padded_cols // 16) * 16
    col_pad = -(-col_count // 16) * 16
    mask_values = obs_mask.astype(jnp.bfloat16)
    spread = (
        jnp.arange(chan_count)[None, :] // group_width == jnp.arange(group_count)[:, None]
    ).astype(jnp.bfloat16)
    own_mask = jnp.dot(
        mask_values.reshape(row_count * col_count, group_count), spread,
        preferred_element_type=jnp.float32,
    ).astype(jnp.bfloat16).reshape(row_count, col_count, chan_count)
    masked = features * own_mask
    packed = jnp.concatenate([masked, mask_values], axis=-1)
    packed = with_halo(packed, (("lat", 0),), 1, False)
    packed = with_halo(packed, (("lon", 1),), tap_reach, True)
    packed = jnp.pad(packed, ((0, 0), (0, lane_rows - padded_cols), (0, 0)))
    full_input = packed[..., :chan_count].reshape((row_count + 2) * lane_rows, chan_count)
    full_mask = jnp.dot(
        packed[..., chan_count:].reshape((row_count + 2) * lane_rows, group_count), spread,
        preferred_element_type=jnp.float32,
    ).astype(jnp.bfloat16)

    offsets = jnp.arange(tap_count) - tap_reach
    allowed = jnp.abs(offsets)[None, :] <= band_width[:, None]
    global_taps = filter_taps * allowed[:, None, None, :].astype(jnp.bfloat16)
    first_row = lax.axis_index("lat") * row_count
    local_taps = lax.dynamic_slice_in_dim(global_taps, first_row, row_count, 0)
    padded_index = jnp.arange(lane_rows)
    output_index = jnp.arange(col_pad)
    tap_index = jnp.arange(tap_count)
    forward_table = (
        (padded_index[None, None, :] - output_index[None, :, None] == tap_index[:, None, None])
        & (output_index[None, :, None] < col_count)
    ).astype(jnp.bfloat16)
    band = (
        jnp.einsum("ibae,ejp->ibajp", local_taps, forward_table, preferred_element_type=jnp.float32)
        .astype(jnp.bfloat16)
    )

    eye = jnp.eye(group_count, dtype=mixing.dtype)
    mix_blocks = jnp.einsum("gbco,gh->bgcho", mixing, eye).reshape(basis_count, chan_count, chan_count)
    mix_blocks_t = jnp.einsum("gbco,gh->bhogc", mixing, eye).reshape(
        basis_count, chan_count, chan_count
    )
    upstream = jnp.pad(cotangent, ((0, 0), (0, col_pad - col_count), (0, 0)))

    vmem = pl.BlockSpec(memory_space=pltpu.VMEM)
    params = pltpu.CompilerParams(vmem_limit_bytes=48 * 1024 * 1024)
    infilled, grad_blocks, pulled = pl.pallas_call(
        forward_kernel,
        out_shape=(
            jax.ShapeDtypeStruct((row_count, col_count, chan_count), jnp.bfloat16),
            jax.ShapeDtypeStruct((basis_count, group_width, chan_count), jnp.float32),
            jax.ShapeDtypeStruct((row_count, basis_count * col_pad, chan_count), jnp.bfloat16),
        ),
        in_specs=[vmem] * 6,
        out_specs=[vmem] * 3,
        scratch_shapes=[pltpu.VMEM((basis_count, chan_count, chan_count), jnp.float32)],
        compiler_params=params,
        cost_estimate=pl.CostEstimate(
            flops=2 * row_count * basis_count * col_pad * chan_count * (6 * lane_rows + 3 * chan_count),
            transcendentals=0,
            bytes_accessed=8 * (row_count + 2) * lane_rows * chan_count,
        ),
    )(full_input, full_mask, band, upstream, mix_blocks, mix_blocks_t)

    cell_count = row_count * lax.axis_size("lat") * col_count * lax.axis_size("lon")
    lat_count = lax.axis_size("lat")
    if lat_count % 2 == 0:
        first = lax.ppermute(grad_blocks, "lat", [(i, i ^ 1) for i in range(lat_count)])
        dense = butterfly_sum(grad_blocks + first, ("lat", "lon"), skip=1)
    else:
        first = grad_blocks
        dense = butterfly_sum(grad_blocks, ("lat", "lon"))
    dense = dense * (1.0 / math.sqrt(cell_count))
    weight_grad = dense.reshape(basis_count, group_width, group_count, group_width).transpose(2, 0, 1, 3)

    collected = pl.pallas_call(
        adjoint_kernel,
        out_shape=jax.ShapeDtypeStruct(((row_count + 2) * lane_rows, chan_count), jnp.float32),
        in_specs=[vmem, vmem, pl.BlockSpec(memory_space=pl.ANY)],
        out_specs=vmem,
        compiler_params=params,
        cost_estimate=pl.CostEstimate(
            flops=6 * row_count * basis_count * col_pad * lane_rows * chan_count,
            transcendentals=0,
            bytes_accessed=6 * (row_count + 2) * lane_rows * chan_count,
        ),
    )(band, pulled, first)

    collected = collected.reshape(row_count + 2, lane_rows, chan_count)[:, :padded_cols]
    from_below = passed_along(collected[0:1], "lat", -1)
    from_above = passed_along(collected[row_count + 1 : row_count + 2], "lat", 1)
    inner_rows = (
        collected[1 : row_count + 1]
        + jnp.pad(from_above, ((0, row_count - 1), (0, 0), (0, 0)))
        + jnp.pad(from_below, ((row_count - 1, 0), (0, 0), (0, 0)))
    )
    left_rim = inner_rows[:, :tap_reach]
    right_rim = inner_rows[:, col_count + tap_reach :]
    from_right = from_behind(left_rim.astype(jnp.bfloat16), "lon", -1).astype(left_rim.dtype)
    from_left = from_behind(right_rim, "lon", 1)
    gathered = (
        inner_rows[:, tap_reach : tap_reach + col_count]
        + jnp.pad(from_right, ((0, 0), (col_count - tap_reach, 0), (0, 0)))
        + jnp.pad(from_left, ((0, 0), (0, col_count - tap_reach), (0, 0)))
    )
    input_grad = (gathered * own_mask).astype(jnp.bfloat16)
    return (infilled, input_grad, weight_grad)


def solution(mesh):
    placed = (P("lat", "lon", None), P("lat", "lon", None), P(), P(), P(), P("lat", "lon", None))
    return jax.shard_map(
        local,
        mesh=mesh,
        in_specs=placed,
        out_specs=(P("lat", "lon", None), P("lat", "lon", None), P()),
        check_vma=False,
    )
```

```python
import math

import jax
import jax.numpy as jnp
from jax import lax
from jax.experimental import pallas as pl
from jax.experimental.pallas import tpu as pltpu
from jax.sharding import PartitionSpec as P


def with_halo(block, sides, width, periodic):
    for axis, dim in sides:
        count = lax.axis_size(axis)
        forward = [(i, i + 1) for i in range(count - 1)]
        if periodic:
            forward.append((count - 1, 0))
        backward = [(target, source) for source, target in forward]
        low = lax.ppermute(
            lax.slice_in_dim(block, block.shape[dim] - width, None, axis=dim), axis, forward
        )
        high = lax.ppermute(lax.slice_in_dim(block, 0, width, axis=dim), axis, backward)
        block = jnp.concatenate([low, block, high], axis=dim)
    return block


def passed_along(block, axis, distance):
    devices = range(lax.axis_size(axis))
    route = [(i - distance, i) for i in devices if i - distance in devices]
    return lax.ppermute(block, axis, route)


def from_behind(x, axis, by):
    size = lax.axis_size(axis)
    return lax.ppermute(x, axis, [(i, (i + by) % size) for i in range(size)])


def butterfly_sum(value, axes, skip=0):
    for axis in axes:
        count = lax.axis_size(axis)
        if count & (count - 1):
            value = lax.psum(value, axis)
            continue
        step = 1
        while step < count:
            if skip:
                skip -= 1
                step *= 2
                continue
            partner = lax.ppermute(value, axis, [(i, i ^ step) for i in range(count)])
            value = value + partner
            step *= 2
    return value


def forward_kernel(x_ref, m_ref, t_ref, cot_ref, w_ref, inf_ref, wg_ref, pulled_ref, acc_ref):
    rows, basis_count, lat_taps, col_pad, lane_rows = t_ref.shape
    col_count = inf_ref.shape[1]
    chan_count = w_ref.shape[1]
    group_width = wg_ref.shape[1]
    acc_ref[...] = jnp.zeros_like(acc_ref)

    def body(i, carry):
        numerator = None
        denominator = None
        for a in range(lat_taps):
            band = t_ref[i, :, a].reshape(basis_count * col_pad, lane_rows)
            start = pl.multiple_of((i + a) * lane_rows, lane_rows)
            num = jnp.dot(band, x_ref[pl.ds(start, lane_rows), :], preferred_element_type=jnp.float32)
            den = jnp.dot(band, m_ref[pl.ds(start, lane_rows), :], preferred_element_type=jnp.float32)
            numerator = num if numerator is None else numerator + num
            denominator = den if denominator is None else denominator + den
        safe = jnp.maximum(denominator, 1.0)
        scaled = (numerator / safe).astype(jnp.bfloat16)
        upstream = cot_ref[i]
        out = jnp.zeros((col_pad, chan_count), jnp.float32)
        for b in range(basis_count):
            part = scaled[b * col_pad : (b + 1) * col_pad]
            out = out + jnp.dot(part, w_ref[b], preferred_element_type=jnp.float32)
            acc_ref[b] += lax.dot_general(
                part, upstream, (((0,), (0,)), ((), ())), preferred_element_type=jnp.float32
            )
            back = lax.dot_general(
                upstream, w_ref[b], (((1,), (1,)), ((), ())), preferred_element_type=jnp.float32
            )
            pulled_ref[i, b * col_pad : (b + 1) * col_pad, :] = (
                back / safe[b * col_pad : (b + 1) * col_pad]
            ).astype(jnp.bfloat16)
        inf_ref[i] = out[:col_count].astype(inf_ref.dtype)
        return carry

    lax.fori_loop(0, rows, body, 0)
    lane = lax.broadcasted_iota(jnp.int32, (group_width, chan_count), 1) // group_width
    for b in range(basis_count):
        total = jnp.zeros((group_width, chan_count), jnp.float32)
        for g in range(chan_count // group_width):
            block = acc_ref[b, g * group_width : (g + 1) * group_width, :]
            total = total + jnp.where(lane == g, block, 0.0)
        wg_ref[b] = total


def adjoint_kernel(t_ref, pulled_ref, order_ref, col_ref):
    rows, basis_count, lat_taps, col_pad, lane_rows = t_ref.shape
    col_ref[...] = jnp.zeros_like(col_ref)

    def body(i, carry):
        pulled = pulled_ref[i]
        for a in range(lat_taps):
            band = t_ref[i, :, a].reshape(basis_count * col_pad, lane_rows)
            start = pl.multiple_of((i + a) * lane_rows, lane_rows)
            term = lax.dot_general(
                band, pulled, (((0,), (0,)), ((), ())), preferred_element_type=jnp.float32
            )
            col_ref[pl.ds(start, lane_rows), :] += term
        return carry

    lax.fori_loop(0, rows, body, 0)


def local(features, obs_mask, filter_taps, band_width, mixing, cotangent):
    row_count, col_count, chan_count = features.shape
    group_count = obs_mask.shape[2]
    group_width = chan_count // group_count
    basis_count = mixing.shape[1]
    tap_count = filter_taps.shape[3]
    tap_reach = (tap_count - 1) // 2
    padded_cols = col_count + 2 * tap_reach
    lane_rows = -(-padded_cols // 16) * 16
    col_pad = -(-col_count // 16) * 16
    mask_values = obs_mask.astype(jnp.bfloat16)
    spread = (
        jnp.arange(chan_count)[None, :] // group_width == jnp.arange(group_count)[:, None]
    ).astype(jnp.bfloat16)
    own_mask = jnp.dot(
        mask_values.reshape(row_count * col_count, group_count), spread,
        preferred_element_type=jnp.float32,
    ).astype(jnp.bfloat16).reshape(row_count, col_count, chan_count)
    masked = features * own_mask
    packed = jnp.concatenate([masked, mask_values], axis=-1)
    packed = with_halo(packed, (("lat", 0),), 1, False)
    packed = with_halo(packed, (("lon", 1),), tap_reach, True)
    packed = jnp.pad(packed, ((0, 0), (0, lane_rows - padded_cols), (0, 0)))
    full_input = packed[..., :chan_count].reshape((row_count + 2) * lane_rows, chan_count)
    full_mask = jnp.dot(
        packed[..., chan_count:].reshape((row_count + 2) * lane_rows, group_count), spread,
        preferred_element_type=jnp.float32,
    ).astype(jnp.bfloat16)

    offsets = jnp.arange(tap_count) - tap_reach
    allowed = jnp.abs(offsets)[None, :] <= band_width[:, None]
    global_taps = filter_taps * allowed[:, None, None, :].astype(jnp.bfloat16)
    first_row = lax.axis_index("lat") * row_count
    local_taps = lax.dynamic_slice_in_dim(global_taps, first_row, row_count, 0)
    padded_index = jnp.arange(lane_rows)
    output_index = jnp.arange(col_pad)
    tap_index = jnp.arange(tap_count)
    forward_table = (
        (padded_index[None, None, :] - output_index[None, :, None] == tap_index[:, None, None])
        & (output_index[None, :, None] < col_count)
    ).astype(jnp.bfloat16)
    band = (
        jnp.einsum("ibae,ejp->ibajp", local_taps, forward_table, preferred_element_type=jnp.float32)
        .astype(jnp.bfloat16)
    )

    eye = jnp.eye(group_count, dtype=mixing.dtype)
    mix_blocks = jnp.einsum("gbco,gh->bgcho", mixing, eye).reshape(basis_count, chan_count, chan_count)
    upstream = jnp.pad(cotangent, ((0, 0), (0, col_pad - col_count), (0, 0)))

    vmem = pl.BlockSpec(memory_space=pltpu.VMEM)
    params = pltpu.CompilerParams(vmem_limit_bytes=48 * 1024 * 1024)
    infilled, grad_blocks, pulled = pl.pallas_call(
        forward_kernel,
        out_shape=(
            jax.ShapeDtypeStruct((row_count, col_count, chan_count), jnp.bfloat16),
            jax.ShapeDtypeStruct((basis_count, group_width, chan_count), jnp.float32),
            jax.ShapeDtypeStruct((row_count, basis_count * col_pad, chan_count), jnp.bfloat16),
        ),
        in_specs=[vmem] * 5,
        out_specs=[vmem] * 3,
        scratch_shapes=[pltpu.VMEM((basis_count, chan_count, chan_count), jnp.float32)],
        compiler_params=params,
        cost_estimate=pl.CostEstimate(
            flops=2 * row_count * basis_count * col_pad * chan_count * (6 * lane_rows + 3 * chan_count),
            transcendentals=0,
            bytes_accessed=8 * (row_count + 2) * lane_rows * chan_count,
        ),
    )(full_input, full_mask, band, upstream, mix_blocks)

    cell_count = row_count * lax.axis_size("lat") * col_count * lax.axis_size("lon")
    lat_count = lax.axis_size("lat")
    if lat_count % 2 == 0:
        first = lax.ppermute(grad_blocks, "lat", [(i, i ^ 1) for i in range(lat_count)])
        dense = butterfly_sum(grad_blocks + first, ("lat", "lon"), skip=1)
    else:
        first = grad_blocks
        dense = butterfly_sum(grad_blocks, ("lat", "lon"))
    dense = dense * (1.0 / math.sqrt(cell_count))
    weight_grad = dense.reshape(basis_count, group_width, group_count, group_width).transpose(2, 0, 1, 3)

    collected = pl.pallas_call(
        adjoint_kernel,
        out_shape=jax.ShapeDtypeStruct(((row_count + 2) * lane_rows, chan_count), jnp.float32),
        in_specs=[vmem, vmem, pl.BlockSpec(memory_space=pl.ANY)],
        out_specs=vmem,
        compiler_params=params,
        cost_estimate=pl.CostEstimate(
            flops=6 * row_count * basis_count * col_pad * lane_rows * chan_count,
            transcendentals=0,
            bytes_accessed=6 * (row_count + 2) * lane_rows * chan_count,
        ),
    )(band, pulled, first)

    collected = collected.reshape(row_count + 2, lane_rows, chan_count)[:, :padded_cols]
    from_below = passed_along(collected[0:1], "lat", -1)
    from_above = passed_along(collected[row_count + 1 : row_count + 2], "lat", 1)
    inner_rows = (
        collected[1 : row_count + 1]
        + jnp.pad(from_above, ((0, row_count - 1), (0, 0), (0, 0)))
        + jnp.pad(from_below, ((row_count - 1, 0), (0, 0), (0, 0)))
    )
    left_rim = inner_rows[:, :tap_reach]
    right_rim = inner_rows[:, col_count + tap_reach :]
    from_right = from_behind(left_rim.astype(jnp.bfloat16), "lon", -1).astype(left_rim.dtype)
    from_left = from_behind(right_rim, "lon", 1)
    gathered = (
        inner_rows[:, tap_reach : tap_reach + col_count]
        + jnp.pad(from_right, ((0, 0), (col_count - tap_reach, 0), (0, 0)))
        + jnp.pad(from_left, ((0, 0), (0, col_count - tap_reach), (0, 0)))
    )
    input_grad = (gathered * own_mask).astype(jnp.bfloat16)
    return (infilled, input_grad, weight_grad)


def solution(mesh):
    placed = (P("lat", "lon", None), P("lat", "lon", None), P(), P(), P(), P("lat", "lon", None))
    return jax.shard_map(
        local,
        mesh=mesh,
        in_specs=placed,
        out_specs=(P("lat", "lon", None), P("lat", "lon", None), P()),
        check_vma=False,
    )
```

```python
import math

import jax
import jax.numpy as jnp
from jax import lax
from jax.experimental import pallas as pl
from jax.experimental.pallas import tpu as pltpu
from jax.sharding import PartitionSpec as P


def with_halo(block, sides, width, periodic):
    for axis, dim in sides:
        count = lax.axis_size(axis)
        forward = [(i, i + 1) for i in range(count - 1)]
        if periodic:
            forward.append((count - 1, 0))
        backward = [(target, source) for source, target in forward]
        low = lax.ppermute(
            lax.slice_in_dim(block, block.shape[dim] - width, None, axis=dim), axis, forward
        )
        high = lax.ppermute(lax.slice_in_dim(block, 0, width, axis=dim), axis, backward)
        block = jnp.concatenate([low, block, high], axis=dim)
    return block


def passed_along(block, axis, distance):
    devices = range(lax.axis_size(axis))
    route = [(i - distance, i) for i in devices if i - distance in devices]
    return lax.ppermute(block, axis, route)


def from_behind(x, axis, by):
    size = lax.axis_size(axis)
    return lax.ppermute(x, axis, [(i, (i + by) % size) for i in range(size)])


def butterfly_sum(value, axes, skip=0):
    for axis in axes:
        count = lax.axis_size(axis)
        if count & (count - 1):
            value = lax.psum(value, axis)
            continue
        step = 1
        while step < count:
            if skip:
                skip -= 1
                step *= 2
                continue
            partner = lax.ppermute(value, axis, [(i, i ^ step) for i in range(count)])
            value = value + partner
            step *= 2
    return value


def forward_kernel(x_ref, m_ref, t_ref, cot_ref, w_ref, inf_ref, wg_ref, pulled_ref, scaled_ref):
    rows, basis_count, lat_taps, col_pad, lane_rows = t_ref.shape
    col_count = inf_ref.shape[1]
    chan_count = w_ref.shape[1]
    group_width = wg_ref.shape[1]

    def body(i, carry):
        numerator = None
        denominator = None
        for a in range(lat_taps):
            band = t_ref[i, :, a].reshape(basis_count * col_pad, lane_rows)
            start = pl.multiple_of((i + a) * lane_rows, lane_rows)
            num = jnp.dot(band, x_ref[pl.ds(start, lane_rows), :], preferred_element_type=jnp.float32)
            den = jnp.dot(band, m_ref[pl.ds(start, lane_rows), :], preferred_element_type=jnp.float32)
            numerator = num if numerator is None else numerator + num
            denominator = den if denominator is None else denominator + den
        safe = jnp.maximum(denominator, 1.0)
        scaled = (numerator / safe).astype(jnp.bfloat16)
        upstream = cot_ref[i]
        out = jnp.zeros((col_pad, chan_count), jnp.float32)
        for b in range(basis_count):
            part = scaled[b * col_pad : (b + 1) * col_pad]
            out = out + jnp.dot(part, w_ref[b], preferred_element_type=jnp.float32)
            scaled_ref[b, pl.ds(pl.multiple_of(i * col_pad, col_pad), col_pad), :] = part
            back = lax.dot_general(
                upstream, w_ref[b], (((1,), (1,)), ((), ())), preferred_element_type=jnp.float32
            )
            pulled_ref[i, b * col_pad : (b + 1) * col_pad, :] = (
                back / safe[b * col_pad : (b + 1) * col_pad]
            ).astype(jnp.bfloat16)
        inf_ref[i] = out[:col_count].astype(inf_ref.dtype)
        return carry

    lax.fori_loop(0, rows, body, 0)
    lane = lax.broadcasted_iota(jnp.int32, (group_width, chan_count), 1) // group_width
    upstream_all = cot_ref[...].reshape(rows * col_pad, chan_count)
    for b in range(basis_count):
        grad = lax.dot_general(
            scaled_ref[b], upstream_all, (((0,), (0,)), ((), ())), preferred_element_type=jnp.float32
        )
        total = jnp.zeros((group_width, chan_count), jnp.float32)
        for g in range(chan_count // group_width):
            block = grad[g * group_width : (g + 1) * group_width, :]
            total = total + jnp.where(lane == g, block, 0.0)
        wg_ref[b] = total


def adjoint_kernel(t_ref, pulled_ref, order_ref, col_ref):
    rows, basis_count, lat_taps, col_pad, lane_rows = t_ref.shape
    col_ref[...] = jnp.zeros_like(col_ref)

    def body(i, carry):
        pulled = pulled_ref[i]
        for a in range(lat_taps):
            band = t_ref[i, :, a].reshape(basis_count * col_pad, lane_rows)
            start = pl.multiple_of((i + a) * lane_rows, lane_rows)
            term = lax.dot_general(
                band, pulled, (((0,), (0,)), ((), ())), preferred_element_type=jnp.float32
            )
            col_ref[pl.ds(start, lane_rows), :] += term
        return carry

    lax.fori_loop(0, rows, body, 0)


def local(features, obs_mask, filter_taps, band_width, mixing, cotangent):
    row_count, col_count, chan_count = features.shape
    group_count = obs_mask.shape[2]
    group_width = chan_count // group_count
    basis_count = mixing.shape[1]
    tap_count = filter_taps.shape[3]
    tap_reach = (tap_count - 1) // 2
    padded_cols = col_count + 2 * tap_reach
    lane_rows = -(-padded_cols // 16) * 16
    col_pad = -(-col_count // 16) * 16
    mask_values = obs_mask.astype(jnp.bfloat16)
    spread = (
        jnp.arange(chan_count)[None, :] // group_width == jnp.arange(group_count)[:, None]
    ).astype(jnp.bfloat16)
    own_mask = jnp.dot(
        mask_values.reshape(row_count * col_count, group_count), spread,
        preferred_element_type=jnp.float32,
    ).astype(jnp.bfloat16).reshape(row_count, col_count, chan_count)
    masked = features * own_mask
    packed = jnp.concatenate([masked, mask_values], axis=-1)
    packed = with_halo(packed, (("lat", 0),), 1, False)
    packed = with_halo(packed, (("lon", 1),), tap_reach, True)
    packed = jnp.pad(packed, ((0, 0), (0, lane_rows - padded_cols), (0, 0)))
    full_input = packed[..., :chan_count].reshape((row_count + 2) * lane_rows, chan_count)
    full_mask = jnp.dot(
        packed[..., chan_count:].reshape((row_count + 2) * lane_rows, group_count), spread,
        preferred_element_type=jnp.float32,
    ).astype(jnp.bfloat16)

    offsets = jnp.arange(tap_count) - tap_reach
    allowed = jnp.abs(offsets)[None, :] <= band_width[:, None]
    global_taps = filter_taps * allowed[:, None, None, :].astype(jnp.bfloat16)
    first_row = lax.axis_index("lat") * row_count
    local_taps = lax.dynamic_slice_in_dim(global_taps, first_row, row_count, 0)
    padded_index = jnp.arange(lane_rows)
    output_index = jnp.arange(col_pad)
    tap_index = jnp.arange(tap_count)
    forward_table = (
        (padded_index[None, None, :] - output_index[None, :, None] == tap_index[:, None, None])
        & (output_index[None, :, None] < col_count)
    ).astype(jnp.bfloat16)
    band = (
        jnp.einsum("ibae,ejp->ibajp", local_taps, forward_table, preferred_element_type=jnp.float32)
        .astype(jnp.bfloat16)
    )

    eye = jnp.eye(group_count, dtype=mixing.dtype)
    mix_blocks = jnp.einsum("gbco,gh->bgcho", mixing, eye).reshape(basis_count, chan_count, chan_count)
    upstream = jnp.pad(cotangent, ((0, 0), (0, col_pad - col_count), (0, 0)))

    vmem = pl.BlockSpec(memory_space=pltpu.VMEM)
    params = pltpu.CompilerParams(vmem_limit_bytes=48 * 1024 * 1024)
    infilled, grad_blocks, pulled = pl.pallas_call(
        forward_kernel,
        out_shape=(
            jax.ShapeDtypeStruct((row_count, col_count, chan_count), jnp.bfloat16),
            jax.ShapeDtypeStruct((basis_count, group_width, chan_count), jnp.float32),
            jax.ShapeDtypeStruct((row_count, basis_count * col_pad, chan_count), jnp.bfloat16),
        ),
        in_specs=[vmem] * 5,
        out_specs=[vmem] * 3,
        scratch_shapes=[pltpu.VMEM((basis_count, row_count * col_pad, chan_count), jnp.bfloat16)],
        compiler_params=params,
        cost_estimate=pl.CostEstimate(
            flops=2 * row_count * basis_count * col_pad * chan_count * (6 * lane_rows + 3 * chan_count),
            transcendentals=0,
            bytes_accessed=8 * (row_count + 2) * lane_rows * chan_count,
        ),
    )(full_input, full_mask, band, upstream, mix_blocks)

    cell_count = row_count * lax.axis_size("lat") * col_count * lax.axis_size("lon")
    lat_count = lax.axis_size("lat")
    if lat_count % 2 == 0:
        first = lax.ppermute(grad_blocks, "lat", [(i, i ^ 1) for i in range(lat_count)])
        dense = butterfly_sum(grad_blocks + first, ("lat", "lon"), skip=1)
    else:
        first = grad_blocks
        dense = butterfly_sum(grad_blocks, ("lat", "lon"))
    dense = dense * (1.0 / math.sqrt(cell_count))
    weight_grad = dense.reshape(basis_count, group_width, group_count, group_width).transpose(2, 0, 1, 3)

    collected = pl.pallas_call(
        adjoint_kernel,
        out_shape=jax.ShapeDtypeStruct(((row_count + 2) * lane_rows, chan_count), jnp.float32),
        in_specs=[vmem, vmem, pl.BlockSpec(memory_space=pl.ANY)],
        out_specs=vmem,
        compiler_params=params,
        cost_estimate=pl.CostEstimate(
            flops=6 * row_count * basis_count * col_pad * lane_rows * chan_count,
            transcendentals=0,
            bytes_accessed=6 * (row_count + 2) * lane_rows * chan_count,
        ),
    )(band, pulled, first)

    collected = collected.reshape(row_count + 2, lane_rows, chan_count)[:, :padded_cols]
    from_below = passed_along(collected[0:1], "lat", -1)
    from_above = passed_along(collected[row_count + 1 : row_count + 2], "lat", 1)
    inner_rows = (
        collected[1 : row_count + 1]
        + jnp.pad(from_above, ((0, row_count - 1), (0, 0), (0, 0)))
        + jnp.pad(from_below, ((row_count - 1, 0), (0, 0), (0, 0)))
    )
    left_rim = inner_rows[:, :tap_reach]
    right_rim = inner_rows[:, col_count + tap_reach :]
    from_right = from_behind(left_rim.astype(jnp.bfloat16), "lon", -1).astype(left_rim.dtype)
    from_left = from_behind(right_rim, "lon", 1)
    gathered = (
        inner_rows[:, tap_reach : tap_reach + col_count]
        + jnp.pad(from_right, ((0, 0), (col_count - tap_reach, 0), (0, 0)))
        + jnp.pad(from_left, ((0, 0), (0, col_count - tap_reach), (0, 0)))
    )
    input_grad = (gathered * own_mask).astype(jnp.bfloat16)
    return (infilled, input_grad, weight_grad)


def solution(mesh):
    placed = (P("lat", "lon", None), P("lat", "lon", None), P(), P(), P(), P("lat", "lon", None))
    return jax.shard_map(
        local,
        mesh=mesh,
        in_specs=placed,
        out_specs=(P("lat", "lon", None), P("lat", "lon", None), P()),
        check_vma=False,
    )
```

```python
import math

import jax
import jax.numpy as jnp
from jax import lax
from jax.experimental import pallas as pl
from jax.experimental.pallas import tpu as pltpu
from jax.sharding import PartitionSpec as P


def with_halo(block, sides, width, periodic):
    for axis, dim in sides:
        count = lax.axis_size(axis)
        forward = [(i, i + 1) for i in range(count - 1)]
        if periodic:
            forward.append((count - 1, 0))
        backward = [(target, source) for source, target in forward]
        low = lax.ppermute(
            lax.slice_in_dim(block, block.shape[dim] - width, None, axis=dim), axis, forward
        )
        high = lax.ppermute(lax.slice_in_dim(block, 0, width, axis=dim), axis, backward)
        block = jnp.concatenate([low, block, high], axis=dim)
    return block


def passed_along(block, axis, distance):
    devices = range(lax.axis_size(axis))
    route = [(i - distance, i) for i in devices if i - distance in devices]
    return lax.ppermute(block, axis, route)


def from_behind(x, axis, by):
    size = lax.axis_size(axis)
    return lax.ppermute(x, axis, [(i, (i + by) % size) for i in range(size)])


def butterfly_sum(value, axes, skip=0):
    for axis in axes:
        count = lax.axis_size(axis)
        if count & (count - 1):
            value = lax.psum(value, axis)
            continue
        step = 1
        while step < count:
            if skip:
                skip -= 1
                step *= 2
                continue
            partner = lax.ppermute(value, axis, [(i, i ^ step) for i in range(count)])
            value = value + partner
            step *= 2
    return value


def forward_kernel(x_ref, m_ref, t_ref, cot_ref, w_ref, inf_ref, wg_ref, pulled_ref, scaled_ref, safe_ref):
    rows, basis_count, lat_taps, col_pad, lane_rows = t_ref.shape
    col_count = inf_ref.shape[1]
    chan_count = w_ref.shape[1]
    group_width = wg_ref.shape[1]

    def body(i, carry):
        numerator = None
        denominator = None
        for a in range(lat_taps):
            band = t_ref[i, :, a].reshape(basis_count * col_pad, lane_rows)
            start = pl.multiple_of((i + a) * lane_rows, lane_rows)
            num = jnp.dot(band, x_ref[pl.ds(start, lane_rows), :], preferred_element_type=jnp.float32)
            den = jnp.dot(band, m_ref[pl.ds(start, lane_rows), :], preferred_element_type=jnp.float32)
            numerator = num if numerator is None else numerator + num
            denominator = den if denominator is None else denominator + den
        safe = jnp.maximum(denominator, 1.0)
        scaled = (numerator / safe).astype(jnp.bfloat16)
        rows_at = pl.ds(pl.multiple_of(i * col_pad, col_pad), col_pad)
        for b in range(basis_count):
            scaled_ref[b, rows_at, :] = scaled[b * col_pad : (b + 1) * col_pad]
            safe_ref[b, rows_at, :] = safe[b * col_pad : (b + 1) * col_pad]
        return carry

    lax.fori_loop(0, rows, body, 0)
    lane = lax.broadcasted_iota(jnp.int32, (group_width, chan_count), 1) // group_width
    upstream_all = cot_ref[...].reshape(rows * col_pad, chan_count)
    out = None
    for b in range(basis_count):
        part = scaled_ref[b]
        mixed = jnp.dot(part, w_ref[b], preferred_element_type=jnp.float32)
        out = mixed if out is None else out + mixed
        grad = lax.dot_general(
            part, upstream_all, (((0,), (0,)), ((), ())), preferred_element_type=jnp.float32
        )
        total = jnp.zeros((group_width, chan_count), jnp.float32)
        for g in range(chan_count // group_width):
            block = grad[g * group_width : (g + 1) * group_width, :]
            total = total + jnp.where(lane == g, block, 0.0)
        wg_ref[b] = total
        back = lax.dot_general(
            upstream_all, w_ref[b], (((1,), (1,)), ((), ())), preferred_element_type=jnp.float32
        )
        pulled_ref[b] = (back / safe_ref[b]).astype(jnp.bfloat16)
    for i in range(rows):
        inf_ref[i] = out[i * col_pad : i * col_pad + col_count].astype(inf_ref.dtype)


def adjoint_kernel(t_ref, pulled_ref, order_ref, col_ref):
    rows, basis_count, lat_taps, col_pad, lane_rows = t_ref.shape
    col_ref[...] = jnp.zeros_like(col_ref)

    def body(i, carry):
        rows_at = pl.ds(pl.multiple_of(i * col_pad, col_pad), col_pad)
        pulled = jnp.concatenate([pulled_ref[b, rows_at, :] for b in range(basis_count)], axis=0)
        for a in range(lat_taps):
            band = t_ref[i, :, a].reshape(basis_count * col_pad, lane_rows)
            start = pl.multiple_of((i + a) * lane_rows, lane_rows)
            term = lax.dot_general(
                band, pulled, (((0,), (0,)), ((), ())), preferred_element_type=jnp.float32
            )
            col_ref[pl.ds(start, lane_rows), :] += term
        return carry

    lax.fori_loop(0, rows, body, 0)


def local(features, obs_mask, filter_taps, band_width, mixing, cotangent):
    row_count, col_count, chan_count = features.shape
    group_count = obs_mask.shape[2]
    group_width = chan_count // group_count
    basis_count = mixing.shape[1]
    tap_count = filter_taps.shape[3]
    tap_reach = (tap_count - 1) // 2
    padded_cols = col_count + 2 * tap_reach
    lane_rows = -(-padded_cols // 16) * 16
    col_pad = -(-col_count // 16) * 16
    mask_values = obs_mask.astype(jnp.bfloat16)
    spread = (
        jnp.arange(chan_count)[None, :] // group_width == jnp.arange(group_count)[:, None]
    ).astype(jnp.bfloat16)
    own_mask = jnp.dot(
        mask_values.reshape(row_count * col_count, group_count), spread,
        preferred_element_type=jnp.float32,
    ).astype(jnp.bfloat16).reshape(row_count, col_count, chan_count)
    masked = features * own_mask
    packed = jnp.concatenate([masked, mask_values], axis=-1)
    packed = with_halo(packed, (("lat", 0),), 1, False)
    packed = with_halo(packed, (("lon", 1),), tap_reach, True)
    packed = jnp.pad(packed, ((0, 0), (0, lane_rows - padded_cols), (0, 0)))
    full_input = packed[..., :chan_count].reshape((row_count + 2) * lane_rows, chan_count)
    full_mask = jnp.dot(
        packed[..., chan_count:].reshape((row_count + 2) * lane_rows, group_count), spread,
        preferred_element_type=jnp.float32,
    ).astype(jnp.bfloat16)

    offsets = jnp.arange(tap_count) - tap_reach
    allowed = jnp.abs(offsets)[None, :] <= band_width[:, None]
    global_taps = filter_taps * allowed[:, None, None, :].astype(jnp.bfloat16)
    first_row = lax.axis_index("lat") * row_count
    local_taps = lax.dynamic_slice_in_dim(global_taps, first_row, row_count, 0)
    padded_index = jnp.arange(lane_rows)
    output_index = jnp.arange(col_pad)
    tap_index = jnp.arange(tap_count)
    forward_table = (
        (padded_index[None, None, :] - output_index[None, :, None] == tap_index[:, None, None])
        & (output_index[None, :, None] < col_count)
    ).astype(jnp.bfloat16)
    band = (
        jnp.einsum("ibae,ejp->ibajp", local_taps, forward_table, preferred_element_type=jnp.float32)
        .astype(jnp.bfloat16)
    )

    eye = jnp.eye(group_count, dtype=mixing.dtype)
    mix_blocks = jnp.einsum("gbco,gh->bgcho", mixing, eye).reshape(basis_count, chan_count, chan_count)
    upstream = jnp.pad(cotangent, ((0, 0), (0, col_pad - col_count), (0, 0)))

    vmem = pl.BlockSpec(memory_space=pltpu.VMEM)
    params = pltpu.CompilerParams(vmem_limit_bytes=48 * 1024 * 1024)
    infilled, grad_blocks, pulled = pl.pallas_call(
        forward_kernel,
        out_shape=(
            jax.ShapeDtypeStruct((row_count, col_count, chan_count), jnp.bfloat16),
            jax.ShapeDtypeStruct((basis_count, group_width, chan_count), jnp.float32),
            jax.ShapeDtypeStruct((basis_count, row_count * col_pad, chan_count), jnp.bfloat16),
        ),
        in_specs=[vmem] * 5,
        out_specs=[vmem] * 3,
        scratch_shapes=[
            pltpu.VMEM((basis_count, row_count * col_pad, chan_count), jnp.bfloat16),
            pltpu.VMEM((basis_count, row_count * col_pad, chan_count), jnp.float32),
        ],
        compiler_params=params,
        cost_estimate=pl.CostEstimate(
            flops=2 * row_count * basis_count * col_pad * chan_count * (6 * lane_rows + 3 * chan_count),
            transcendentals=0,
            bytes_accessed=8 * (row_count + 2) * lane_rows * chan_count,
        ),
    )(full_input, full_mask, band, upstream, mix_blocks)

    cell_count = row_count * lax.axis_size("lat") * col_count * lax.axis_size("lon")
    lat_count = lax.axis_size("lat")
    if lat_count % 2 == 0:
        first = lax.ppermute(grad_blocks, "lat", [(i, i ^ 1) for i in range(lat_count)])
        dense = butterfly_sum(grad_blocks + first, ("lat", "lon"), skip=1)
    else:
        first = grad_blocks
        dense = butterfly_sum(grad_blocks, ("lat", "lon"))
    dense = dense * (1.0 / math.sqrt(cell_count))
    weight_grad = dense.reshape(basis_count, group_width, group_count, group_width).transpose(2, 0, 1, 3)

    collected = pl.pallas_call(
        adjoint_kernel,
        out_shape=jax.ShapeDtypeStruct(((row_count + 2) * lane_rows, chan_count), jnp.float32),
        in_specs=[vmem, vmem, pl.BlockSpec(memory_space=pl.ANY)],
        out_specs=vmem,
        compiler_params=params,
        cost_estimate=pl.CostEstimate(
            flops=6 * row_count * basis_count * col_pad * lane_rows * chan_count,
            transcendentals=0,
            bytes_accessed=6 * (row_count + 2) * lane_rows * chan_count,
        ),
    )(band, pulled, first)

    collected = collected.reshape(row_count + 2, lane_rows, chan_count)[:, :padded_cols]
    from_below = passed_along(collected[0:1], "lat", -1)
    from_above = passed_along(collected[row_count + 1 : row_count + 2], "lat", 1)
    inner_rows = (
        collected[1 : row_count + 1]
        + jnp.pad(from_above, ((0, row_count - 1), (0, 0), (0, 0)))
        + jnp.pad(from_below, ((row_count - 1, 0), (0, 0), (0, 0)))
    )
    left_rim = inner_rows[:, :tap_reach]
    right_rim = inner_rows[:, col_count + tap_reach :]
    from_right = from_behind(left_rim.astype(jnp.bfloat16), "lon", -1).astype(left_rim.dtype)
    from_left = from_behind(right_rim, "lon", 1)
    gathered = (
        inner_rows[:, tap_reach : tap_reach + col_count]
        + jnp.pad(from_right, ((0, 0), (col_count - tap_reach, 0), (0, 0)))
        + jnp.pad(from_left, ((0, 0), (0, col_count - tap_reach), (0, 0)))
    )
    input_grad = (gathered * own_mask).astype(jnp.bfloat16)
    return (infilled, input_grad, weight_grad)


def solution(mesh):
    placed = (P("lat", "lon", None), P("lat", "lon", None), P(), P(), P(), P("lat", "lon", None))
    return jax.shard_map(
        local,
        mesh=mesh,
        in_specs=placed,
        out_specs=(P("lat", "lon", None), P("lat", "lon", None), P()),
        check_vma=False,
    )
```

```python
import math

import jax
import jax.numpy as jnp
from jax import lax
from jax.experimental import pallas as pl
from jax.experimental.pallas import tpu as pltpu
from jax.sharding import PartitionSpec as P


def with_halo(block, sides, width, periodic):
    for axis, dim in sides:
        count = lax.axis_size(axis)
        forward = [(i, i + 1) for i in range(count - 1)]
        if periodic:
            forward.append((count - 1, 0))
        backward = [(target, source) for source, target in forward]
        low = lax.ppermute(
            lax.slice_in_dim(block, block.shape[dim] - width, None, axis=dim), axis, forward
        )
        high = lax.ppermute(lax.slice_in_dim(block, 0, width, axis=dim), axis, backward)
        block = jnp.concatenate([low, block, high], axis=dim)
    return block


def passed_along(block, axis, distance):
    devices = range(lax.axis_size(axis))
    route = [(i - distance, i) for i in devices if i - distance in devices]
    return lax.ppermute(block, axis, route)


def from_behind(x, axis, by):
    size = lax.axis_size(axis)
    return lax.ppermute(x, axis, [(i, (i + by) % size) for i in range(size)])


def ring_sum(value, axis):
    count = lax.axis_size(axis)
    me = lax.axis_index(axis)
    received = [value] + [
        lax.ppermute(value, axis, [(i, (i + shift) % count) for i in range(count)])
        for shift in range(1, count)
    ]
    total = None
    for owner in range(count):
        piece = None
        for shift in range(count):
            chosen = jnp.where((me - shift) % count == owner, received[shift], 0.0)
            piece = chosen if piece is None else piece + chosen
        total = piece if total is None else total + piece
    return total


def butterfly_sum(value, axes, skip=0):
    for axis in axes:
        count = lax.axis_size(axis)
        if count <= 4 and not skip:
            value = ring_sum(value, axis)
            continue
        if count & (count - 1):
            value = lax.psum(value, axis)
            continue
        step = 1
        while step < count:
            if skip:
                skip -= 1
                step *= 2
                continue
            partner = lax.ppermute(value, axis, [(i, i ^ step) for i in range(count)])
            value = value + partner
            step *= 2
    return value


def forward_kernel(x_ref, m_ref, t_ref, cot_ref, w_ref, inf_ref, wg_ref, pulled_ref, scaled_ref, safe_ref):
    rows, basis_count, lat_taps, col_pad, lane_rows = t_ref.shape
    col_count = inf_ref.shape[1]
    chan_count = w_ref.shape[1]
    group_width = wg_ref.shape[1]

    def body(i, carry):
        numerator = None
        denominator = None
        for a in range(lat_taps):
            band = t_ref[i, :, a].reshape(basis_count * col_pad, lane_rows)
            start = pl.multiple_of((i + a) * lane_rows, lane_rows)
            num = jnp.dot(band, x_ref[pl.ds(start, lane_rows), :], preferred_element_type=jnp.float32)
            den = jnp.dot(band, m_ref[pl.ds(start, lane_rows), :], preferred_element_type=jnp.float32)
            numerator = num if numerator is None else numerator + num
            denominator = den if denominator is None else denominator + den
        safe = jnp.maximum(denominator, 1.0)
        scaled = (numerator / safe).astype(jnp.bfloat16)
        rows_at = pl.ds(pl.multiple_of(i * col_pad, col_pad), col_pad)
        for b in range(basis_count):
            scaled_ref[b, rows_at, :] = scaled[b * col_pad : (b + 1) * col_pad]
            safe_ref[b, rows_at, :] = safe[b * col_pad : (b + 1) * col_pad]
        return carry

    lax.fori_loop(0, rows, body, 0)
    lane = lax.broadcasted_iota(jnp.int32, (group_width, chan_count), 1) // group_width
    upstream_all = cot_ref[...].reshape(rows * col_pad, chan_count)
    out = None
    for b in range(basis_count):
        part = scaled_ref[b]
        mixed = jnp.dot(part, w_ref[b], preferred_element_type=jnp.float32)
        out = mixed if out is None else out + mixed
        grad = lax.dot_general(
            part, upstream_all, (((0,), (0,)), ((), ())), preferred_element_type=jnp.float32
        )
        total = jnp.zeros((group_width, chan_count), jnp.float32)
        for g in range(chan_count // group_width):
            block = grad[g * group_width : (g + 1) * group_width, :]
            total = total + jnp.where(lane == g, block, 0.0)
        wg_ref[b] = total
        back = lax.dot_general(
            upstream_all, w_ref[b], (((1,), (1,)), ((), ())), preferred_element_type=jnp.float32
        )
        pulled_ref[b] = (back / safe_ref[b]).astype(jnp.bfloat16)
    for i in range(rows):
        inf_ref[i] = out[i * col_pad : i * col_pad + col_count].astype(inf_ref.dtype)


def adjoint_kernel(t_ref, pulled_ref, order_ref, col_ref):
    rows, basis_count, lat_taps, col_pad, lane_rows = t_ref.shape
    col_ref[...] = jnp.zeros_like(col_ref)

    def body(i, carry):
        rows_at = pl.ds(pl.multiple_of(i * col_pad, col_pad), col_pad)
        pulled = jnp.concatenate([pulled_ref[b, rows_at, :] for b in range(basis_count)], axis=0)
        for a in range(lat_taps):
            band = t_ref[i, :, a].reshape(basis_count * col_pad, lane_rows)
            start = pl.multiple_of((i + a) * lane_rows, lane_rows)
            term = lax.dot_general(
                band, pulled, (((0,), (0,)), ((), ())), preferred_element_type=jnp.float32
            )
            col_ref[pl.ds(start, lane_rows), :] += term
        return carry

    lax.fori_loop(0, rows, body, 0)


def local(features, obs_mask, filter_taps, band_width, mixing, cotangent):
    row_count, col_count, chan_count = features.shape
    group_count = obs_mask.shape[2]
    group_width = chan_count // group_count
    basis_count = mixing.shape[1]
    tap_count = filter_taps.shape[3]
    tap_reach = (tap_count - 1) // 2
    padded_cols = col_count + 2 * tap_reach
    lane_rows = -(-padded_cols // 16) * 16
    col_pad = -(-col_count // 16) * 16
    mask_values = obs_mask.astype(jnp.bfloat16)
    spread = (
        jnp.arange(chan_count)[None, :] // group_width == jnp.arange(group_count)[:, None]
    ).astype(jnp.bfloat16)
    own_mask = jnp.dot(
        mask_values.reshape(row_count * col_count, group_count), spread,
        preferred_element_type=jnp.float32,
    ).astype(jnp.bfloat16).reshape(row_count, col_count, chan_count)
    masked = features * own_mask
    packed = jnp.concatenate([masked, mask_values], axis=-1)
    packed = with_halo(packed, (("lat", 0),), 1, False)
    packed = with_halo(packed, (("lon", 1),), tap_reach, True)
    packed = jnp.pad(packed, ((0, 0), (0, lane_rows - padded_cols), (0, 0)))
    full_input = packed[..., :chan_count].reshape((row_count + 2) * lane_rows, chan_count)
    full_mask = jnp.dot(
        packed[..., chan_count:].reshape((row_count + 2) * lane_rows, group_count), spread,
        preferred_element_type=jnp.float32,
    ).astype(jnp.bfloat16)

    offsets = jnp.arange(tap_count) - tap_reach
    allowed = jnp.abs(offsets)[None, :] <= band_width[:, None]
    global_taps = filter_taps * allowed[:, None, None, :].astype(jnp.bfloat16)
    first_row = lax.axis_index("lat") * row_count
    local_taps = lax.dynamic_slice_in_dim(global_taps, first_row, row_count, 0)
    padded_index = jnp.arange(lane_rows)
    output_index = jnp.arange(col_pad)
    tap_index = jnp.arange(tap_count)
    forward_table = (
        (padded_index[None, None, :] - output_index[None, :, None] == tap_index[:, None, None])
        & (output_index[None, :, None] < col_count)
    ).astype(jnp.bfloat16)
    band = (
        jnp.einsum("ibae,ejp->ibajp", local_taps, forward_table, preferred_element_type=jnp.float32)
        .astype(jnp.bfloat16)
    )

    eye = jnp.eye(group_count, dtype=mixing.dtype)
    mix_blocks = jnp.einsum("gbco,gh->bgcho", mixing, eye).reshape(basis_count, chan_count, chan_count)
    upstream = jnp.pad(cotangent, ((0, 0), (0, col_pad - col_count), (0, 0)))

    vmem = pl.BlockSpec(memory_space=pltpu.VMEM)
    params = pltpu.CompilerParams(vmem_limit_bytes=48 * 1024 * 1024)
    infilled, grad_blocks, pulled = pl.pallas_call(
        forward_kernel,
        out_shape=(
            jax.ShapeDtypeStruct((row_count, col_count, chan_count), jnp.bfloat16),
            jax.ShapeDtypeStruct((basis_count, group_width, chan_count), jnp.float32),
            jax.ShapeDtypeStruct((basis_count, row_count * col_pad, chan_count), jnp.bfloat16),
        ),
        in_specs=[vmem] * 5,
        out_specs=[vmem] * 3,
        scratch_shapes=[
            pltpu.VMEM((basis_count, row_count * col_pad, chan_count), jnp.bfloat16),
            pltpu.VMEM((basis_count, row_count * col_pad, chan_count), jnp.float32),
        ],
        compiler_params=params,
        cost_estimate=pl.CostEstimate(
            flops=2 * row_count * basis_count * col_pad * chan_count * (6 * lane_rows + 3 * chan_count),
            transcendentals=0,
            bytes_accessed=8 * (row_count + 2) * lane_rows * chan_count,
        ),
    )(full_input, full_mask, band, upstream, mix_blocks)

    cell_count = row_count * lax.axis_size("lat") * col_count * lax.axis_size("lon")
    lat_count = lax.axis_size("lat")
    if lat_count % 2 == 0:
        first = lax.ppermute(grad_blocks, "lat", [(i, i ^ 1) for i in range(lat_count)])
        dense = butterfly_sum(grad_blocks + first, ("lat", "lon"), skip=1)
    else:
        first = grad_blocks
        dense = butterfly_sum(grad_blocks, ("lat", "lon"))
    dense = dense * (1.0 / math.sqrt(cell_count))
    weight_grad = dense.reshape(basis_count, group_width, group_count, group_width).transpose(2, 0, 1, 3)

    collected = pl.pallas_call(
        adjoint_kernel,
        out_shape=jax.ShapeDtypeStruct(((row_count + 2) * lane_rows, chan_count), jnp.float32),
        in_specs=[vmem, vmem, pl.BlockSpec(memory_space=pl.ANY)],
        out_specs=vmem,
        compiler_params=params,
        cost_estimate=pl.CostEstimate(
            flops=6 * row_count * basis_count * col_pad * lane_rows * chan_count,
            transcendentals=0,
            bytes_accessed=6 * (row_count + 2) * lane_rows * chan_count,
        ),
    )(band, pulled, first)

    collected = collected.reshape(row_count + 2, lane_rows, chan_count)[:, :padded_cols]
    from_below = passed_along(collected[0:1], "lat", -1)
    from_above = passed_along(collected[row_count + 1 : row_count + 2], "lat", 1)
    inner_rows = (
        collected[1 : row_count + 1]
        + jnp.pad(from_above, ((0, row_count - 1), (0, 0), (0, 0)))
        + jnp.pad(from_below, ((row_count - 1, 0), (0, 0), (0, 0)))
    )
    left_rim = inner_rows[:, :tap_reach]
    right_rim = inner_rows[:, col_count + tap_reach :]
    from_right = from_behind(left_rim.astype(jnp.bfloat16), "lon", -1).astype(left_rim.dtype)
    from_left = from_behind(right_rim, "lon", 1)
    gathered = (
        inner_rows[:, tap_reach : tap_reach + col_count]
        + jnp.pad(from_right, ((0, 0), (col_count - tap_reach, 0), (0, 0)))
        + jnp.pad(from_left, ((0, 0), (0, col_count - tap_reach), (0, 0)))
    )
    input_grad = (gathered * own_mask).astype(jnp.bfloat16)
    return (infilled, input_grad, weight_grad)


def solution(mesh):
    placed = (P("lat", "lon", None), P("lat", "lon", None), P(), P(), P(), P("lat", "lon", None))
    return jax.shard_map(
        local,
        mesh=mesh,
        in_specs=placed,
        out_specs=(P("lat", "lon", None), P("lat", "lon", None), P()),
        check_vma=False,
    )
```

```python
import math

import jax
import jax.numpy as jnp
from jax import lax
from jax.experimental import pallas as pl
from jax.experimental.pallas import tpu as pltpu
from jax.sharding import PartitionSpec as P


def with_halo(block, sides, width, periodic):
    for axis, dim in sides:
        count = lax.axis_size(axis)
        forward = [(i, i + 1) for i in range(count - 1)]
        if periodic:
            forward.append((count - 1, 0))
        backward = [(target, source) for source, target in forward]
        low = lax.ppermute(
            lax.slice_in_dim(block, block.shape[dim] - width, None, axis=dim), axis, forward
        )
        high = lax.ppermute(lax.slice_in_dim(block, 0, width, axis=dim), axis, backward)
        block = jnp.concatenate([low, block, high], axis=dim)
    return block


def passed_along(block, axis, distance):
    devices = range(lax.axis_size(axis))
    route = [(i - distance, i) for i in devices if i - distance in devices]
    return lax.ppermute(block, axis, route)


def from_behind(x, axis, by):
    size = lax.axis_size(axis)
    return lax.ppermute(x, axis, [(i, (i + by) % size) for i in range(size)])


def butterfly_sum(value, rounds):
    for axis, step in rounds:
        count = lax.axis_size(axis)
        partner = lax.ppermute(value, axis, [(i, i ^ step) for i in range(count)])
        value = value + partner
    return value


def butterfly_rounds(axis):
    count = lax.axis_size(axis)
    return [(axis, 1 << k) for k in range(count.bit_length() - 1)]


def forward_kernel(x_ref, m_ref, t_ref, cot_ref, w_ref, inf_ref, wg_ref, pulled_ref, scaled_ref, safe_ref):
    rows, basis_count, lat_taps, col_pad, lane_rows = t_ref.shape
    col_count = inf_ref.shape[1]
    chan_count = w_ref.shape[1]
    group_width = wg_ref.shape[1]

    def body(i, carry):
        numerator = None
        denominator = None
        for a in range(lat_taps):
            band = t_ref[i, :, a].reshape(basis_count * col_pad, lane_rows)
            start = pl.multiple_of((i + a) * lane_rows, lane_rows)
            num = jnp.dot(band, x_ref[pl.ds(start, lane_rows), :], preferred_element_type=jnp.float32)
            den = jnp.dot(band, m_ref[pl.ds(start, lane_rows), :], preferred_element_type=jnp.float32)
            numerator = num if numerator is None else numerator + num
            denominator = den if denominator is None else denominator + den
        safe = jnp.maximum(denominator, 1.0)
        scaled = (numerator / safe).astype(jnp.bfloat16)
        rows_at = pl.ds(pl.multiple_of(i * col_pad, col_pad), col_pad)
        for b in range(basis_count):
            scaled_ref[b, rows_at, :] = scaled[b * col_pad : (b + 1) * col_pad]
            safe_ref[b, rows_at, :] = safe[b * col_pad : (b + 1) * col_pad]
        return carry

    lax.fori_loop(0, rows, body, 0)
    lane = lax.broadcasted_iota(jnp.int32, (group_width, chan_count), 1) // group_width
    upstream_all = cot_ref[...].reshape(rows * col_pad, chan_count)
    out = None
    for b in range(basis_count):
        part = scaled_ref[b]
        mixed = jnp.dot(part, w_ref[b], preferred_element_type=jnp.float32)
        out = mixed if out is None else out + mixed
        grad = lax.dot_general(
            part, upstream_all, (((0,), (0,)), ((), ())), preferred_element_type=jnp.float32
        )
        total = jnp.zeros((group_width, chan_count), jnp.float32)
        for g in range(chan_count // group_width):
            block = grad[g * group_width : (g + 1) * group_width, :]
            total = total + jnp.where(lane == g, block, 0.0)
        wg_ref[b] = total
        back = lax.dot_general(
            upstream_all, w_ref[b], (((1,), (1,)), ((), ())), preferred_element_type=jnp.float32
        )
        pulled_ref[b] = (back / safe_ref[b]).astype(jnp.bfloat16)
    for i in range(rows):
        inf_ref[i] = out[i * col_pad : i * col_pad + col_count].astype(inf_ref.dtype)


def adjoint_kernel(t_ref, pulled_ref, order_ref, col_ref):
    rows, basis_count, lat_taps, col_pad, lane_rows = t_ref.shape
    col_ref[...] = jnp.zeros_like(col_ref)

    def body(i, carry):
        rows_at = pl.ds(pl.multiple_of(i * col_pad, col_pad), col_pad)
        pulled = jnp.concatenate([pulled_ref[b, rows_at, :] for b in range(basis_count)], axis=0)
        for a in range(lat_taps):
            band = t_ref[i, :, a].reshape(basis_count * col_pad, lane_rows)
            start = pl.multiple_of((i + a) * lane_rows, lane_rows)
            term = lax.dot_general(
                band, pulled, (((0,), (0,)), ((), ())), preferred_element_type=jnp.float32
            )
            col_ref[pl.ds(start, lane_rows), :] += term
        return carry

    lax.fori_loop(0, rows, body, 0)


def local(features, obs_mask, filter_taps, band_width, mixing, cotangent):
    row_count, col_count, chan_count = features.shape
    group_count = obs_mask.shape[2]
    group_width = chan_count // group_count
    basis_count = mixing.shape[1]
    tap_count = filter_taps.shape[3]
    tap_reach = (tap_count - 1) // 2
    padded_cols = col_count + 2 * tap_reach
    lane_rows = -(-padded_cols // 16) * 16
    col_pad = -(-col_count // 16) * 16
    mask_values = obs_mask.astype(jnp.bfloat16)
    spread = (
        jnp.arange(chan_count)[None, :] // group_width == jnp.arange(group_count)[:, None]
    ).astype(jnp.bfloat16)
    own_mask = jnp.dot(
        mask_values.reshape(row_count * col_count, group_count), spread,
        preferred_element_type=jnp.float32,
    ).astype(jnp.bfloat16).reshape(row_count, col_count, chan_count)
    masked = features * own_mask
    packed = jnp.concatenate([masked, mask_values], axis=-1)
    packed = with_halo(packed, (("lat", 0),), 1, False)
    packed = with_halo(packed, (("lon", 1),), tap_reach, True)
    packed = jnp.pad(packed, ((0, 0), (0, lane_rows - padded_cols), (0, 0)))
    full_input = packed[..., :chan_count].reshape((row_count + 2) * lane_rows, chan_count)
    full_mask = jnp.dot(
        packed[..., chan_count:].reshape((row_count + 2) * lane_rows, group_count), spread,
        preferred_element_type=jnp.float32,
    ).astype(jnp.bfloat16)

    offsets = jnp.arange(tap_count) - tap_reach
    allowed = jnp.abs(offsets)[None, :] <= band_width[:, None]
    global_taps = filter_taps * allowed[:, None, None, :].astype(jnp.bfloat16)
    first_row = lax.axis_index("lat") * row_count
    local_taps = lax.dynamic_slice_in_dim(global_taps, first_row, row_count, 0)
    padded_index = jnp.arange(lane_rows)
    output_index = jnp.arange(col_pad)
    tap_index = jnp.arange(tap_count)
    forward_table = (
        (padded_index[None, None, :] - output_index[None, :, None] == tap_index[:, None, None])
        & (output_index[None, :, None] < col_count)
    ).astype(jnp.bfloat16)
    band = (
        jnp.einsum("ibae,ejp->ibajp", local_taps, forward_table, preferred_element_type=jnp.float32)
        .astype(jnp.bfloat16)
    )

    eye = jnp.eye(group_count, dtype=mixing.dtype)
    mix_blocks = jnp.einsum("gbco,gh->bgcho", mixing, eye).reshape(basis_count, chan_count, chan_count)
    upstream = jnp.pad(cotangent, ((0, 0), (0, col_pad - col_count), (0, 0)))

    vmem = pl.BlockSpec(memory_space=pltpu.VMEM)
    params = pltpu.CompilerParams(vmem_limit_bytes=48 * 1024 * 1024)
    infilled, grad_blocks, pulled = pl.pallas_call(
        forward_kernel,
        out_shape=(
            jax.ShapeDtypeStruct((row_count, col_count, chan_count), jnp.bfloat16),
            jax.ShapeDtypeStruct((basis_count, group_width, chan_count), jnp.float32),
            jax.ShapeDtypeStruct((basis_count, row_count * col_pad, chan_count), jnp.bfloat16),
        ),
        in_specs=[vmem] * 5,
        out_specs=[vmem] * 3,
        scratch_shapes=[
            pltpu.VMEM((basis_count, row_count * col_pad, chan_count), jnp.bfloat16),
            pltpu.VMEM((basis_count, row_count * col_pad, chan_count), jnp.float32),
        ],
        compiler_params=params,
        cost_estimate=pl.CostEstimate(
            flops=2 * row_count * basis_count * col_pad * chan_count * (6 * lane_rows + 3 * chan_count),
            transcendentals=0,
            bytes_accessed=8 * (row_count + 2) * lane_rows * chan_count,
        ),
    )(full_input, full_mask, band, upstream, mix_blocks)

    cell_count = row_count * lax.axis_size("lat") * col_count * lax.axis_size("lon")
    lat_count = lax.axis_size("lat")
    lon_count = lax.axis_size("lon")
    if lat_count & (lat_count - 1) or lon_count & (lon_count - 1):
        first = grad_blocks
        dense = lax.psum(grad_blocks, ("lat", "lon"))
    else:
        first = lax.ppermute(grad_blocks, "lat", [(i, i ^ 1) for i in range(lat_count)])
        rounds = butterfly_rounds("lon") + butterfly_rounds("lat")[1:]
        dense = butterfly_sum(grad_blocks + first, rounds)
    dense = dense * (1.0 / math.sqrt(cell_count))
    weight_grad = dense.reshape(basis_count, group_width, group_count, group_width).transpose(2, 0, 1, 3)

    collected = pl.pallas_call(
        adjoint_kernel,
        out_shape=jax.ShapeDtypeStruct(((row_count + 2) * lane_rows, chan_count), jnp.float32),
        in_specs=[vmem, vmem, pl.BlockSpec(memory_space=pl.ANY)],
        out_specs=vmem,
        compiler_params=params,
        cost_estimate=pl.CostEstimate(
            flops=6 * row_count * basis_count * col_pad * lane_rows * chan_count,
            transcendentals=0,
            bytes_accessed=6 * (row_count + 2) * lane_rows * chan_count,
        ),
    )(band, pulled, first)

    collected = collected.reshape(row_count + 2, lane_rows, chan_count)[:, :padded_cols]
    from_below = passed_along(collected[0:1], "lat", -1)
    from_above = passed_along(collected[row_count + 1 : row_count + 2], "lat", 1)
    inner_rows = (
        collected[1 : row_count + 1]
        + jnp.pad(from_above, ((0, row_count - 1), (0, 0), (0, 0)))
        + jnp.pad(from_below, ((row_count - 1, 0), (0, 0), (0, 0)))
    )
    left_rim = inner_rows[:, :tap_reach]
    right_rim = inner_rows[:, col_count + tap_reach :]
    from_right = from_behind(left_rim.astype(jnp.bfloat16), "lon", -1).astype(left_rim.dtype)
    from_left = from_behind(right_rim, "lon", 1)
    gathered = (
        inner_rows[:, tap_reach : tap_reach + col_count]
        + jnp.pad(from_right, ((0, 0), (col_count - tap_reach, 0), (0, 0)))
        + jnp.pad(from_left, ((0, 0), (0, col_count - tap_reach), (0, 0)))
    )
    input_grad = (gathered * own_mask).astype(jnp.bfloat16)
    return (infilled, input_grad, weight_grad)


def solution(mesh):
    placed = (P("lat", "lon", None), P("lat", "lon", None), P(), P(), P(), P("lat", "lon", None))
    return jax.shard_map(
        local,
        mesh=mesh,
        in_specs=placed,
        out_specs=(P("lat", "lon", None), P("lat", "lon", None), P()),
        check_vma=False,
    )
```

```python
import math

import jax
import jax.numpy as jnp
from jax import lax
from jax.experimental import pallas as pl
from jax.experimental.pallas import tpu as pltpu
from jax.sharding import PartitionSpec as P


def with_halo(block, sides, width, periodic):
    for axis, dim in sides:
        count = lax.axis_size(axis)
        forward = [(i, i + 1) for i in range(count - 1)]
        if periodic:
            forward.append((count - 1, 0))
        backward = [(target, source) for source, target in forward]
        low = lax.ppermute(
            lax.slice_in_dim(block, block.shape[dim] - width, None, axis=dim), axis, forward
        )
        high = lax.ppermute(lax.slice_in_dim(block, 0, width, axis=dim), axis, backward)
        block = jnp.concatenate([low, block, high], axis=dim)
    return block


def passed_along(block, axis, distance):
    devices = range(lax.axis_size(axis))
    route = [(i - distance, i) for i in devices if i - distance in devices]
    return lax.ppermute(block, axis, route)


def from_behind(x, axis, by):
    size = lax.axis_size(axis)
    return lax.ppermute(x, axis, [(i, (i + by) % size) for i in range(size)])


def butterfly_sum(value, axes, skip=0):
    for axis in axes:
        count = lax.axis_size(axis)
        if count & (count - 1):
            value = lax.psum(value, axis)
            continue
        step = 1
        while step < count:
            if skip:
                skip -= 1
                step *= 2
                continue
            partner = lax.ppermute(value, axis, [(i, i ^ step) for i in range(count)])
            value = value + partner
            step *= 2
    return value


def forward_kernel(x_ref, m_ref, t_ref, cot_ref, w_ref, inf_ref, wg_ref, pulled_ref, scaled_ref, safe_ref):
    rows, basis_count, lat_taps, col_pad, lane_rows = t_ref.shape
    col_count = inf_ref.shape[1]
    chan_count = w_ref.shape[1]
    group_width = wg_ref.shape[1]

    def body(i, carry):
        numerator = None
        denominator = None
        for a in range(lat_taps):
            band = t_ref[i, :, a].reshape(basis_count * col_pad, lane_rows)
            start = pl.multiple_of((i + a) * lane_rows, lane_rows)
            num = jnp.dot(band, x_ref[pl.ds(start, lane_rows), :], preferred_element_type=jnp.float32)
            den = jnp.dot(band, m_ref[pl.ds(start, lane_rows), :], preferred_element_type=jnp.float32)
            numerator = num if numerator is None else numerator + num
            denominator = den if denominator is None else denominator + den
        safe = jnp.maximum(denominator, 1.0)
        scaled = (numerator / safe).astype(jnp.bfloat16)
        rows_at = pl.ds(pl.multiple_of(i * col_pad, col_pad), col_pad)
        for b in range(basis_count):
            scaled_ref[b, rows_at, :] = scaled[b * col_pad : (b + 1) * col_pad]
            safe_ref[b, rows_at, :] = safe[b * col_pad : (b + 1) * col_pad]
        return carry

    lax.fori_loop(0, rows, body, 0, unroll=2)
    lane = lax.broadcasted_iota(jnp.int32, (group_width, chan_count), 1) // group_width
    upstream_all = cot_ref[...].reshape(rows * col_pad, chan_count)
    out = None
    for b in range(basis_count):
        part = scaled_ref[b]
        mixed = jnp.dot(part, w_ref[b], preferred_element_type=jnp.float32)
        out = mixed if out is None else out + mixed
        grad = lax.dot_general(
            part, upstream_all, (((0,), (0,)), ((), ())), preferred_element_type=jnp.float32
        )
        total = jnp.zeros((group_width, chan_count), jnp.float32)
        for g in range(chan_count // group_width):
            block = grad[g * group_width : (g + 1) * group_width, :]
            total = total + jnp.where(lane == g, block, 0.0)
        wg_ref[b] = total
        back = lax.dot_general(
            upstream_all, w_ref[b], (((1,), (1,)), ((), ())), preferred_element_type=jnp.float32
        )
        pulled_ref[b] = (back / safe_ref[b]).astype(jnp.bfloat16)
    for i in range(rows):
        inf_ref[i] = out[i * col_pad : i * col_pad + col_count].astype(inf_ref.dtype)


def adjoint_kernel(t_ref, pulled_ref, order_ref, col_ref):
    rows, basis_count, lat_taps, col_pad, lane_rows = t_ref.shape
    col_ref[...] = jnp.zeros_like(col_ref)

    def body(i, carry):
        rows_at = pl.ds(pl.multiple_of(i * col_pad, col_pad), col_pad)
        pulled = jnp.concatenate([pulled_ref[b, rows_at, :] for b in range(basis_count)], axis=0)
        for a in range(lat_taps):
            band = t_ref[i, :, a].reshape(basis_count * col_pad, lane_rows)
            start = pl.multiple_of((i + a) * lane_rows, lane_rows)
            term = lax.dot_general(
                band, pulled, (((0,), (0,)), ((), ())), preferred_element_type=jnp.float32
            )
            col_ref[pl.ds(start, lane_rows), :] += term
        return carry

    lax.fori_loop(0, rows, body, 0, unroll=2)


def local(features, obs_mask, filter_taps, band_width, mixing, cotangent):
    row_count, col_count, chan_count = features.shape
    group_count = obs_mask.shape[2]
    group_width = chan_count // group_count
    basis_count = mixing.shape[1]
    tap_count = filter_taps.shape[3]
    tap_reach = (tap_count - 1) // 2
    padded_cols = col_count + 2 * tap_reach
    lane_rows = -(-padded_cols // 16) * 16
    col_pad = -(-col_count // 16) * 16
    mask_values = obs_mask.astype(jnp.bfloat16)
    spread = (
        jnp.arange(chan_count)[None, :] // group_width == jnp.arange(group_count)[:, None]
    ).astype(jnp.bfloat16)
    own_mask = jnp.dot(
        mask_values.reshape(row_count * col_count, group_count), spread,
        preferred_element_type=jnp.float32,
    ).astype(jnp.bfloat16).reshape(row_count, col_count, chan_count)
    masked = features * own_mask
    packed = jnp.concatenate([masked, mask_values], axis=-1)
    packed = with_halo(packed, (("lat", 0),), 1, False)
    packed = with_halo(packed, (("lon", 1),), tap_reach, True)
    packed = jnp.pad(packed, ((0, 0), (0, lane_rows - padded_cols), (0, 0)))
    full_input = packed[..., :chan_count].reshape((row_count + 2) * lane_rows, chan_count)
    full_mask = jnp.dot(
        packed[..., chan_count:].reshape((row_count + 2) * lane_rows, group_count), spread,
        preferred_element_type=jnp.float32,
    ).astype(jnp.bfloat16)

    offsets = jnp.arange(tap_count) - tap_reach
    allowed = jnp.abs(offsets)[None, :] <= band_width[:, None]
    global_taps = filter_taps * allowed[:, None, None, :].astype(jnp.bfloat16)
    first_row = lax.axis_index("lat") * row_count
    local_taps = lax.dynamic_slice_in_dim(global_taps, first_row, row_count, 0)
    padded_index = jnp.arange(lane_rows)
    output_index = jnp.arange(col_pad)
    tap_index = jnp.arange(tap_count)
    forward_table = (
        (padded_index[None, None, :] - output_index[None, :, None] == tap_index[:, None, None])
        & (output_index[None, :, None] < col_count)
    ).astype(jnp.bfloat16)
    band = (
        jnp.einsum("ibae,ejp->ibajp", local_taps, forward_table, preferred_element_type=jnp.float32)
        .astype(jnp.bfloat16)
    )

    eye = jnp.eye(group_count, dtype=mixing.dtype)
    mix_blocks = jnp.einsum("gbco,gh->bgcho", mixing, eye).reshape(basis_count, chan_count, chan_count)
    upstream = jnp.pad(cotangent, ((0, 0), (0, col_pad - col_count), (0, 0)))

    vmem = pl.BlockSpec(memory_space=pltpu.VMEM)
    params = pltpu.CompilerParams(vmem_limit_bytes=48 * 1024 * 1024)
    infilled, grad_blocks, pulled = pl.pallas_call(
        forward_kernel,
        out_shape=(
            jax.ShapeDtypeStruct((row_count, col_count, chan_count), jnp.bfloat16),
            jax.ShapeDtypeStruct((basis_count, group_width, chan_count), jnp.float32),
            jax.ShapeDtypeStruct((basis_count, row_count * col_pad, chan_count), jnp.bfloat16),
        ),
        in_specs=[vmem] * 5,
        out_specs=[vmem] * 3,
        scratch_shapes=[
            pltpu.VMEM((basis_count, row_count * col_pad, chan_count), jnp.bfloat16),
            pltpu.VMEM((basis_count, row_count * col_pad, chan_count), jnp.float32),
        ],
        compiler_params=params,
        cost_estimate=pl.CostEstimate(
            flops=2 * row_count * basis_count * col_pad * chan_count * (6 * lane_rows + 3 * chan_count),
            transcendentals=0,
            bytes_accessed=8 * (row_count + 2) * lane_rows * chan_count,
        ),
    )(full_input, full_mask, band, upstream, mix_blocks)

    cell_count = row_count * lax.axis_size("lat") * col_count * lax.axis_size("lon")
    lat_count = lax.axis_size("lat")
    if lat_count % 2 == 0:
        first = lax.ppermute(grad_blocks, "lat", [(i, i ^ 1) for i in range(lat_count)])
        dense = butterfly_sum(grad_blocks + first, ("lat", "lon"), skip=1)
    else:
        first = grad_blocks
        dense = butterfly_sum(grad_blocks, ("lat", "lon"))
    dense = dense * (1.0 / math.sqrt(cell_count))
    weight_grad = dense.reshape(basis_count, group_width, group_count, group_width).transpose(2, 0, 1, 3)

    collected = pl.pallas_call(
        adjoint_kernel,
        out_shape=jax.ShapeDtypeStruct(((row_count + 2) * lane_rows, chan_count), jnp.float32),
        in_specs=[vmem, vmem, pl.BlockSpec(memory_space=pl.ANY)],
        out_specs=vmem,
        compiler_params=params,
        cost_estimate=pl.CostEstimate(
            flops=6 * row_count * basis_count * col_pad * lane_rows * chan_count,
            transcendentals=0,
            bytes_accessed=6 * (row_count + 2) * lane_rows * chan_count,
        ),
    )(band, pulled, first)

    collected = collected.reshape(row_count + 2, lane_rows, chan_count)[:, :padded_cols]
    from_below = passed_along(collected[0:1], "lat", -1)
    from_above = passed_along(collected[row_count + 1 : row_count + 2], "lat", 1)
    inner_rows = (
        collected[1 : row_count + 1]
        + jnp.pad(from_above, ((0, row_count - 1), (0, 0), (0, 0)))
        + jnp.pad(from_below, ((row_count - 1, 0), (0, 0), (0, 0)))
    )
    left_rim = inner_rows[:, :tap_reach]
    right_rim = inner_rows[:, col_count + tap_reach :]
    from_right = from_behind(left_rim.astype(jnp.bfloat16), "lon", -1).astype(left_rim.dtype)
    from_left = from_behind(right_rim, "lon", 1)
    gathered = (
        inner_rows[:, tap_reach : tap_reach + col_count]
        + jnp.pad(from_right, ((0, 0), (col_count - tap_reach, 0), (0, 0)))
        + jnp.pad(from_left, ((0, 0), (0, col_count - tap_reach), (0, 0)))
    )
    input_grad = (gathered * own_mask).astype(jnp.bfloat16)
    return (infilled, input_grad, weight_grad)


def solution(mesh):
    placed = (P("lat", "lon", None), P("lat", "lon", None), P(), P(), P(), P("lat", "lon", None))
    return jax.shard_map(
        local,
        mesh=mesh,
        in_specs=placed,
        out_specs=(P("lat", "lon", None), P("lat", "lon", None), P()),
        check_vma=False,
    )
```

```python
import math

import jax
import jax.numpy as jnp
from jax import lax
from jax.experimental import pallas as pl
from jax.experimental.pallas import tpu as pltpu
from jax.sharding import PartitionSpec as P


def with_halo(block, sides, width, periodic):
    for axis, dim in sides:
        count = lax.axis_size(axis)
        forward = [(i, i + 1) for i in range(count - 1)]
        if periodic:
            forward.append((count - 1, 0))
        backward = [(target, source) for source, target in forward]
        low = lax.ppermute(
            lax.slice_in_dim(block, block.shape[dim] - width, None, axis=dim), axis, forward
        )
        high = lax.ppermute(lax.slice_in_dim(block, 0, width, axis=dim), axis, backward)
        block = jnp.concatenate([low, block, high], axis=dim)
    return block


def passed_along(block, axis, distance):
    devices = range(lax.axis_size(axis))
    route = [(i - distance, i) for i in devices if i - distance in devices]
    return lax.ppermute(block, axis, route)


def from_behind(x, axis, by):
    size = lax.axis_size(axis)
    return lax.ppermute(x, axis, [(i, (i + by) % size) for i in range(size)])


def butterfly_sum(value, axes, skip=0):
    for axis in axes:
        count = lax.axis_size(axis)
        if count & (count - 1):
            value = lax.psum(value, axis)
            continue
        step = 1
        while step < count:
            if skip:
                skip -= 1
                step *= 2
                continue
            partner = lax.ppermute(value, axis, [(i, i ^ step) for i in range(count)])
            value = value + partner
            step *= 2
    return value


def forward_kernel(x_ref, m_ref, t_ref, cot_ref, w_ref, inf_ref, wg_ref, pulled_ref, scaled_ref, safe_ref):
    rows, basis_count, lat_taps, col_pad, lane_rows = t_ref.shape
    col_count = inf_ref.shape[1]
    chan_count = w_ref.shape[1]
    group_width = wg_ref.shape[1]

    def body(i, carry):
        numerator = None
        denominator = None
        for a in range(lat_taps):
            band = t_ref[i, :, a].reshape(basis_count * col_pad, lane_rows)
            start = pl.multiple_of((i + a) * lane_rows, lane_rows)
            num = jnp.dot(band, x_ref[pl.ds(start, lane_rows), :], preferred_element_type=jnp.float32)
            den = jnp.dot(band, m_ref[pl.ds(start, lane_rows), :], preferred_element_type=jnp.float32)
            numerator = num if numerator is None else numerator + num
            denominator = den if denominator is None else denominator + den
        safe = jnp.maximum(denominator, 1.0)
        scaled = (numerator / safe).astype(jnp.bfloat16)
        rows_at = pl.ds(pl.multiple_of(i * col_pad, col_pad), col_pad)
        for b in range(basis_count):
            scaled_ref[b, rows_at, :] = scaled[b * col_pad : (b + 1) * col_pad]
            safe_ref[b, rows_at, :] = safe[b * col_pad : (b + 1) * col_pad]
        return carry

    lax.fori_loop(0, rows, body, 0, unroll=4)
    lane = lax.broadcasted_iota(jnp.int32, (group_width, chan_count), 1) // group_width
    upstream_all = cot_ref[...].reshape(rows * col_pad, chan_count)
    out = None
    for b in range(basis_count):
        part = scaled_ref[b]
        mixed = jnp.dot(part, w_ref[b], preferred_element_type=jnp.float32)
        out = mixed if out is None else out + mixed
        grad = lax.dot_general(
            part, upstream_all, (((0,), (0,)), ((), ())), preferred_element_type=jnp.float32
        )
        total = jnp.zeros((group_width, chan_count), jnp.float32)
        for g in range(chan_count // group_width):
            block = grad[g * group_width : (g + 1) * group_width, :]
            total = total + jnp.where(lane == g, block, 0.0)
        wg_ref[b] = total
        back = lax.dot_general(
            upstream_all, w_ref[b], (((1,), (1,)), ((), ())), preferred_element_type=jnp.float32
        )
        pulled_ref[b] = (back / safe_ref[b]).astype(jnp.bfloat16)
    for i in range(rows):
        inf_ref[i] = out[i * col_pad : i * col_pad + col_count].astype(inf_ref.dtype)


def adjoint_kernel(t_ref, pulled_ref, order_ref, col_ref):
    rows, basis_count, lat_taps, col_pad, lane_rows = t_ref.shape
    col_ref[...] = jnp.zeros_like(col_ref)

    def body(i, carry):
        rows_at = pl.ds(pl.multiple_of(i * col_pad, col_pad), col_pad)
        pulled = jnp.concatenate([pulled_ref[b, rows_at, :] for b in range(basis_count)], axis=0)
        for a in range(lat_taps):
            band = t_ref[i, :, a].reshape(basis_count * col_pad, lane_rows)
            start = pl.multiple_of((i + a) * lane_rows, lane_rows)
            term = lax.dot_general(
                band, pulled, (((0,), (0,)), ((), ())), preferred_element_type=jnp.float32
            )
            col_ref[pl.ds(start, lane_rows), :] += term
        return carry

    lax.fori_loop(0, rows, body, 0, unroll=4)


def local(features, obs_mask, filter_taps, band_width, mixing, cotangent):
    row_count, col_count, chan_count = features.shape
    group_count = obs_mask.shape[2]
    group_width = chan_count // group_count
    basis_count = mixing.shape[1]
    tap_count = filter_taps.shape[3]
    tap_reach = (tap_count - 1) // 2
    padded_cols = col_count + 2 * tap_reach
    lane_rows = -(-padded_cols // 16) * 16
    col_pad = -(-col_count // 16) * 16
    mask_values = obs_mask.astype(jnp.bfloat16)
    spread = (
        jnp.arange(chan_count)[None, :] // group_width == jnp.arange(group_count)[:, None]
    ).astype(jnp.bfloat16)
    own_mask = jnp.dot(
        mask_values.reshape(row_count * col_count, group_count), spread,
        preferred_element_type=jnp.float32,
    ).astype(jnp.bfloat16).reshape(row_count, col_count, chan_count)
    masked = features * own_mask
    packed = jnp.concatenate([masked, mask_values], axis=-1)
    packed = with_halo(packed, (("lat", 0),), 1, False)
    packed = with_halo(packed, (("lon", 1),), tap_reach, True)
    packed = jnp.pad(packed, ((0, 0), (0, lane_rows - padded_cols), (0, 0)))
    full_input = packed[..., :chan_count].reshape((row_count + 2) * lane_rows, chan_count)
    full_mask = jnp.dot(
        packed[..., chan_count:].reshape((row_count + 2) * lane_rows, group_count), spread,
        preferred_element_type=jnp.float32,
    ).astype(jnp.bfloat16)

    offsets = jnp.arange(tap_count) - tap_reach
    allowed = jnp.abs(offsets)[None, :] <= band_width[:, None]
    global_taps = filter_taps * allowed[:, None, None, :].astype(jnp.bfloat16)
    first_row = lax.axis_index("lat") * row_count
    local_taps = lax.dynamic_slice_in_dim(global_taps, first_row, row_count, 0)
    padded_index = jnp.arange(lane_rows)
    output_index = jnp.arange(col_pad)
    tap_index = jnp.arange(tap_count)
    forward_table = (
        (padded_index[None, None, :] - output_index[None, :, None] == tap_index[:, None, None])
        & (output_index[None, :, None] < col_count)
    ).astype(jnp.bfloat16)
    band = (
        jnp.einsum("ibae,ejp->ibajp", local_taps, forward_table, preferred_element_type=jnp.float32)
        .astype(jnp.bfloat16)
    )

    eye = jnp.eye(group_count, dtype=mixing.dtype)
    mix_blocks = jnp.einsum("gbco,gh->bgcho", mixing, eye).reshape(basis_count, chan_count, chan_count)
    upstream = jnp.pad(cotangent, ((0, 0), (0, col_pad - col_count), (0, 0)))

    vmem = pl.BlockSpec(memory_space=pltpu.VMEM)
    params = pltpu.CompilerParams(vmem_limit_bytes=48 * 1024 * 1024)
    infilled, grad_blocks, pulled = pl.pallas_call(
        forward_kernel,
        out_shape=(
            jax.ShapeDtypeStruct((row_count, col_count, chan_count), jnp.bfloat16),
            jax.ShapeDtypeStruct((basis_count, group_width, chan_count), jnp.float32),
            jax.ShapeDtypeStruct((basis_count, row_count * col_pad, chan_count), jnp.bfloat16),
        ),
        in_specs=[vmem] * 5,
        out_specs=[vmem] * 3,
        scratch_shapes=[
            pltpu.VMEM((basis_count, row_count * col_pad, chan_count), jnp.bfloat16),
            pltpu.VMEM((basis_count, row_count * col_pad, chan_count), jnp.float32),
        ],
        compiler_params=params,
        cost_estimate=pl.CostEstimate(
            flops=2 * row_count * basis_count * col_pad * chan_count * (6 * lane_rows + 3 * chan_count),
            transcendentals=0,
            bytes_accessed=8 * (row_count + 2) * lane_rows * chan_count,
        ),
    )(full_input, full_mask, band, upstream, mix_blocks)

    cell_count = row_count * lax.axis_size("lat") * col_count * lax.axis_size("lon")
    lat_count = lax.axis_size("lat")
    if lat_count % 2 == 0:
        first = lax.ppermute(grad_blocks, "lat", [(i, i ^ 1) for i in range(lat_count)])
        dense = butterfly_sum(grad_blocks + first, ("lat", "lon"), skip=1)
    else:
        first = grad_blocks
        dense = butterfly_sum(grad_blocks, ("lat", "lon"))
    dense = dense * (1.0 / math.sqrt(cell_count))
    weight_grad = dense.reshape(basis_count, group_width, group_count, group_width).transpose(2, 0, 1, 3)

    collected = pl.pallas_call(
        adjoint_kernel,
        out_shape=jax.ShapeDtypeStruct(((row_count + 2) * lane_rows, chan_count), jnp.float32),
        in_specs=[vmem, vmem, pl.BlockSpec(memory_space=pl.ANY)],
        out_specs=vmem,
        compiler_params=params,
        cost_estimate=pl.CostEstimate(
            flops=6 * row_count * basis_count * col_pad * lane_rows * chan_count,
            transcendentals=0,
            bytes_accessed=6 * (row_count + 2) * lane_rows * chan_count,
        ),
    )(band, pulled, first)

    collected = collected.reshape(row_count + 2, lane_rows, chan_count)[:, :padded_cols]
    from_below = passed_along(collected[0:1], "lat", -1)
    from_above = passed_along(collected[row_count + 1 : row_count + 2], "lat", 1)
    inner_rows = (
        collected[1 : row_count + 1]
        + jnp.pad(from_above, ((0, row_count - 1), (0, 0), (0, 0)))
        + jnp.pad(from_below, ((row_count - 1, 0), (0, 0), (0, 0)))
    )
    left_rim = inner_rows[:, :tap_reach]
    right_rim = inner_rows[:, col_count + tap_reach :]
    from_right = from_behind(left_rim.astype(jnp.bfloat16), "lon", -1).astype(left_rim.dtype)
    from_left = from_behind(right_rim, "lon", 1)
    gathered = (
        inner_rows[:, tap_reach : tap_reach + col_count]
        + jnp.pad(from_right, ((0, 0), (col_count - tap_reach, 0), (0, 0)))
        + jnp.pad(from_left, ((0, 0), (0, col_count - tap_reach), (0, 0)))
    )
    input_grad = (gathered * own_mask).astype(jnp.bfloat16)
    return (infilled, input_grad, weight_grad)


def solution(mesh):
    placed = (P("lat", "lon", None), P("lat", "lon", None), P(), P(), P(), P("lat", "lon", None))
    return jax.shard_map(
        local,
        mesh=mesh,
        in_specs=placed,
        out_specs=(P("lat", "lon", None), P("lat", "lon", None), P()),
        check_vma=False,
    )
```

```python
import math

import jax
import jax.numpy as jnp
from jax import lax
from jax.experimental import pallas as pl
from jax.experimental.pallas import tpu as pltpu
from jax.sharding import PartitionSpec as P


def with_halo(block, sides, width, periodic):
    for axis, dim in sides:
        count = lax.axis_size(axis)
        forward = [(i, i + 1) for i in range(count - 1)]
        if periodic:
            forward.append((count - 1, 0))
        backward = [(target, source) for source, target in forward]
        low = lax.ppermute(
            lax.slice_in_dim(block, block.shape[dim] - width, None, axis=dim), axis, forward
        )
        high = lax.ppermute(lax.slice_in_dim(block, 0, width, axis=dim), axis, backward)
        block = jnp.concatenate([low, block, high], axis=dim)
    return block


def passed_along(block, axis, distance):
    devices = range(lax.axis_size(axis))
    route = [(i - distance, i) for i in devices if i - distance in devices]
    return lax.ppermute(block, axis, route)


def from_behind(x, axis, by):
    size = lax.axis_size(axis)
    return lax.ppermute(x, axis, [(i, (i + by) % size) for i in range(size)])


def butterfly_sum(value, axes, skip=0):
    for axis in axes:
        count = lax.axis_size(axis)
        if count & (count - 1):
            value = lax.psum(value, axis)
            continue
        step = 1
        while step < count:
            if skip:
                skip -= 1
                step *= 2
                continue
            partner = lax.ppermute(value, axis, [(i, i ^ step) for i in range(count)])
            value = value + partner
            step *= 2
    return value


def forward_kernel(x_ref, m_ref, t_ref, cot_ref, w_ref, inf_ref, wg_ref, pulled_ref, scaled_ref, safe_ref):
    rows, basis_count, lat_taps, col_pad, lane_rows = t_ref.shape
    col_count = inf_ref.shape[1]
    chan_count = w_ref.shape[1]
    group_width = wg_ref.shape[1]

    def body(i, carry):
        numerator = None
        denominator = None
        for a in range(lat_taps):
            band = t_ref[i, :, a].reshape(basis_count * col_pad, lane_rows)
            start = pl.multiple_of((i + a) * lane_rows, lane_rows)
            num = jnp.dot(band, x_ref[pl.ds(start, lane_rows), :], preferred_element_type=jnp.float32)
            den = jnp.dot(band, m_ref[pl.ds(start, lane_rows), :], preferred_element_type=jnp.float32)
            numerator = num if numerator is None else numerator + num
            denominator = den if denominator is None else denominator + den
        safe = jnp.maximum(denominator, 1.0)
        scaled = (numerator / safe).astype(jnp.bfloat16)
        rows_at = pl.ds(pl.multiple_of(i * col_pad, col_pad), col_pad)
        for b in range(basis_count):
            scaled_ref[b, rows_at, :] = scaled[b * col_pad : (b + 1) * col_pad]
            safe_ref[b, rows_at, :] = safe[b * col_pad : (b + 1) * col_pad]
        return carry

    lax.fori_loop(0, rows, body, 0, unroll=8)
    lane = lax.broadcasted_iota(jnp.int32, (group_width, chan_count), 1) // group_width
    upstream_all = cot_ref[...].reshape(rows * col_pad, chan_count)
    out = None
    for b in range(basis_count):
        part = scaled_ref[b]
        mixed = jnp.dot(part, w_ref[b], preferred_element_type=jnp.float32)
        out = mixed if out is None else out + mixed
        grad = lax.dot_general(
            part, upstream_all, (((0,), (0,)), ((), ())), preferred_element_type=jnp.float32
        )
        total = jnp.zeros((group_width, chan_count), jnp.float32)
        for g in range(chan_count // group_width):
            block = grad[g * group_width : (g + 1) * group_width, :]
            total = total + jnp.where(lane == g, block, 0.0)
        wg_ref[b] = total
        back = lax.dot_general(
            upstream_all, w_ref[b], (((1,), (1,)), ((), ())), preferred_element_type=jnp.float32
        )
        pulled_ref[b] = (back / safe_ref[b]).astype(jnp.bfloat16)
    for i in range(rows):
        inf_ref[i] = out[i * col_pad : i * col_pad + col_count].astype(inf_ref.dtype)


def adjoint_kernel(t_ref, pulled_ref, order_ref, col_ref):
    rows, basis_count, lat_taps, col_pad, lane_rows = t_ref.shape
    col_ref[...] = jnp.zeros_like(col_ref)

    def body(i, carry):
        rows_at = pl.ds(pl.multiple_of(i * col_pad, col_pad), col_pad)
        pulled = jnp.concatenate([pulled_ref[b, rows_at, :] for b in range(basis_count)], axis=0)
        for a in range(lat_taps):
            band = t_ref[i, :, a].reshape(basis_count * col_pad, lane_rows)
            start = pl.multiple_of((i + a) * lane_rows, lane_rows)
            term = lax.dot_general(
                band, pulled, (((0,), (0,)), ((), ())), preferred_element_type=jnp.float32
            )
            col_ref[pl.ds(start, lane_rows), :] += term
        return carry

    lax.fori_loop(0, rows, body, 0, unroll=8)


def local(features, obs_mask, filter_taps, band_width, mixing, cotangent):
    row_count, col_count, chan_count = features.shape
    group_count = obs_mask.shape[2]
    group_width = chan_count // group_count
    basis_count = mixing.shape[1]
    tap_count = filter_taps.shape[3]
    tap_reach = (tap_count - 1) // 2
    padded_cols = col_count + 2 * tap_reach
    lane_rows = -(-padded_cols // 16) * 16
    col_pad = -(-col_count // 16) * 16
    mask_values = obs_mask.astype(jnp.bfloat16)
    spread = (
        jnp.arange(chan_count)[None, :] // group_width == jnp.arange(group_count)[:, None]
    ).astype(jnp.bfloat16)
    own_mask = jnp.dot(
        mask_values.reshape(row_count * col_count, group_count), spread,
        preferred_element_type=jnp.float32,
    ).astype(jnp.bfloat16).reshape(row_count, col_count, chan_count)
    masked = features * own_mask
    packed = jnp.concatenate([masked, mask_values], axis=-1)
    packed = with_halo(packed, (("lat", 0),), 1, False)
    packed = with_halo(packed, (("lon", 1),), tap_reach, True)
    packed = jnp.pad(packed, ((0, 0), (0, lane_rows - padded_cols), (0, 0)))
    full_input = packed[..., :chan_count].reshape((row_count + 2) * lane_rows, chan_count)
    full_mask = jnp.dot(
        packed[..., chan_count:].reshape((row_count + 2) * lane_rows, group_count), spread,
        preferred_element_type=jnp.float32,
    ).astype(jnp.bfloat16)

    offsets = jnp.arange(tap_count) - tap_reach
    allowed = jnp.abs(offsets)[None, :] <= band_width[:, None]
    global_taps = filter_taps * allowed[:, None, None, :].astype(jnp.bfloat16)
    first_row = lax.axis_index("lat") * row_count
    local_taps = lax.dynamic_slice_in_dim(global_taps, first_row, row_count, 0)
    padded_index = jnp.arange(lane_rows)
    output_index = jnp.arange(col_pad)
    tap_index = jnp.arange(tap_count)
    forward_table = (
        (padded_index[None, None, :] - output_index[None, :, None] == tap_index[:, None, None])
        & (output_index[None, :, None] < col_count)
    ).astype(jnp.bfloat16)
    band = (
        jnp.einsum("ibae,ejp->ibajp", local_taps, forward_table, preferred_element_type=jnp.float32)
        .astype(jnp.bfloat16)
    )

    eye = jnp.eye(group_count, dtype=mixing.dtype)
    mix_blocks = jnp.einsum("gbco,gh->bgcho", mixing, eye).reshape(basis_count, chan_count, chan_count)
    upstream = jnp.pad(cotangent, ((0, 0), (0, col_pad - col_count), (0, 0)))

    vmem = pl.BlockSpec(memory_space=pltpu.VMEM)
    params = pltpu.CompilerParams(vmem_limit_bytes=48 * 1024 * 1024)
    infilled, grad_blocks, pulled = pl.pallas_call(
        forward_kernel,
        out_shape=(
            jax.ShapeDtypeStruct((row_count, col_count, chan_count), jnp.bfloat16),
            jax.ShapeDtypeStruct((basis_count, group_width, chan_count), jnp.float32),
            jax.ShapeDtypeStruct((basis_count, row_count * col_pad, chan_count), jnp.bfloat16),
        ),
        in_specs=[vmem] * 5,
        out_specs=[vmem] * 3,
        scratch_shapes=[
            pltpu.VMEM((basis_count, row_count * col_pad, chan_count), jnp.bfloat16),
            pltpu.VMEM((basis_count, row_count * col_pad, chan_count), jnp.float32),
        ],
        compiler_params=params,
        cost_estimate=pl.CostEstimate(
            flops=2 * row_count * basis_count * col_pad * chan_count * (6 * lane_rows + 3 * chan_count),
            transcendentals=0,
            bytes_accessed=8 * (row_count + 2) * lane_rows * chan_count,
        ),
    )(full_input, full_mask, band, upstream, mix_blocks)

    cell_count = row_count * lax.axis_size("lat") * col_count * lax.axis_size("lon")
    lat_count = lax.axis_size("lat")
    if lat_count % 2 == 0:
        first = lax.ppermute(grad_blocks, "lat", [(i, i ^ 1) for i in range(lat_count)])
        dense = butterfly_sum(grad_blocks + first, ("lat", "lon"), skip=1)
    else:
        first = grad_blocks
        dense = butterfly_sum(grad_blocks, ("lat", "lon"))
    dense = dense * (1.0 / math.sqrt(cell_count))
    weight_grad = dense.reshape(basis_count, group_width, group_count, group_width).transpose(2, 0, 1, 3)

    collected = pl.pallas_call(
        adjoint_kernel,
        out_shape=jax.ShapeDtypeStruct(((row_count + 2) * lane_rows, chan_count), jnp.float32),
        in_specs=[vmem, vmem, pl.BlockSpec(memory_space=pl.ANY)],
        out_specs=vmem,
        compiler_params=params,
        cost_estimate=pl.CostEstimate(
            flops=6 * row_count * basis_count * col_pad * lane_rows * chan_count,
            transcendentals=0,
            bytes_accessed=6 * (row_count + 2) * lane_rows * chan_count,
        ),
    )(band, pulled, first)

    collected = collected.reshape(row_count + 2, lane_rows, chan_count)[:, :padded_cols]
    from_below = passed_along(collected[0:1], "lat", -1)
    from_above = passed_along(collected[row_count + 1 : row_count + 2], "lat", 1)
    inner_rows = (
        collected[1 : row_count + 1]
        + jnp.pad(from_above, ((0, row_count - 1), (0, 0), (0, 0)))
        + jnp.pad(from_below, ((row_count - 1, 0), (0, 0), (0, 0)))
    )
    left_rim = inner_rows[:, :tap_reach]
    right_rim = inner_rows[:, col_count + tap_reach :]
    from_right = from_behind(left_rim.astype(jnp.bfloat16), "lon", -1).astype(left_rim.dtype)
    from_left = from_behind(right_rim, "lon", 1)
    gathered = (
        inner_rows[:, tap_reach : tap_reach + col_count]
        + jnp.pad(from_right, ((0, 0), (col_count - tap_reach, 0), (0, 0)))
        + jnp.pad(from_left, ((0, 0), (0, col_count - tap_reach), (0, 0)))
    )
    input_grad = (gathered * own_mask).astype(jnp.bfloat16)
    return (infilled, input_grad, weight_grad)


def solution(mesh):
    placed = (P("lat", "lon", None), P("lat", "lon", None), P(), P(), P(), P("lat", "lon", None))
    return jax.shard_map(
        local,
        mesh=mesh,
        in_specs=placed,
        out_specs=(P("lat", "lon", None), P("lat", "lon", None), P()),
        check_vma=False,
    )
```

```python
import math

import jax
import jax.numpy as jnp
from jax import lax
from jax.experimental import pallas as pl
from jax.experimental.pallas import tpu as pltpu
from jax.sharding import PartitionSpec as P


def with_halo(block, sides, width, periodic):
    for axis, dim in sides:
        count = lax.axis_size(axis)
        forward = [(i, i + 1) for i in range(count - 1)]
        if periodic:
            forward.append((count - 1, 0))
        backward = [(target, source) for source, target in forward]
        low = lax.ppermute(
            lax.slice_in_dim(block, block.shape[dim] - width, None, axis=dim), axis, forward
        )
        high = lax.ppermute(lax.slice_in_dim(block, 0, width, axis=dim), axis, backward)
        block = jnp.concatenate([low, block, high], axis=dim)
    return block


def passed_along(block, axis, distance):
    devices = range(lax.axis_size(axis))
    route = [(i - distance, i) for i in devices if i - distance in devices]
    return lax.ppermute(block, axis, route)


def from_behind(x, axis, by):
    size = lax.axis_size(axis)
    return lax.ppermute(x, axis, [(i, (i + by) % size) for i in range(size)])


def butterfly_sum(value, axes, skip=0):
    for axis in axes:
        count = lax.axis_size(axis)
        if count & (count - 1):
            value = lax.psum(value, axis)
            continue
        step = 1
        while step < count:
            if skip:
                skip -= 1
                step *= 2
                continue
            partner = lax.ppermute(value, axis, [(i, i ^ step) for i in range(count)])
            value = value + partner
            step *= 2
    return value


def forward_kernel(x_ref, m_ref, t_ref, cot_ref, w_ref, inf_ref, wg_ref, pulled_ref, scaled_ref, safe_ref):
    rows, basis_count, lat_taps, col_pad, lane_rows = t_ref.shape
    col_count = inf_ref.shape[1]
    chan_count = w_ref.shape[1]
    group_width = wg_ref.shape[1]

    def body(i, carry):
        numerator = None
        denominator = None
        for a in range(lat_taps):
            band = t_ref[i, :, a].reshape(basis_count * col_pad, lane_rows)
            start = pl.multiple_of((i + a) * lane_rows, lane_rows)
            num = jnp.dot(band, x_ref[pl.ds(start, lane_rows), :], preferred_element_type=jnp.float32)
            den = jnp.dot(band, m_ref[pl.ds(start, lane_rows), :], preferred_element_type=jnp.float32)
            numerator = num if numerator is None else numerator + num
            denominator = den if denominator is None else denominator + den
        safe = jnp.maximum(denominator, 1.0)
        scaled = (numerator / safe).astype(jnp.bfloat16)
        rows_at = pl.ds(pl.multiple_of(i * col_pad, col_pad), col_pad)
        for b in range(basis_count):
            scaled_ref[b, rows_at, :] = scaled[b * col_pad : (b + 1) * col_pad]
            safe_ref[b, rows_at, :] = safe[b * col_pad : (b + 1) * col_pad]
        return carry

    lax.fori_loop(0, rows, body, 0, unroll=True)
    lane = lax.broadcasted_iota(jnp.int32, (group_width, chan_count), 1) // group_width
    upstream_all = cot_ref[...].reshape(rows * col_pad, chan_count)
    out = None
    for b in range(basis_count):
        part = scaled_ref[b]
        mixed = jnp.dot(part, w_ref[b], preferred_element_type=jnp.float32)
        out = mixed if out is None else out + mixed
        grad = lax.dot_general(
            part, upstream_all, (((0,), (0,)), ((), ())), preferred_element_type=jnp.float32
        )
        total = jnp.zeros((group_width, chan_count), jnp.float32)
        for g in range(chan_count // group_width):
            block = grad[g * group_width : (g + 1) * group_width, :]
            total = total + jnp.where(lane == g, block, 0.0)
        wg_ref[b] = total
        back = lax.dot_general(
            upstream_all, w_ref[b], (((1,), (1,)), ((), ())), preferred_element_type=jnp.float32
        )
        pulled_ref[b] = (back / safe_ref[b]).astype(jnp.bfloat16)
    for i in range(rows):
        inf_ref[i] = out[i * col_pad : i * col_pad + col_count].astype(inf_ref.dtype)


def adjoint_kernel(t_ref, pulled_ref, order_ref, col_ref):
    rows, basis_count, lat_taps, col_pad, lane_rows = t_ref.shape
    col_ref[...] = jnp.zeros_like(col_ref)

    def body(i, carry):
        rows_at = pl.ds(pl.multiple_of(i * col_pad, col_pad), col_pad)
        pulled = jnp.concatenate([pulled_ref[b, rows_at, :] for b in range(basis_count)], axis=0)
        for a in range(lat_taps):
            band = t_ref[i, :, a].reshape(basis_count * col_pad, lane_rows)
            start = pl.multiple_of((i + a) * lane_rows, lane_rows)
            term = lax.dot_general(
                band, pulled, (((0,), (0,)), ((), ())), preferred_element_type=jnp.float32
            )
            col_ref[pl.ds(start, lane_rows), :] += term
        return carry

    lax.fori_loop(0, rows, body, 0, unroll=True)


def local(features, obs_mask, filter_taps, band_width, mixing, cotangent):
    row_count, col_count, chan_count = features.shape
    group_count = obs_mask.shape[2]
    group_width = chan_count // group_count
    basis_count = mixing.shape[1]
    tap_count = filter_taps.shape[3]
    tap_reach = (tap_count - 1) // 2
    padded_cols = col_count + 2 * tap_reach
    lane_rows = -(-padded_cols // 16) * 16
    col_pad = -(-col_count // 16) * 16
    mask_values = obs_mask.astype(jnp.bfloat16)
    spread = (
        jnp.arange(chan_count)[None, :] // group_width == jnp.arange(group_count)[:, None]
    ).astype(jnp.bfloat16)
    own_mask = jnp.dot(
        mask_values.reshape(row_count * col_count, group_count), spread,
        preferred_element_type=jnp.float32,
    ).astype(jnp.bfloat16).reshape(row_count, col_count, chan_count)
    masked = features * own_mask
    packed = jnp.concatenate([masked, mask_values], axis=-1)
    packed = with_halo(packed, (("lat", 0),), 1, False)
    packed = with_halo(packed, (("lon", 1),), tap_reach, True)
    packed = jnp.pad(packed, ((0, 0), (0, lane_rows - padded_cols), (0, 0)))
    full_input = packed[..., :chan_count].reshape((row_count + 2) * lane_rows, chan_count)
    full_mask = jnp.dot(
        packed[..., chan_count:].reshape((row_count + 2) * lane_rows, group_count), spread,
        preferred_element_type=jnp.float32,
    ).astype(jnp.bfloat16)

    offsets = jnp.arange(tap_count) - tap_reach
    allowed = jnp.abs(offsets)[None, :] <= band_width[:, None]
    global_taps = filter_taps * allowed[:, None, None, :].astype(jnp.bfloat16)
    first_row = lax.axis_index("lat") * row_count
    local_taps = lax.dynamic_slice_in_dim(global_taps, first_row, row_count, 0)
    padded_index = jnp.arange(lane_rows)
    output_index = jnp.arange(col_pad)
    tap_index = jnp.arange(tap_count)
    forward_table = (
        (padded_index[None, None, :] - output_index[None, :, None] == tap_index[:, None, None])
        & (output_index[None, :, None] < col_count)
    ).astype(jnp.bfloat16)
    band = (
        jnp.einsum("ibae,ejp->ibajp", local_taps, forward_table, preferred_element_type=jnp.float32)
        .astype(jnp.bfloat16)
    )

    eye = jnp.eye(group_count, dtype=mixing.dtype)
    mix_blocks = jnp.einsum("gbco,gh->bgcho", mixing, eye).reshape(basis_count, chan_count, chan_count)
    upstream = jnp.pad(cotangent, ((0, 0), (0, col_pad - col_count), (0, 0)))

    vmem = pl.BlockSpec(memory_space=pltpu.VMEM)
    params = pltpu.CompilerParams(vmem_limit_bytes=48 * 1024 * 1024)
    infilled, grad_blocks, pulled = pl.pallas_call(
        forward_kernel,
        out_shape=(
            jax.ShapeDtypeStruct((row_count, col_count, chan_count), jnp.bfloat16),
            jax.ShapeDtypeStruct((basis_count, group_width, chan_count), jnp.float32),
            jax.ShapeDtypeStruct((basis_count, row_count * col_pad, chan_count), jnp.bfloat16),
        ),
        in_specs=[vmem] * 5,
        out_specs=[vmem] * 3,
        scratch_shapes=[
            pltpu.VMEM((basis_count, row_count * col_pad, chan_count), jnp.bfloat16),
            pltpu.VMEM((basis_count, row_count * col_pad, chan_count), jnp.float32),
        ],
        compiler_params=params,
        cost_estimate=pl.CostEstimate(
            flops=2 * row_count * basis_count * col_pad * chan_count * (6 * lane_rows + 3 * chan_count),
            transcendentals=0,
            bytes_accessed=8 * (row_count + 2) * lane_rows * chan_count,
        ),
    )(full_input, full_mask, band, upstream, mix_blocks)

    cell_count = row_count * lax.axis_size("lat") * col_count * lax.axis_size("lon")
    lat_count = lax.axis_size("lat")
    if lat_count % 2 == 0:
        first = lax.ppermute(grad_blocks, "lat", [(i, i ^ 1) for i in range(lat_count)])
        dense = butterfly_sum(grad_blocks + first, ("lat", "lon"), skip=1)
    else:
        first = grad_blocks
        dense = butterfly_sum(grad_blocks, ("lat", "lon"))
    dense = dense * (1.0 / math.sqrt(cell_count))
    weight_grad = dense.reshape(basis_count, group_width, group_count, group_width).transpose(2, 0, 1, 3)

    collected = pl.pallas_call(
        adjoint_kernel,
        out_shape=jax.ShapeDtypeStruct(((row_count + 2) * lane_rows, chan_count), jnp.float32),
        in_specs=[vmem, vmem, pl.BlockSpec(memory_space=pl.ANY)],
        out_specs=vmem,
        compiler_params=params,
        cost_estimate=pl.CostEstimate(
            flops=6 * row_count * basis_count * col_pad * lane_rows * chan_count,
            transcendentals=0,
            bytes_accessed=6 * (row_count + 2) * lane_rows * chan_count,
        ),
    )(band, pulled, first)

    collected = collected.reshape(row_count + 2, lane_rows, chan_count)[:, :padded_cols]
    from_below = passed_along(collected[0:1], "lat", -1)
    from_above = passed_along(collected[row_count + 1 : row_count + 2], "lat", 1)
    inner_rows = (
        collected[1 : row_count + 1]
        + jnp.pad(from_above, ((0, row_count - 1), (0, 0), (0, 0)))
        + jnp.pad(from_below, ((row_count - 1, 0), (0, 0), (0, 0)))
    )
    left_rim = inner_rows[:, :tap_reach]
    right_rim = inner_rows[:, col_count + tap_reach :]
    from_right = from_behind(left_rim.astype(jnp.bfloat16), "lon", -1).astype(left_rim.dtype)
    from_left = from_behind(right_rim, "lon", 1)
    gathered = (
        inner_rows[:, tap_reach : tap_reach + col_count]
        + jnp.pad(from_right, ((0, 0), (col_count - tap_reach, 0), (0, 0)))
        + jnp.pad(from_left, ((0, 0), (0, col_count - tap_reach), (0, 0)))
    )
    input_grad = (gathered * own_mask).astype(jnp.bfloat16)
    return (infilled, input_grad, weight_grad)


def solution(mesh):
    placed = (P("lat", "lon", None), P("lat", "lon", None), P(), P(), P(), P("lat", "lon", None))
    return jax.shard_map(
        local,
        mesh=mesh,
        in_specs=placed,
        out_specs=(P("lat", "lon", None), P("lat", "lon", None), P()),
        check_vma=False,
    )
```

```python
import math

import jax
import jax.numpy as jnp
from jax import lax
from jax.experimental import pallas as pl
from jax.experimental.pallas import tpu as pltpu
from jax.sharding import PartitionSpec as P


def with_halo(block, sides, width, periodic):
    for axis, dim in sides:
        count = lax.axis_size(axis)
        forward = [(i, i + 1) for i in range(count - 1)]
        if periodic:
            forward.append((count - 1, 0))
        backward = [(target, source) for source, target in forward]
        low = lax.ppermute(
            lax.slice_in_dim(block, block.shape[dim] - width, None, axis=dim), axis, forward
        )
        high = lax.ppermute(lax.slice_in_dim(block, 0, width, axis=dim), axis, backward)
        block = jnp.concatenate([low, block, high], axis=dim)
    return block


def passed_along(block, axis, distance):
    devices = range(lax.axis_size(axis))
    route = [(i - distance, i) for i in devices if i - distance in devices]
    return lax.ppermute(block, axis, route)


def from_behind(x, axis, by):
    size = lax.axis_size(axis)
    return lax.ppermute(x, axis, [(i, (i + by) % size) for i in range(size)])


def butterfly_sum(value, axes, skip=0):
    for axis in axes:
        count = lax.axis_size(axis)
        if count & (count - 1):
            value = lax.psum(value, axis)
            continue
        step = 1
        while step < count:
            if skip:
                skip -= 1
                step *= 2
                continue
            partner = lax.ppermute(value, axis, [(i, i ^ step) for i in range(count)])
            value = value + partner
            step *= 2
    return value


def pair_round(value, lat_step, lon_step):
    lat_count = lax.axis_size("lat")
    lon_count = lax.axis_size("lon")
    across_lat = lax.ppermute(value, "lat", [(i, i ^ lat_step) for i in range(lat_count)])
    across_lon = lax.ppermute(value, "lon", [(i, i ^ lon_step) for i in range(lon_count)])
    diagonal = lax.ppermute(
        value,
        ("lat", "lon"),
        [
            (a * lon_count + b, (a ^ lat_step) * lon_count + (b ^ lon_step))
            for a in range(lat_count)
            for b in range(lon_count)
        ],
    )
    held = {(0, 0): value, (1, 0): across_lat, (0, 1): across_lon, (1, 1): diagonal}
    my_lat = (lax.axis_index("lat") // lat_step) % 2
    my_lon = (lax.axis_index("lon") // lon_step) % 2
    total = None
    for x in (0, 1):
        for y in (0, 1):
            piece = None
            for (dx, dy), part in held.items():
                chosen = jnp.where(((my_lat ^ x) == dx) & ((my_lon ^ y) == dy), part, 0.0)
                piece = chosen if piece is None else piece + chosen
            total = piece if total is None else total + piece
    return total


def forward_kernel(x_ref, m_ref, t_ref, cot_ref, w_ref, inf_ref, wg_ref, pulled_ref, scaled_ref, safe_ref):
    rows, basis_count, lat_taps, col_pad, lane_rows = t_ref.shape
    col_count = inf_ref.shape[1]
    chan_count = w_ref.shape[1]
    group_width = wg_ref.shape[1]

    def body(i, carry):
        numerator = None
        denominator = None
        for a in range(lat_taps):
            band = t_ref[i, :, a].reshape(basis_count * col_pad, lane_rows)
            start = pl.multiple_of((i + a) * lane_rows, lane_rows)
            num = jnp.dot(band, x_ref[pl.ds(start, lane_rows), :], preferred_element_type=jnp.float32)
            den = jnp.dot(band, m_ref[pl.ds(start, lane_rows), :], preferred_element_type=jnp.float32)
            numerator = num if numerator is None else numerator + num
            denominator = den if denominator is None else denominator + den
        safe = jnp.maximum(denominator, 1.0)
        scaled = (numerator / safe).astype(jnp.bfloat16)
        rows_at = pl.ds(pl.multiple_of(i * col_pad, col_pad), col_pad)
        for b in range(basis_count):
            scaled_ref[b, rows_at, :] = scaled[b * col_pad : (b + 1) * col_pad]
            safe_ref[b, rows_at, :] = safe[b * col_pad : (b + 1) * col_pad]
        return carry

    lax.fori_loop(0, rows, body, 0, unroll=True)
    lane = lax.broadcasted_iota(jnp.int32, (group_width, chan_count), 1) // group_width
    upstream_all = cot_ref[...].reshape(rows * col_pad, chan_count)
    out = None
    for b in range(basis_count):
        part = scaled_ref[b]
        mixed = jnp.dot(part, w_ref[b], preferred_element_type=jnp.float32)
        out = mixed if out is None else out + mixed
        grad = lax.dot_general(
            part, upstream_all, (((0,), (0,)), ((), ())), preferred_element_type=jnp.float32
        )
        total = jnp.zeros((group_width, chan_count), jnp.float32)
        for g in range(chan_count // group_width):
            block = grad[g * group_width : (g + 1) * group_width, :]
            total = total + jnp.where(lane == g, block, 0.0)
        wg_ref[b] = total
        back = lax.dot_general(
            upstream_all, w_ref[b], (((1,), (1,)), ((), ())), preferred_element_type=jnp.float32
        )
        pulled_ref[b] = (back / safe_ref[b]).astype(jnp.bfloat16)
    for i in range(rows):
        inf_ref[i] = out[i * col_pad : i * col_pad + col_count].astype(inf_ref.dtype)


def adjoint_kernel(t_ref, pulled_ref, order_ref, col_ref):
    rows, basis_count, lat_taps, col_pad, lane_rows = t_ref.shape
    col_ref[...] = jnp.zeros_like(col_ref)

    def body(i, carry):
        rows_at = pl.ds(pl.multiple_of(i * col_pad, col_pad), col_pad)
        pulled = jnp.concatenate([pulled_ref[b, rows_at, :] for b in range(basis_count)], axis=0)
        for a in range(lat_taps):
            band = t_ref[i, :, a].reshape(basis_count * col_pad, lane_rows)
            start = pl.multiple_of((i + a) * lane_rows, lane_rows)
            term = lax.dot_general(
                band, pulled, (((0,), (0,)), ((), ())), preferred_element_type=jnp.float32
            )
            col_ref[pl.ds(start, lane_rows), :] += term
        return carry

    lax.fori_loop(0, rows, body, 0, unroll=True)


def local(features, obs_mask, filter_taps, band_width, mixing, cotangent):
    row_count, col_count, chan_count = features.shape
    group_count = obs_mask.shape[2]
    group_width = chan_count // group_count
    basis_count = mixing.shape[1]
    tap_count = filter_taps.shape[3]
    tap_reach = (tap_count - 1) // 2
    padded_cols = col_count + 2 * tap_reach
    lane_rows = -(-padded_cols // 16) * 16
    col_pad = -(-col_count // 16) * 16
    mask_values = obs_mask.astype(jnp.bfloat16)
    spread = (
        jnp.arange(chan_count)[None, :] // group_width == jnp.arange(group_count)[:, None]
    ).astype(jnp.bfloat16)
    own_mask = jnp.dot(
        mask_values.reshape(row_count * col_count, group_count), spread,
        preferred_element_type=jnp.float32,
    ).astype(jnp.bfloat16).reshape(row_count, col_count, chan_count)
    masked = features * own_mask
    packed = jnp.concatenate([masked, mask_values], axis=-1)
    packed = with_halo(packed, (("lat", 0),), 1, False)
    packed = with_halo(packed, (("lon", 1),), tap_reach, True)
    packed = jnp.pad(packed, ((0, 0), (0, lane_rows - padded_cols), (0, 0)))
    full_input = packed[..., :chan_count].reshape((row_count + 2) * lane_rows, chan_count)
    full_mask = jnp.dot(
        packed[..., chan_count:].reshape((row_count + 2) * lane_rows, group_count), spread,
        preferred_element_type=jnp.float32,
    ).astype(jnp.bfloat16)

    offsets = jnp.arange(tap_count) - tap_reach
    allowed = jnp.abs(offsets)[None, :] <= band_width[:, None]
    global_taps = filter_taps * allowed[:, None, None, :].astype(jnp.bfloat16)
    first_row = lax.axis_index("lat") * row_count
    local_taps = lax.dynamic_slice_in_dim(global_taps, first_row, row_count, 0)
    padded_index = jnp.arange(lane_rows)
    output_index = jnp.arange(col_pad)
    tap_index = jnp.arange(tap_count)
    forward_table = (
        (padded_index[None, None, :] - output_index[None, :, None] == tap_index[:, None, None])
        & (output_index[None, :, None] < col_count)
    ).astype(jnp.bfloat16)
    band = (
        jnp.einsum("ibae,ejp->ibajp", local_taps, forward_table, preferred_element_type=jnp.float32)
        .astype(jnp.bfloat16)
    )

    eye = jnp.eye(group_count, dtype=mixing.dtype)
    mix_blocks = jnp.einsum("gbco,gh->bgcho", mixing, eye).reshape(basis_count, chan_count, chan_count)
    upstream = jnp.pad(cotangent, ((0, 0), (0, col_pad - col_count), (0, 0)))

    vmem = pl.BlockSpec(memory_space=pltpu.VMEM)
    params = pltpu.CompilerParams(vmem_limit_bytes=48 * 1024 * 1024)
    infilled, grad_blocks, pulled = pl.pallas_call(
        forward_kernel,
        out_shape=(
            jax.ShapeDtypeStruct((row_count, col_count, chan_count), jnp.bfloat16),
            jax.ShapeDtypeStruct((basis_count, group_width, chan_count), jnp.float32),
            jax.ShapeDtypeStruct((basis_count, row_count * col_pad, chan_count), jnp.bfloat16),
        ),
        in_specs=[vmem] * 5,
        out_specs=[vmem] * 3,
        scratch_shapes=[
            pltpu.VMEM((basis_count, row_count * col_pad, chan_count), jnp.bfloat16),
            pltpu.VMEM((basis_count, row_count * col_pad, chan_count), jnp.float32),
        ],
        compiler_params=params,
        cost_estimate=pl.CostEstimate(
            flops=2 * row_count * basis_count * col_pad * chan_count * (6 * lane_rows + 3 * chan_count),
            transcendentals=0,
            bytes_accessed=8 * (row_count + 2) * lane_rows * chan_count,
        ),
    )(full_input, full_mask, band, upstream, mix_blocks)

    cell_count = row_count * lax.axis_size("lat") * col_count * lax.axis_size("lon")
    lat_count = lax.axis_size("lat")
    lon_count = lax.axis_size("lon")
    if lat_count > 1 and not lat_count & (lat_count - 1) and not lon_count & (lon_count - 1):
        first = lax.ppermute(grad_blocks, "lat", [(i, i ^ 1) for i in range(lat_count)])
        dense = grad_blocks + first
        lat_steps = [1 << k for k in range(1, lat_count.bit_length() - 1)]
        lon_steps = [1 << k for k in range(lon_count.bit_length() - 1)]
        while lat_steps and lon_steps:
            dense = pair_round(dense, lat_steps.pop(0), lon_steps.pop(0))
        for step in lat_steps:
            dense = dense + lax.ppermute(dense, "lat", [(i, i ^ step) for i in range(lat_count)])
        for step in lon_steps:
            dense = dense + lax.ppermute(dense, "lon", [(i, i ^ step) for i in range(lon_count)])
    else:
        first = grad_blocks
        dense = butterfly_sum(grad_blocks, ("lat", "lon"))
    dense = dense * (1.0 / math.sqrt(cell_count))
    weight_grad = dense.reshape(basis_count, group_width, group_count, group_width).transpose(2, 0, 1, 3)

    collected = pl.pallas_call(
        adjoint_kernel,
        out_shape=jax.ShapeDtypeStruct(((row_count + 2) * lane_rows, chan_count), jnp.float32),
        in_specs=[vmem, vmem, pl.BlockSpec(memory_space=pl.ANY)],
        out_specs=vmem,
        compiler_params=params,
        cost_estimate=pl.CostEstimate(
            flops=6 * row_count * basis_count * col_pad * lane_rows * chan_count,
            transcendentals=0,
            bytes_accessed=6 * (row_count + 2) * lane_rows * chan_count,
        ),
    )(band, pulled, first)

    collected = collected.reshape(row_count + 2, lane_rows, chan_count)[:, :padded_cols]
    from_below = passed_along(collected[0:1], "lat", -1)
    from_above = passed_along(collected[row_count + 1 : row_count + 2], "lat", 1)
    inner_rows = (
        collected[1 : row_count + 1]
        + jnp.pad(from_above, ((0, row_count - 1), (0, 0), (0, 0)))
        + jnp.pad(from_below, ((row_count - 1, 0), (0, 0), (0, 0)))
    )
    left_rim = inner_rows[:, :tap_reach]
    right_rim = inner_rows[:, col_count + tap_reach :]
    from_right = from_behind(left_rim.astype(jnp.bfloat16), "lon", -1).astype(left_rim.dtype)
    from_left = from_behind(right_rim, "lon", 1)
    gathered = (
        inner_rows[:, tap_reach : tap_reach + col_count]
        + jnp.pad(from_right, ((0, 0), (col_count - tap_reach, 0), (0, 0)))
        + jnp.pad(from_left, ((0, 0), (0, col_count - tap_reach), (0, 0)))
    )
    input_grad = (gathered * own_mask).astype(jnp.bfloat16)
    return (infilled, input_grad, weight_grad)


def solution(mesh):
    placed = (P("lat", "lon", None), P("lat", "lon", None), P(), P(), P(), P("lat", "lon", None))
    return jax.shard_map(
        local,
        mesh=mesh,
        in_specs=placed,
        out_specs=(P("lat", "lon", None), P("lat", "lon", None), P()),
        check_vma=False,
    )
```

```python
import math

import jax
import jax.numpy as jnp
from jax import lax
from jax.experimental import pallas as pl
from jax.experimental.pallas import tpu as pltpu
from jax.sharding import PartitionSpec as P


def with_halo(block, sides, width, periodic):
    for axis, dim in sides:
        count = lax.axis_size(axis)
        forward = [(i, i + 1) for i in range(count - 1)]
        if periodic:
            forward.append((count - 1, 0))
        backward = [(target, source) for source, target in forward]
        low = lax.ppermute(
            lax.slice_in_dim(block, block.shape[dim] - width, None, axis=dim), axis, forward
        )
        high = lax.ppermute(lax.slice_in_dim(block, 0, width, axis=dim), axis, backward)
        block = jnp.concatenate([low, block, high], axis=dim)
    return block


def passed_along(block, axis, distance):
    devices = range(lax.axis_size(axis))
    route = [(i - distance, i) for i in devices if i - distance in devices]
    return lax.ppermute(block, axis, route)


def from_behind(x, axis, by):
    size = lax.axis_size(axis)
    return lax.ppermute(x, axis, [(i, (i + by) % size) for i in range(size)])


def butterfly_sum(value, axes, skip=0):
    for axis in axes:
        count = lax.axis_size(axis)
        if count & (count - 1):
            value = lax.psum(value, axis)
            continue
        step = 1
        while step < count:
            if skip:
                skip -= 1
                step *= 2
                continue
            partner = lax.ppermute(value, axis, [(i, i ^ step) for i in range(count)])
            value = value + partner
            step *= 2
    return value


def forward_kernel(x_ref, m_ref, t_ref, cot_ref, w_ref, inf_ref, wg_ref, scaled_ref):
    rows, basis_count, lat_taps, col_pad, lane_rows = t_ref.shape
    col_count = inf_ref.shape[1]
    chan_count = w_ref.shape[1]
    group_width = wg_ref.shape[1]

    def body(i, carry):
        numerator = None
        denominator = None
        for a in range(lat_taps):
            band = t_ref[i, :, a].reshape(basis_count * col_pad, lane_rows)
            start = pl.multiple_of((i + a) * lane_rows, lane_rows)
            num = jnp.dot(band, x_ref[pl.ds(start, lane_rows), :], preferred_element_type=jnp.float32)
            den = jnp.dot(band, m_ref[pl.ds(start, lane_rows), :], preferred_element_type=jnp.float32)
            numerator = num if numerator is None else numerator + num
            denominator = den if denominator is None else denominator + den
        safe = jnp.maximum(denominator, 1.0)
        scaled = (numerator / safe).astype(jnp.bfloat16)
        rows_at = pl.ds(pl.multiple_of(i * col_pad, col_pad), col_pad)
        for b in range(basis_count):
            scaled_ref[b, rows_at, :] = scaled[b * col_pad : (b + 1) * col_pad]
        return carry

    lax.fori_loop(0, rows, body, 0, unroll=True)
    lane = lax.broadcasted_iota(jnp.int32, (group_width, chan_count), 1) // group_width
    upstream_all = cot_ref[...].reshape(rows * col_pad, chan_count)
    out = None
    for b in range(basis_count):
        part = scaled_ref[b]
        grad = lax.dot_general(
            part, upstream_all, (((0,), (0,)), ((), ())), preferred_element_type=jnp.float32
        )
        total = jnp.zeros((group_width, chan_count), jnp.float32)
        for g in range(chan_count // group_width):
            block = grad[g * group_width : (g + 1) * group_width, :]
            total = total + jnp.where(lane == g, block, 0.0)
        wg_ref[b] = total
        mixed = jnp.dot(part, w_ref[b], preferred_element_type=jnp.float32)
        out = mixed if out is None else out + mixed
    for i in range(rows):
        inf_ref[i] = out[i * col_pad : i * col_pad + col_count].astype(inf_ref.dtype)


def adjoint_kernel(m_ref, t_ref, cot_ref, w_ref, order_ref, col_ref, safe_ref, pulled_ref):
    rows, basis_count, lat_taps, col_pad, lane_rows = t_ref.shape
    chan_count = w_ref.shape[1]
    col_ref[...] = jnp.zeros_like(col_ref)

    def guard(i, carry):
        denominator = None
        for a in range(lat_taps):
            band = t_ref[i, :, a].reshape(basis_count * col_pad, lane_rows)
            start = pl.multiple_of((i + a) * lane_rows, lane_rows)
            den = jnp.dot(band, m_ref[pl.ds(start, lane_rows), :], preferred_element_type=jnp.float32)
            denominator = den if denominator is None else denominator + den
        safe = jnp.maximum(denominator, 1.0)
        rows_at = pl.ds(pl.multiple_of(i * col_pad, col_pad), col_pad)
        for b in range(basis_count):
            safe_ref[b, rows_at, :] = safe[b * col_pad : (b + 1) * col_pad]
        return carry

    lax.fori_loop(0, rows, guard, 0, unroll=True)
    upstream_all = cot_ref[...].reshape(rows * col_pad, chan_count)
    for b in range(basis_count):
        back = lax.dot_general(
            upstream_all, w_ref[b], (((1,), (1,)), ((), ())), preferred_element_type=jnp.float32
        )
        pulled_ref[b] = (back / safe_ref[b]).astype(jnp.bfloat16)

    def body(i, carry):
        rows_at = pl.ds(pl.multiple_of(i * col_pad, col_pad), col_pad)
        pulled = jnp.concatenate([pulled_ref[b, rows_at, :] for b in range(basis_count)], axis=0)
        for a in range(lat_taps):
            band = t_ref[i, :, a].reshape(basis_count * col_pad, lane_rows)
            start = pl.multiple_of((i + a) * lane_rows, lane_rows)
            term = lax.dot_general(
                band, pulled, (((0,), (0,)), ((), ())), preferred_element_type=jnp.float32
            )
            col_ref[pl.ds(start, lane_rows), :] += term
        return carry

    lax.fori_loop(0, rows, body, 0, unroll=True)


def local(features, obs_mask, filter_taps, band_width, mixing, cotangent):
    row_count, col_count, chan_count = features.shape
    group_count = obs_mask.shape[2]
    group_width = chan_count // group_count
    basis_count = mixing.shape[1]
    tap_count = filter_taps.shape[3]
    tap_reach = (tap_count - 1) // 2
    padded_cols = col_count + 2 * tap_reach
    lane_rows = -(-padded_cols // 16) * 16
    col_pad = -(-col_count // 16) * 16
    mask_values = obs_mask.astype(jnp.bfloat16)
    spread = (
        jnp.arange(chan_count)[None, :] // group_width == jnp.arange(group_count)[:, None]
    ).astype(jnp.bfloat16)
    own_mask = jnp.dot(
        mask_values.reshape(row_count * col_count, group_count), spread,
        preferred_element_type=jnp.float32,
    ).astype(jnp.bfloat16).reshape(row_count, col_count, chan_count)
    masked = features * own_mask
    packed = jnp.concatenate([masked, mask_values], axis=-1)
    packed = with_halo(packed, (("lat", 0),), 1, False)
    packed = with_halo(packed, (("lon", 1),), tap_reach, True)
    packed = jnp.pad(packed, ((0, 0), (0, lane_rows - padded_cols), (0, 0)))
    full_input = packed[..., :chan_count].reshape((row_count + 2) * lane_rows, chan_count)
    full_mask = jnp.dot(
        packed[..., chan_count:].reshape((row_count + 2) * lane_rows, group_count), spread,
        preferred_element_type=jnp.float32,
    ).astype(jnp.bfloat16)

    offsets = jnp.arange(tap_count) - tap_reach
    allowed = jnp.abs(offsets)[None, :] <= band_width[:, None]
    global_taps = filter_taps * allowed[:, None, None, :].astype(jnp.bfloat16)
    first_row = lax.axis_index("lat") * row_count
    local_taps = lax.dynamic_slice_in_dim(global_taps, first_row, row_count, 0)
    padded_index = jnp.arange(lane_rows)
    output_index = jnp.arange(col_pad)
    tap_index = jnp.arange(tap_count)
    forward_table = (
        (padded_index[None, None, :] - output_index[None, :, None] == tap_index[:, None, None])
        & (output_index[None, :, None] < col_count)
    ).astype(jnp.bfloat16)
    band = (
        jnp.einsum("ibae,ejp->ibajp", local_taps, forward_table, preferred_element_type=jnp.float32)
        .astype(jnp.bfloat16)
    )

    eye = jnp.eye(group_count, dtype=mixing.dtype)
    mix_blocks = jnp.einsum("gbco,gh->bgcho", mixing, eye).reshape(basis_count, chan_count, chan_count)
    upstream = jnp.pad(cotangent, ((0, 0), (0, col_pad - col_count), (0, 0)))

    vmem = pl.BlockSpec(memory_space=pltpu.VMEM)
    params = pltpu.CompilerParams(vmem_limit_bytes=48 * 1024 * 1024)
    infilled, grad_blocks = pl.pallas_call(
        forward_kernel,
        out_shape=(
            jax.ShapeDtypeStruct((row_count, col_count, chan_count), jnp.bfloat16),
            jax.ShapeDtypeStruct((basis_count, group_width, chan_count), jnp.float32),
        ),
        in_specs=[vmem] * 5,
        out_specs=[vmem] * 2,
        scratch_shapes=[
            pltpu.VMEM((basis_count, row_count * col_pad, chan_count), jnp.bfloat16),
        ],
        compiler_params=params,
        cost_estimate=pl.CostEstimate(
            flops=2 * row_count * basis_count * col_pad * chan_count * (6 * lane_rows + 3 * chan_count),
            transcendentals=0,
            bytes_accessed=8 * (row_count + 2) * lane_rows * chan_count,
        ),
    )(full_input, full_mask, band, upstream, mix_blocks)

    cell_count = row_count * lax.axis_size("lat") * col_count * lax.axis_size("lon")
    lat_count = lax.axis_size("lat")
    if lat_count % 2 == 0:
        first = lax.ppermute(grad_blocks, "lat", [(i, i ^ 1) for i in range(lat_count)])
        dense = butterfly_sum(grad_blocks + first, ("lat", "lon"), skip=1)
    else:
        first = grad_blocks
        dense = butterfly_sum(grad_blocks, ("lat", "lon"))
    dense = dense * (1.0 / math.sqrt(cell_count))
    weight_grad = dense.reshape(basis_count, group_width, group_count, group_width).transpose(2, 0, 1, 3)

    collected = pl.pallas_call(
        adjoint_kernel,
        out_shape=jax.ShapeDtypeStruct(((row_count + 2) * lane_rows, chan_count), jnp.float32),
        in_specs=[vmem] * 4 + [pl.BlockSpec(memory_space=pl.ANY)],
        out_specs=vmem,
        scratch_shapes=[
            pltpu.VMEM((basis_count, row_count * col_pad, chan_count), jnp.float32),
            pltpu.VMEM((basis_count, row_count * col_pad, chan_count), jnp.bfloat16),
        ],
        compiler_params=params,
        cost_estimate=pl.CostEstimate(
            flops=6 * row_count * basis_count * col_pad * lane_rows * chan_count,
            transcendentals=0,
            bytes_accessed=6 * (row_count + 2) * lane_rows * chan_count,
        ),
    )(full_mask, band, upstream, mix_blocks, first)

    collected = collected.reshape(row_count + 2, lane_rows, chan_count)[:, :padded_cols]
    from_below = passed_along(collected[0:1], "lat", -1)
    from_above = passed_along(collected[row_count + 1 : row_count + 2], "lat", 1)
    inner_rows = (
        collected[1 : row_count + 1]
        + jnp.pad(from_above, ((0, row_count - 1), (0, 0), (0, 0)))
        + jnp.pad(from_below, ((row_count - 1, 0), (0, 0), (0, 0)))
    )
    left_rim = inner_rows[:, :tap_reach]
    right_rim = inner_rows[:, col_count + tap_reach :]
    from_right = from_behind(left_rim.astype(jnp.bfloat16), "lon", -1).astype(left_rim.dtype)
    from_left = from_behind(right_rim, "lon", 1)
    gathered = (
        inner_rows[:, tap_reach : tap_reach + col_count]
        + jnp.pad(from_right, ((0, 0), (col_count - tap_reach, 0), (0, 0)))
        + jnp.pad(from_left, ((0, 0), (0, col_count - tap_reach), (0, 0)))
    )
    input_grad = (gathered * own_mask).astype(jnp.bfloat16)
    return (infilled, input_grad, weight_grad)


def solution(mesh):
    placed = (P("lat", "lon", None), P("lat", "lon", None), P(), P(), P(), P("lat", "lon", None))
    return jax.shard_map(
        local,
        mesh=mesh,
        in_specs=placed,
        out_specs=(P("lat", "lon", None), P("lat", "lon", None), P()),
        check_vma=False,
    )
```

```python
import math

import jax
import jax.numpy as jnp
from jax import lax
from jax.experimental import pallas as pl
from jax.experimental.pallas import tpu as pltpu
from jax.sharding import PartitionSpec as P


def with_halo(block, sides, width, periodic):
    for axis, dim in sides:
        count = lax.axis_size(axis)
        forward = [(i, i + 1) for i in range(count - 1)]
        if periodic:
            forward.append((count - 1, 0))
        backward = [(target, source) for source, target in forward]
        low = lax.ppermute(
            lax.slice_in_dim(block, block.shape[dim] - width, None, axis=dim), axis, forward
        )
        high = lax.ppermute(lax.slice_in_dim(block, 0, width, axis=dim), axis, backward)
        block = jnp.concatenate([low, block, high], axis=dim)
    return block


def passed_along(block, axis, distance):
    devices = range(lax.axis_size(axis))
    route = [(i - distance, i) for i in devices if i - distance in devices]
    return lax.ppermute(block, axis, route)


def from_behind(x, axis, by):
    size = lax.axis_size(axis)
    return lax.ppermute(x, axis, [(i, (i + by) % size) for i in range(size)])


def butterfly_sum(value, axes, skip=0):
    for axis in axes:
        count = lax.axis_size(axis)
        if count & (count - 1):
            value = lax.psum(value, axis)
            continue
        step = 1
        while step < count:
            if skip:
                skip -= 1
                step *= 2
                continue
            partner = lax.ppermute(value, axis, [(i, i ^ step) for i in range(count)])
            value = value + partner
            step *= 2
    return value


def forward_kernel(x_ref, m_ref, t_ref, cot_ref, w_ref, inf_ref, wg_ref, pulled_ref, scaled_ref, safe_ref):
    rows, basis_count, lat_taps, col_pad, lane_rows = t_ref.shape
    col_count = inf_ref.shape[1]
    chan_count = w_ref.shape[1]
    group_width = wg_ref.shape[1]

    def body(i, carry):
        numerator = None
        denominator = None
        for a in range(lat_taps):
            band = t_ref[i, :, a].reshape(basis_count * col_pad, lane_rows)
            start = pl.multiple_of((i + a) * lane_rows, lane_rows)
            num = jnp.dot(band, x_ref[pl.ds(start, lane_rows), :], preferred_element_type=jnp.float32)
            den = jnp.dot(band, m_ref[pl.ds(start, lane_rows), :], preferred_element_type=jnp.float32)
            numerator = num if numerator is None else numerator + num
            denominator = den if denominator is None else denominator + den
        safe = jnp.maximum(denominator, 1.0)
        scaled = (numerator / safe).astype(jnp.bfloat16)
        rows_at = pl.ds(pl.multiple_of(i * col_pad, col_pad), col_pad)
        for b in range(basis_count):
            scaled_ref[b, rows_at, :] = scaled[b * col_pad : (b + 1) * col_pad]
            safe_ref[b, rows_at, :] = 1.0 / safe[b * col_pad : (b + 1) * col_pad]
        return carry

    lax.fori_loop(0, rows, body, 0, unroll=True)
    lane = lax.broadcasted_iota(jnp.int32, (group_width, chan_count), 1) // group_width
    upstream_all = cot_ref[...].reshape(rows * col_pad, chan_count)
    out = None
    for b in range(basis_count):
        part = scaled_ref[b]
        mixed = jnp.dot(part, w_ref[b], preferred_element_type=jnp.float32)
        out = mixed if out is None else out + mixed
        grad = lax.dot_general(
            part, upstream_all, (((0,), (0,)), ((), ())), preferred_element_type=jnp.float32
        )
        total = jnp.zeros((group_width, chan_count), jnp.float32)
        for g in range(chan_count // group_width):
            block = grad[g * group_width : (g + 1) * group_width, :]
            total = total + jnp.where(lane == g, block, 0.0)
        wg_ref[b] = total
        back = lax.dot_general(
            upstream_all, w_ref[b], (((1,), (1,)), ((), ())), preferred_element_type=jnp.float32
        )
        pulled_ref[b] = (back * safe_ref[b]).astype(jnp.bfloat16)
    for i in range(rows):
        inf_ref[i] = out[i * col_pad : i * col_pad + col_count].astype(inf_ref.dtype)


def adjoint_kernel(t_ref, pulled_ref, order_ref, col_ref):
    rows, basis_count, lat_taps, col_pad, lane_rows = t_ref.shape
    col_ref[...] = jnp.zeros_like(col_ref)

    def body(i, carry):
        rows_at = pl.ds(pl.multiple_of(i * col_pad, col_pad), col_pad)
        pulled = jnp.concatenate([pulled_ref[b, rows_at, :] for b in range(basis_count)], axis=0)
        for a in range(lat_taps):
            band = t_ref[i, :, a].reshape(basis_count * col_pad, lane_rows)
            start = pl.multiple_of((i + a) * lane_rows, lane_rows)
            term = lax.dot_general(
                band, pulled, (((0,), (0,)), ((), ())), preferred_element_type=jnp.float32
            )
            col_ref[pl.ds(start, lane_rows), :] += term
        return carry

    lax.fori_loop(0, rows, body, 0, unroll=True)


def local(features, obs_mask, filter_taps, band_width, mixing, cotangent):
    row_count, col_count, chan_count = features.shape
    group_count = obs_mask.shape[2]
    group_width = chan_count // group_count
    basis_count = mixing.shape[1]
    tap_count = filter_taps.shape[3]
    tap_reach = (tap_count - 1) // 2
    padded_cols = col_count + 2 * tap_reach
    lane_rows = -(-padded_cols // 16) * 16
    col_pad = -(-col_count // 16) * 16
    mask_values = obs_mask.astype(jnp.bfloat16)
    spread = (
        jnp.arange(chan_count)[None, :] // group_width == jnp.arange(group_count)[:, None]
    ).astype(jnp.bfloat16)
    own_mask = jnp.dot(
        mask_values.reshape(row_count * col_count, group_count), spread,
        preferred_element_type=jnp.float32,
    ).astype(jnp.bfloat16).reshape(row_count, col_count, chan_count)
    masked = features * own_mask
    packed = jnp.concatenate([masked, mask_values], axis=-1)
    packed = with_halo(packed, (("lat", 0),), 1, False)
    packed = with_halo(packed, (("lon", 1),), tap_reach, True)
    packed = jnp.pad(packed, ((0, 0), (0, lane_rows - padded_cols), (0, 0)))
    full_input = packed[..., :chan_count].reshape((row_count + 2) * lane_rows, chan_count)
    full_mask = jnp.dot(
        packed[..., chan_count:].reshape((row_count + 2) * lane_rows, group_count), spread,
        preferred_element_type=jnp.float32,
    ).astype(jnp.bfloat16)

    offsets = jnp.arange(tap_count) - tap_reach
    allowed = jnp.abs(offsets)[None, :] <= band_width[:, None]
    global_taps = filter_taps * allowed[:, None, None, :].astype(jnp.bfloat16)
    first_row = lax.axis_index("lat") * row_count
    local_taps = lax.dynamic_slice_in_dim(global_taps, first_row, row_count, 0)
    padded_index = jnp.arange(lane_rows)
    output_index = jnp.arange(col_pad)
    tap_index = jnp.arange(tap_count)
    forward_table = (
        (padded_index[None, None, :] - output_index[None, :, None] == tap_index[:, None, None])
        & (output_index[None, :, None] < col_count)
    ).astype(jnp.bfloat16)
    band = (
        jnp.einsum("ibae,ejp->ibajp", local_taps, forward_table, preferred_element_type=jnp.float32)
        .astype(jnp.bfloat16)
    )

    eye = jnp.eye(group_count, dtype=mixing.dtype)
    mix_blocks = jnp.einsum("gbco,gh->bgcho", mixing, eye).reshape(basis_count, chan_count, chan_count)
    upstream = jnp.pad(cotangent, ((0, 0), (0, col_pad - col_count), (0, 0)))

    vmem = pl.BlockSpec(memory_space=pltpu.VMEM)
    params = pltpu.CompilerParams(vmem_limit_bytes=48 * 1024 * 1024)
    infilled, grad_blocks, pulled = pl.pallas_call(
        forward_kernel,
        out_shape=(
            jax.ShapeDtypeStruct((row_count, col_count, chan_count), jnp.bfloat16),
            jax.ShapeDtypeStruct((basis_count, group_width, chan_count), jnp.float32),
            jax.ShapeDtypeStruct((basis_count, row_count * col_pad, chan_count), jnp.bfloat16),
        ),
        in_specs=[vmem] * 5,
        out_specs=[vmem] * 3,
        scratch_shapes=[
            pltpu.VMEM((basis_count, row_count * col_pad, chan_count), jnp.bfloat16),
            pltpu.VMEM((basis_count, row_count * col_pad, chan_count), jnp.float32),
        ],
        compiler_params=params,
        cost_estimate=pl.CostEstimate(
            flops=2 * row_count * basis_count * col_pad * chan_count * (6 * lane_rows + 3 * chan_count),
            transcendentals=0,
            bytes_accessed=8 * (row_count + 2) * lane_rows * chan_count,
        ),
    )(full_input, full_mask, band, upstream, mix_blocks)

    cell_count = row_count * lax.axis_size("lat") * col_count * lax.axis_size("lon")
    lat_count = lax.axis_size("lat")
    if lat_count % 2 == 0:
        first = lax.ppermute(grad_blocks, "lat", [(i, i ^ 1) for i in range(lat_count)])
        dense = butterfly_sum(grad_blocks + first, ("lat", "lon"), skip=1)
    else:
        first = grad_blocks
        dense = butterfly_sum(grad_blocks, ("lat", "lon"))
    dense = dense * (1.0 / math.sqrt(cell_count))
    weight_grad = dense.reshape(basis_count, group_width, group_count, group_width).transpose(2, 0, 1, 3)

    collected = pl.pallas_call(
        adjoint_kernel,
        out_shape=jax.ShapeDtypeStruct(((row_count + 2) * lane_rows, chan_count), jnp.float32),
        in_specs=[vmem, vmem, pl.BlockSpec(memory_space=pl.ANY)],
        out_specs=vmem,
        compiler_params=params,
        cost_estimate=pl.CostEstimate(
            flops=6 * row_count * basis_count * col_pad * lane_rows * chan_count,
            transcendentals=0,
            bytes_accessed=6 * (row_count + 2) * lane_rows * chan_count,
        ),
    )(band, pulled, first)

    collected = collected.reshape(row_count + 2, lane_rows, chan_count)[:, :padded_cols]
    from_below = passed_along(collected[0:1], "lat", -1)
    from_above = passed_along(collected[row_count + 1 : row_count + 2], "lat", 1)
    inner_rows = (
        collected[1 : row_count + 1]
        + jnp.pad(from_above, ((0, row_count - 1), (0, 0), (0, 0)))
        + jnp.pad(from_below, ((row_count - 1, 0), (0, 0), (0, 0)))
    )
    left_rim = inner_rows[:, :tap_reach]
    right_rim = inner_rows[:, col_count + tap_reach :]
    from_right = from_behind(left_rim.astype(jnp.bfloat16), "lon", -1).astype(left_rim.dtype)
    from_left = from_behind(right_rim, "lon", 1)
    gathered = (
        inner_rows[:, tap_reach : tap_reach + col_count]
        + jnp.pad(from_right, ((0, 0), (col_count - tap_reach, 0), (0, 0)))
        + jnp.pad(from_left, ((0, 0), (0, col_count - tap_reach), (0, 0)))
    )
    input_grad = (gathered * own_mask).astype(jnp.bfloat16)
    return (infilled, input_grad, weight_grad)


def solution(mesh):
    placed = (P("lat", "lon", None), P("lat", "lon", None), P(), P(), P(), P("lat", "lon", None))
    return jax.shard_map(
        local,
        mesh=mesh,
        in_specs=placed,
        out_specs=(P("lat", "lon", None), P("lat", "lon", None), P()),
        check_vma=False,
    )
```

```python
import math

import jax
import jax.numpy as jnp
from jax import lax
from jax.experimental import pallas as pl
from jax.experimental.pallas import tpu as pltpu
from jax.sharding import PartitionSpec as P


def with_halo(block, sides, width, periodic):
    for axis, dim in sides:
        count = lax.axis_size(axis)
        forward = [(i, i + 1) for i in range(count - 1)]
        if periodic:
            forward.append((count - 1, 0))
        backward = [(target, source) for source, target in forward]
        low = lax.ppermute(
            lax.slice_in_dim(block, block.shape[dim] - width, None, axis=dim), axis, forward
        )
        high = lax.ppermute(lax.slice_in_dim(block, 0, width, axis=dim), axis, backward)
        block = jnp.concatenate([low, block, high], axis=dim)
    return block


def passed_along(block, axis, distance):
    devices = range(lax.axis_size(axis))
    route = [(i - distance, i) for i in devices if i - distance in devices]
    return lax.ppermute(block, axis, route)


def from_behind(x, axis, by):
    size = lax.axis_size(axis)
    return lax.ppermute(x, axis, [(i, (i + by) % size) for i in range(size)])


def butterfly_sum(value, axes, skip=0):
    for axis in axes:
        count = lax.axis_size(axis)
        if count & (count - 1):
            value = lax.psum(value, axis)
            continue
        steps = [1 << k for k in range(count.bit_length() - 1)]
        steps = steps[skip:]
        skip = 0
        steps = steps[::-1] if axis == "lat" else steps
        for step in steps:
            partner = lax.ppermute(value, axis, [(i, i ^ step) for i in range(count)])
            value = value + partner
    return value


def forward_kernel(x_ref, m_ref, t_ref, cot_ref, w_ref, inf_ref, wg_ref, pulled_ref, scaled_ref, safe_ref):
    rows, basis_count, lat_taps, col_pad, lane_rows = t_ref.shape
    col_count = inf_ref.shape[1]
    chan_count = w_ref.shape[1]
    group_width = wg_ref.shape[1]

    def body(i, carry):
        numerator = None
        denominator = None
        for a in range(lat_taps):
            band = t_ref[i, :, a].reshape(basis_count * col_pad, lane_rows)
            start = pl.multiple_of((i + a) * lane_rows, lane_rows)
            num = jnp.dot(band, x_ref[pl.ds(start, lane_rows), :], preferred_element_type=jnp.float32)
            den = jnp.dot(band, m_ref[pl.ds(start, lane_rows), :], preferred_element_type=jnp.float32)
            numerator = num if numerator is None else numerator + num
            denominator = den if denominator is None else denominator + den
        safe = jnp.maximum(denominator, 1.0)
        scaled = (numerator / safe).astype(jnp.bfloat16)
        rows_at = pl.ds(pl.multiple_of(i * col_pad, col_pad), col_pad)
        for b in range(basis_count):
            scaled_ref[b, rows_at, :] = scaled[b * col_pad : (b + 1) * col_pad]
            safe_ref[b, rows_at, :] = safe[b * col_pad : (b + 1) * col_pad]
        return carry

    lax.fori_loop(0, rows, body, 0, unroll=True)
    lane = lax.broadcasted_iota(jnp.int32, (group_width, chan_count), 1) // group_width
    upstream_all = cot_ref[...].reshape(rows * col_pad, chan_count)
    out = None
    for b in range(basis_count):
        part = scaled_ref[b]
        mixed = jnp.dot(part, w_ref[b], preferred_element_type=jnp.float32)
        out = mixed if out is None else out + mixed
        grad = lax.dot_general(
            part, upstream_all, (((0,), (0,)), ((), ())), preferred_element_type=jnp.float32
        )
        total = jnp.zeros((group_width, chan_count), jnp.float32)
        for g in range(chan_count // group_width):
            block = grad[g * group_width : (g + 1) * group_width, :]
            total = total + jnp.where(lane == g, block, 0.0)
        wg_ref[b] = total
        back = lax.dot_general(
            upstream_all, w_ref[b], (((1,), (1,)), ((), ())), preferred_element_type=jnp.float32
        )
        pulled_ref[b] = (back / safe_ref[b]).astype(jnp.bfloat16)
    for i in range(rows):
        inf_ref[i] = out[i * col_pad : i * col_pad + col_count].astype(inf_ref.dtype)


def adjoint_kernel(t_ref, pulled_ref, order_ref, col_ref):
    rows, basis_count, lat_taps, col_pad, lane_rows = t_ref.shape
    col_ref[...] = jnp.zeros_like(col_ref)

    def body(i, carry):
        rows_at = pl.ds(pl.multiple_of(i * col_pad, col_pad), col_pad)
        pulled = jnp.concatenate([pulled_ref[b, rows_at, :] for b in range(basis_count)], axis=0)
        for a in range(lat_taps):
            band = t_ref[i, :, a].reshape(basis_count * col_pad, lane_rows)
            start = pl.multiple_of((i + a) * lane_rows, lane_rows)
            term = lax.dot_general(
                band, pulled, (((0,), (0,)), ((), ())), preferred_element_type=jnp.float32
            )
            col_ref[pl.ds(start, lane_rows), :] += term
        return carry

    lax.fori_loop(0, rows, body, 0, unroll=True)


def local(features, obs_mask, filter_taps, band_width, mixing, cotangent):
    row_count, col_count, chan_count = features.shape
    group_count = obs_mask.shape[2]
    group_width = chan_count // group_count
    basis_count = mixing.shape[1]
    tap_count = filter_taps.shape[3]
    tap_reach = (tap_count - 1) // 2
    padded_cols = col_count + 2 * tap_reach
    lane_rows = -(-padded_cols // 16) * 16
    col_pad = -(-col_count // 16) * 16
    mask_values = obs_mask.astype(jnp.bfloat16)
    spread = (
        jnp.arange(chan_count)[None, :] // group_width == jnp.arange(group_count)[:, None]
    ).astype(jnp.bfloat16)
    own_mask = jnp.dot(
        mask_values.reshape(row_count * col_count, group_count), spread,
        preferred_element_type=jnp.float32,
    ).astype(jnp.bfloat16).reshape(row_count, col_count, chan_count)
    masked = features * own_mask
    packed = jnp.concatenate([masked, mask_values], axis=-1)
    packed = with_halo(packed, (("lat", 0),), 1, False)
    packed = with_halo(packed, (("lon", 1),), tap_reach, True)
    packed = jnp.pad(packed, ((0, 0), (0, lane_rows - padded_cols), (0, 0)))
    full_input = packed[..., :chan_count].reshape((row_count + 2) * lane_rows, chan_count)
    full_mask = jnp.dot(
        packed[..., chan_count:].reshape((row_count + 2) * lane_rows, group_count), spread,
        preferred_element_type=jnp.float32,
    ).astype(jnp.bfloat16)

    offsets = jnp.arange(tap_count) - tap_reach
    allowed = jnp.abs(offsets)[None, :] <= band_width[:, None]
    global_taps = filter_taps * allowed[:, None, None, :].astype(jnp.bfloat16)
    first_row = lax.axis_index("lat") * row_count
    local_taps = lax.dynamic_slice_in_dim(global_taps, first_row, row_count, 0)
    padded_index = jnp.arange(lane_rows)
    output_index = jnp.arange(col_pad)
    tap_index = jnp.arange(tap_count)
    forward_table = (
        (padded_index[None, None, :] - output_index[None, :, None] == tap_index[:, None, None])
        & (output_index[None, :, None] < col_count)
    ).astype(jnp.bfloat16)
    band = (
        jnp.einsum("ibae,ejp->ibajp", local_taps, forward_table, preferred_element_type=jnp.float32)
        .astype(jnp.bfloat16)
    )

    eye = jnp.eye(group_count, dtype=mixing.dtype)
    mix_blocks = jnp.einsum("gbco,gh->bgcho", mixing, eye).reshape(basis_count, chan_count, chan_count)
    upstream = jnp.pad(cotangent, ((0, 0), (0, col_pad - col_count), (0, 0)))

    vmem = pl.BlockSpec(memory_space=pltpu.VMEM)
    params = pltpu.CompilerParams(vmem_limit_bytes=48 * 1024 * 1024)
    infilled, grad_blocks, pulled = pl.pallas_call(
        forward_kernel,
        out_shape=(
            jax.ShapeDtypeStruct((row_count, col_count, chan_count), jnp.bfloat16),
            jax.ShapeDtypeStruct((basis_count, group_width, chan_count), jnp.float32),
            jax.ShapeDtypeStruct((basis_count, row_count * col_pad, chan_count), jnp.bfloat16),
        ),
        in_specs=[vmem] * 5,
        out_specs=[vmem] * 3,
        scratch_shapes=[
            pltpu.VMEM((basis_count, row_count * col_pad, chan_count), jnp.bfloat16),
            pltpu.VMEM((basis_count, row_count * col_pad, chan_count), jnp.float32),
        ],
        compiler_params=params,
        cost_estimate=pl.CostEstimate(
            flops=2 * row_count * basis_count * col_pad * chan_count * (6 * lane_rows + 3 * chan_count),
            transcendentals=0,
            bytes_accessed=8 * (row_count + 2) * lane_rows * chan_count,
        ),
    )(full_input, full_mask, band, upstream, mix_blocks)

    cell_count = row_count * lax.axis_size("lat") * col_count * lax.axis_size("lon")
    lat_count = lax.axis_size("lat")
    if lat_count % 2 == 0:
        first = lax.ppermute(grad_blocks, "lat", [(i, i ^ 1) for i in range(lat_count)])
        dense = butterfly_sum(grad_blocks + first, ("lat", "lon"), skip=1)
    else:
        first = grad_blocks
        dense = butterfly_sum(grad_blocks, ("lat", "lon"))
    dense = dense * (1.0 / math.sqrt(cell_count))
    weight_grad = dense.reshape(basis_count, group_width, group_count, group_width).transpose(2, 0, 1, 3)

    collected = pl.pallas_call(
        adjoint_kernel,
        out_shape=jax.ShapeDtypeStruct(((row_count + 2) * lane_rows, chan_count), jnp.float32),
        in_specs=[vmem, vmem, pl.BlockSpec(memory_space=pl.ANY)],
        out_specs=vmem,
        compiler_params=params,
        cost_estimate=pl.CostEstimate(
            flops=6 * row_count * basis_count * col_pad * lane_rows * chan_count,
            transcendentals=0,
            bytes_accessed=6 * (row_count + 2) * lane_rows * chan_count,
        ),
    )(band, pulled, first)

    collected = collected.reshape(row_count + 2, lane_rows, chan_count)[:, :padded_cols]
    from_below = passed_along(collected[0:1], "lat", -1)
    from_above = passed_along(collected[row_count + 1 : row_count + 2], "lat", 1)
    inner_rows = (
        collected[1 : row_count + 1]
        + jnp.pad(from_above, ((0, row_count - 1), (0, 0), (0, 0)))
        + jnp.pad(from_below, ((row_count - 1, 0), (0, 0), (0, 0)))
    )
    left_rim = inner_rows[:, :tap_reach]
    right_rim = inner_rows[:, col_count + tap_reach :]
    from_right = from_behind(left_rim.astype(jnp.bfloat16), "lon", -1).astype(left_rim.dtype)
    from_left = from_behind(right_rim, "lon", 1)
    gathered = (
        inner_rows[:, tap_reach : tap_reach + col_count]
        + jnp.pad(from_right, ((0, 0), (col_count - tap_reach, 0), (0, 0)))
        + jnp.pad(from_left, ((0, 0), (0, col_count - tap_reach), (0, 0)))
    )
    input_grad = (gathered * own_mask).astype(jnp.bfloat16)
    return (infilled, input_grad, weight_grad)


def solution(mesh):
    placed = (P("lat", "lon", None), P("lat", "lon", None), P(), P(), P(), P("lat", "lon", None))
    return jax.shard_map(
        local,
        mesh=mesh,
        in_specs=placed,
        out_specs=(P("lat", "lon", None), P("lat", "lon", None), P()),
        check_vma=False,
    )
```
